32 devices in a mesh: group: 2 (over y), seq: 4 (over z), batch: 2 (over x), chan: 2 (over core).
Axes of the slice: x: 2, y: 2, z: 4, core: 2. Of those that a mesh axis runs over, the one named last changes fastest.
Arguments:
- seq_in: bfloat16 [4, 4096, 768], P(('group', 'batch'), 'seq', 'chan'), parts along dimension 0, may hold values from -6 to 6
- conv_weight: bfloat16 [3, 768, 768], P(None, 'chan'), may hold values from -0.125 to 0.125
- cotangent: bfloat16 [4, 2048, 768], P(('group', 'batch'), 'seq', 'chan'), parts along dimension 0, may hold values from -0.59765625 to 0.59765625
Outputs:
- block_out: bfloat16 [4, 2048, 768], P(('group', 'batch'), 'seq', 'chan'), parts along dimension 0
- input_grad: bfloat16 [4, 4096, 768], P(('group', 'batch'), 'seq', 'chan'), parts along dimension 0
- weight_grad: float32 [6, 768, 768], P('group', 'chan', 'batch'), parts along dimension 0
The draws below stay inside these ranges and needn't reach their ends.
There are 2 independent parts, one for each index of `group`. The reference program is written for one: setup_inputs(seed, part) draws one part's arguments, and reference() takes and returns one part's arrays. A program takes and returns all parts, laid end to end along the dimension named above; an argument that names none is the same for every part. Nothing has to cross between parts.
All inputs are finite; a program needn't handle non-finite values.
Results may differ from the reference program's by a relative error of at most 0.0031.
Values may be sent and summed in bfloat16 or wider, within the bound.
No kernel may reach another device: no remote copies, remote signals or barrier semaphores. Data moves between devices by JAX's collectives and lax.ppermute only.
A program may use at most 64 MiB of HBM per device.

```python
import jax
import jax.numpy as jnp
from jax import lax

C = 768
DILATION_STEP = 256
SAMPLES = 2
LENGTH = 4096
POOLED = 2048


def spiked(array, own_key, source, target, blocks, factor):
    owner, partner = [(jnp.arange(array.shape[position]) // (array.shape[position] // blocks)).reshape([-1 if axis == position else 1 for axis in range(array.ndim)]) for position in (source, target)]
    chosen = jax.random.permutation(own_key, blocks)[partner]
    strong = (owner == chosen) | (owner == (partner + blocks // 2) % blocks)
    return jnp.where(strong, factor * array, array)


def block_scale(stream_key, dims, split, least, largest):
    level, own = 1.0, jax.random.fold_in(stream_key, 6)
    for axis_at, blocks in split:
        steps = jnp.exp(jax.random.uniform(jax.random.fold_in(own, axis_at), (blocks,), jnp.float32, least / len(split), largest / len(split)))
        level = level * jnp.repeat(steps, dims[axis_at] // blocks).reshape([-1 if axis == axis_at else 1 for axis in range(len(dims))])
    return level


def noise(stream_key, dims, width, limit, shards=(), kind=jnp.bfloat16):
    array = jax.random.normal(stream_key, dims, jnp.float32) * width
    if len(shards) > 0:
        array = block_scale(stream_key, dims, shards, -0.22, 0.18) * array
    return jnp.clip(array, min=-limit, max=limit).astype(kind)


def gaussian_with(rng, shape, scale, most, shards, heavy, kind=jnp.bfloat16):
    drawn = scale * jax.random.normal(rng, shape, jnp.float32)
    if shards:
        drawn = drawn * block_scale(rng, shape, shards, -0.22, 0.18)
    return jnp.clip(spiked(drawn, jax.random.fold_in(rng, 3), *heavy), -most, most).astype(kind)


def setup_inputs(seed: int = 0, part: int = 0) -> dict:
    seeds = jax.random.split(jax.random.key(seed), 4)
    part_keys = jax.random.split(jax.random.fold_in(seeds[3], part), 4)
    seq_in = noise(part_keys[0], (SAMPLES, LENGTH, C), 1.0, 6.0, ((0, 2), (1, 4), (2, 2)))
    conv_weight = noise(seeds[1], (3, C, C), (3 * C) ** -0.5, 0.125, ((1, 2),))
    cotangent = gaussian_with(part_keys[2], (SAMPLES, POOLED, C), 0.1, 0.59765625, ((0, 2), (1, 4), (2, 2)), (1, 2, 4, 2.0))
    return {"seq_in": seq_in, "conv_weight": conv_weight, "cotangent": cotangent}


def displaced_taps(values, spread):
    blank = jnp.zeros((spread, values.shape[1]), values.dtype)
    before = jnp.concatenate([blank, values[:-spread]], 0)
    after = jnp.concatenate([values[spread:], blank], 0)
    return (before, after)

def reference(seq_in, conv_weight, cotangent):
    weight_flat = conv_weight.reshape(3 * C, C)
    weight_back = jnp.transpose(conv_weight, (0, 2, 1)).reshape(3 * C, C)

    def one_sample(inputs):
        sample_in, sample_cotangent = inputs
        length = sample_in.shape[0] // 2
        pooled = 0.5 * lax.optimization_barrier(jnp.sum(sample_in.astype(jnp.float32).reshape(length, 2, C), axis=1))
        activation_block = jax.nn.gelu(pooled).astype(jnp.bfloat16)
        activation_earlier, activation_later = displaced_taps(activation_block, DILATION_STEP)
        stacked = jnp.concatenate([activation_earlier, activation_block, activation_later], 1)
        conv_out = jnp.dot(stacked, weight_flat, preferred_element_type=jnp.float32)
        block_out = (pooled + conv_out).astype(jnp.bfloat16)
        cotangent_earlier, cotangent_later = displaced_taps(sample_cotangent, DILATION_STEP)
        cot_stack = jnp.concatenate([cotangent_later, sample_cotangent, cotangent_earlier], 1)
        activ_grad = jnp.dot(cot_stack, weight_back, preferred_element_type=jnp.float32)
        unused, gelu_back = jax.vjp(jax.nn.gelu, pooled)
        pooled_grad = sample_cotangent.astype(jnp.float32) + gelu_back(activ_grad)[0]
        input_grad = jnp.repeat(0.5 * pooled_grad, 2, axis=0).astype(jnp.bfloat16)
        weight_part = jnp.dot(stacked.T, sample_cotangent, preferred_element_type=jnp.float32)
        return (block_out, input_grad, weight_part)
    block_out, input_grad, weight_parts = lax.map(one_sample, (seq_in, cotangent))
    weight_grad = lax.optimization_barrier(jnp.sum(weight_parts, axis=0)).reshape(3, C, C)
    return (block_out, input_grad, weight_grad)
```

```python
import jax
import jax.numpy as jnp
from jax import lax
from jax.sharding import PartitionSpec as P


def shift_from(block, axis, distance):
    size = lax.axis_size(axis)
    route = [(i - distance, i) for i in range(size) if 0 <= i - distance < size]
    return lax.ppermute(block, axis, route)


def half_of(array, index, axis):
    parts = 2
    shape = array.shape
    split = shape[:axis] + (parts, shape[axis] // parts) + shape[axis + 1 :]
    return lax.dynamic_index_in_dim(array.reshape(split), index, axis, keepdims=False)


def shards(seq_in, conv_weight, cotangent):
    local_in = seq_in[0]
    local_cot = cotangent[0]
    rows = local_in.shape[0] // 2
    width = local_in.shape[1]
    spread = rows // 2
    pooled = 0.5 * jnp.sum(local_in.astype(jnp.float32).reshape(rows, 2, width), axis=1)
    activation = jax.nn.gelu(pooled).astype(jnp.bfloat16)

    both = jnp.stack([activation, local_cot])
    from_prev = shift_from(both[:, rows - spread :], "seq", 1)
    from_next = shift_from(both[:, :spread], "seq", -1)
    own_ext = jnp.concatenate([from_prev, both, from_next], 1)
    full_ext = lax.all_gather(own_ext, "chan", axis=2, tiled=True)
    act_full, cot_full = full_ext[0], full_ext[1]

    weight_cols = lax.all_to_all(conv_weight, "chan", 2, 1, tiled=True)
    act_taps = jnp.stack([act_full[k * spread : k * spread + rows] for k in range(3)], 1)
    conv_out = jnp.dot(
        act_taps.reshape(rows, -1),
        weight_cols.reshape(-1, weight_cols.shape[2]),
        preferred_element_type=jnp.float32,
    )
    block_out = (pooled + conv_out).astype(jnp.bfloat16)

    cot_taps = jnp.stack([cot_full[(2 - k) * spread : (2 - k) * spread + rows] for k in range(3)], 1)
    activ_grad = jnp.einsum(
        "tko,kio->ti", cot_taps, conv_weight, preferred_element_type=jnp.float32
    )
    unused, gelu_back = jax.vjp(jax.nn.gelu, pooled)
    pooled_grad = local_cot.astype(jnp.float32) + gelu_back(activ_grad)[0]
    input_grad = jnp.repeat(0.5 * pooled_grad, 2, axis=0).astype(jnp.bfloat16)

    own_taps = jnp.stack([own_ext[0, k * spread : k * spread + rows] for k in range(3)], 1)
    cot_mid = cot_full[spread : spread + rows]
    batch_count = lax.axis_size("batch")
    if batch_count == 2:
        b = lax.axis_index("batch")
        send = jnp.einsum(
            "tki,to->kio", own_taps, half_of(cot_mid, 1 - b, 1), preferred_element_type=jnp.float32
        )
        keep = jnp.einsum(
            "tki,to->kio", own_taps, half_of(cot_mid, b, 1), preferred_element_type=jnp.float32
        )
        summed = keep + lax.ppermute(send, "batch", [(0, 1), (1, 0)])
    else:
        partial = jnp.einsum("tki,to->kio", own_taps, cot_mid, preferred_element_type=jnp.float32)
        summed = lax.psum_scatter(partial, "batch", scatter_dimension=2, tiled=True)
    weight_grad = lax.psum(summed, "seq")
    return (block_out[None], input_grad[None], weight_grad)


def solution(mesh):
    in_specs = (
        P(("group", "batch"), "seq", "chan"),
        P(None, "chan", None),
        P(("group", "batch"), "seq", "chan"),
    )
    out_specs = (
        P(("group", "batch"), "seq", "chan"),
        P(("group", "batch"), "seq", "chan"),
        P("group", "chan", "batch"),
    )
    return jax.shard_map(shards, mesh=mesh, in_specs=in_specs, out_specs=out_specs, check_vma=False)
```

```python
import jax
import jax.numpy as jnp
from jax import lax
from jax.sharding import PartitionSpec as P

SWAP = [(0, 1), (1, 0)]


def shift_from(block, axis, distance):
    size = lax.axis_size(axis)
    route = [(i - distance, i) for i in range(size) if 0 <= i - distance < size]
    return lax.ppermute(block, axis, route)


def half_of(array, index, axis):
    shape = array.shape
    split = shape[:axis] + (2, shape[axis] // 2) + shape[axis + 1 :]
    return lax.dynamic_index_in_dim(array.reshape(split), index, axis, keepdims=False)


def tap_stack(ext, rows, spread, order):
    return jnp.stack([ext[k * spread : k * spread + rows] for k in order], 1)


def line_total(pieces):
    inner = lax.axis_index("seq")
    inner = (inner == 1) | (inner == 2)
    totals = []
    for piece in pieces:
        pair = piece + lax.ppermute(piece, "seq", [(0, 1), (3, 2)])
        whole = pair + lax.ppermute(pair, "seq", [(1, 2), (2, 1)])
        sent = lax.ppermute(whole, "seq", [(1, 0), (2, 3)])
        totals.append(jnp.where(inner, whole, sent))
    return totals


def shards(seq_in, conv_weight, cotangent):
    local_in = seq_in[0]
    local_cot = cotangent[0]
    rows = local_in.shape[0] // 2
    width = local_in.shape[1]
    spread = rows // 2
    c = lax.axis_index("chan")
    pooled = 0.5 * jnp.sum(local_in.astype(jnp.float32).reshape(rows, 2, width), axis=1)
    activation = jax.nn.gelu(pooled).astype(jnp.bfloat16)

    both = jnp.stack([activation, local_cot])
    par_mid = lax.ppermute(both, "chan", SWAP)
    from_prev = shift_from(both[:, rows - spread :], "seq", 1)
    from_next = shift_from(both[:, :spread], "seq", -1)
    par_halo = lax.ppermute(jnp.stack([from_prev, from_next]), "chan", SWAP)
    own_ext = jnp.concatenate([from_prev, both, from_next], 1)
    par_ext = jnp.concatenate([par_halo[0], par_mid, par_halo[1]], 1)

    w_own = half_of(conv_weight, c, 2)
    w_other = half_of(conv_weight, 1 - c, 2)
    w_par = lax.ppermute(w_other, "chan", SWAP)

    conv_out = jnp.einsum(
        "tki,kio->to", tap_stack(own_ext[0], rows, spread, (0, 1, 2)), w_own,
        preferred_element_type=jnp.float32,
    ) + jnp.einsum(
        "tki,kio->to", tap_stack(par_ext[0], rows, spread, (0, 1, 2)), w_par,
        preferred_element_type=jnp.float32,
    )
    block_out = (pooled + conv_out).astype(jnp.bfloat16)

    activ_grad = jnp.einsum(
        "tko,kio->ti", tap_stack(own_ext[1], rows, spread, (2, 1, 0)), w_own,
        preferred_element_type=jnp.float32,
    ) + jnp.einsum(
        "tko,kio->ti", tap_stack(par_ext[1], rows, spread, (2, 1, 0)), w_other,
        preferred_element_type=jnp.float32,
    )
    unused, gelu_back = jax.vjp(jax.nn.gelu, pooled)
    pooled_grad = local_cot.astype(jnp.float32) + gelu_back(activ_grad)[0]
    input_grad = jnp.repeat(0.5 * pooled_grad, 2, axis=0).astype(jnp.bfloat16)

    own_taps = tap_stack(own_ext[0], rows, spread, (0, 1, 2))
    par_cot = par_mid[1]
    batch_count = lax.axis_size("batch")
    seq_count = lax.axis_size("seq")
    if batch_count == 2 and seq_count == 4:
        b = lax.axis_index("batch")
        cot_mine = jnp.where(b == c, local_cot, par_cot)
        cot_theirs = jnp.where(b == c, par_cot, local_cot)
        far_mid = lax.ppermute(jnp.stack([activation, cot_theirs]), "batch", SWAP)
        far_halo = lax.ppermute(jnp.stack([from_prev[0], from_next[0]]), "batch", SWAP)
        far_act = jnp.concatenate([far_halo[0], far_mid[0], far_halo[1]], 0)
        far_taps = tap_stack(far_act, rows, spread, (0, 1, 2))
        pieces = []
        for k in (1, 0, 2):
            grad_k = jnp.dot(
                own_taps[:, k].T, cot_mine, preferred_element_type=jnp.float32
            ) + jnp.dot(far_taps[:, k].T, far_mid[1], preferred_element_type=jnp.float32)
            pieces.extend(jnp.split(grad_k, 2, 0))
        totals = line_total(pieces)
        by_k = {k: jnp.concatenate(totals[2 * n : 2 * n + 2], 0) for n, k in enumerate((1, 0, 2))}
        weight_grad = jnp.stack([by_k[0], by_k[1], by_k[2]])
    else:
        lo = jnp.where(c == 0, local_cot, par_cot)
        hi = jnp.where(c == 0, par_cot, local_cot)
        cot_full = jnp.concatenate([lo, hi], 1)
        partial = jnp.einsum("tki,to->kio", own_taps, cot_full, preferred_element_type=jnp.float32)
        summed = lax.psum_scatter(partial, "batch", scatter_dimension=2, tiled=True)
        weight_grad = lax.psum(summed, "seq")
    return (block_out[None], input_grad[None], weight_grad)


def solution(mesh):
    in_specs = (
        P(("group", "batch"), "seq", "chan"),
        P(None, "chan", None),
        P(("group", "batch"), "seq", "chan"),
    )
    out_specs = (
        P(("group", "batch"), "seq", "chan"),
        P(("group", "batch"), "seq", "chan"),
        P("group", "chan", "batch"),
    )
    return jax.shard_map(shards, mesh=mesh, in_specs=in_specs, out_specs=out_specs, check_vma=False)
```

```python
import jax
import jax.numpy as jnp
from jax import lax
from jax.sharding import PartitionSpec as P

SWAP = [(0, 1), (1, 0)]


def shift_from(block, axis, distance):
    size = lax.axis_size(axis)
    route = [(i - distance, i) for i in range(size) if 0 <= i - distance < size]
    return lax.ppermute(block, axis, route)


def half_of(array, index, axis):
    size = array.shape[axis] // 2
    return lax.dynamic_slice_in_dim(array, index * size, size, axis)


def tap_stack(ext, rows, spread, order):
    return jnp.stack([ext[k * spread : k * spread + rows] for k in order], 1)


def line_total(pieces):
    position = lax.axis_index("seq")
    inner = (position == 1) | (position == 2)
    inward, outward, middle = [(0, 1), (3, 2)], [(1, 0), (2, 3)], [(1, 2), (2, 1)]
    count = len(pieces)
    pairs, wholes, totals = {}, {}, {}
    for step in range(count + 2):
        going_in = step < count
        going_out = step >= 2
        if going_in and going_out:
            sent = jnp.where(inner, wholes[step - 2], pieces[step])
            got = lax.ppermute(sent, "seq", inward + outward)
        elif going_in:
            got = lax.ppermute(pieces[step], "seq", inward)
        else:
            got = lax.ppermute(wholes[step - 2], "seq", outward)
        if going_in:
            pairs[step] = pieces[step] + got
        if going_out:
            totals[step - 2] = jnp.where(inner, wholes[step - 2], got)
        if 1 <= step <= count:
            ready = pairs[step - 1]
            wholes[step - 1] = ready + lax.ppermute(ready, "seq", middle)
    return [totals[n] for n in range(count)]


def shards(seq_in, conv_weight, cotangent):
    local_in = seq_in[0]
    local_cot = cotangent[0]
    rows = local_in.shape[0] // 2
    width = local_in.shape[1]
    spread = rows // 2
    c = lax.axis_index("chan")
    pooled = 0.5 * (local_in[0::2].astype(jnp.float32) + local_in[1::2].astype(jnp.float32))
    activation = jax.nn.gelu(pooled).astype(jnp.bfloat16)

    both = jnp.stack([activation, local_cot])
    par_mid = lax.ppermute(both, "chan", SWAP)
    from_prev = shift_from(both[:, rows - spread :], "seq", 1)
    from_next = shift_from(both[:, :spread], "seq", -1)
    par_halo = lax.ppermute(jnp.stack([from_prev, from_next]), "chan", SWAP)
    own_ext = jnp.concatenate([from_prev, both, from_next], 1)
    par_ext = jnp.concatenate([par_halo[0], par_mid, par_halo[1]], 1)

    w_own = half_of(conv_weight, c, 2)
    w_other = half_of(conv_weight, 1 - c, 2)
    w_par = lax.ppermute(w_other, "chan", SWAP)

    conv_out = jnp.einsum(
        "tki,kio->to", tap_stack(own_ext[0], rows, spread, (0, 1, 2)), w_own,
        preferred_element_type=jnp.float32,
    ) + jnp.einsum(
        "tki,kio->to", tap_stack(par_ext[0], rows, spread, (0, 1, 2)), w_par,
        preferred_element_type=jnp.float32,
    )
    block_out = (pooled + conv_out).astype(jnp.bfloat16)

    activ_grad = jnp.einsum(
        "tko,kio->ti", tap_stack(own_ext[1], rows, spread, (2, 1, 0)), w_own,
        preferred_element_type=jnp.float32,
    ) + jnp.einsum(
        "tko,kio->ti", tap_stack(par_ext[1], rows, spread, (2, 1, 0)), w_other,
        preferred_element_type=jnp.float32,
    )
    unused, gelu_back = jax.vjp(jax.nn.gelu, pooled)
    pooled_grad = local_cot.astype(jnp.float32) + gelu_back(activ_grad)[0]
    input_grad = jnp.repeat(0.5 * pooled_grad, 2, axis=0).astype(jnp.bfloat16)

    own_taps = tap_stack(own_ext[0], rows, spread, (0, 1, 2))
    par_cot = par_mid[1]
    batch_count = lax.axis_size("batch")
    seq_count = lax.axis_size("seq")
    if batch_count == 2 and seq_count == 4:
        b = lax.axis_index("batch")
        cot_mine = jnp.where(b == c, local_cot, par_cot)
        cot_theirs = jnp.where(b == c, par_cot, local_cot)
        far_mid = lax.ppermute(jnp.stack([activation, cot_theirs]), "batch", SWAP)
        far_halo = lax.ppermute(jnp.stack([from_prev[0], from_next[0]]), "batch", SWAP)
        far_act = jnp.concatenate([far_halo[0], far_mid[0], far_halo[1]], 0)
        far_taps = tap_stack(far_act, rows, spread, (0, 1, 2))
        pieces = []
        for k in (1, 0, 2):
            grad_k = jnp.dot(
                own_taps[:, k].T, cot_mine, preferred_element_type=jnp.float32
            ) + jnp.dot(far_taps[:, k].T, far_mid[1], preferred_element_type=jnp.float32)
            pieces.extend(jnp.split(grad_k, 2, 0))
        totals = line_total(pieces)
        by_k = {k: jnp.concatenate(totals[2 * n : 2 * n + 2], 0) for n, k in enumerate((1, 0, 2))}
        weight_grad = jnp.stack([by_k[0], by_k[1], by_k[2]])
    else:
        lo = jnp.where(c == 0, local_cot, par_cot)
        hi = jnp.where(c == 0, par_cot, local_cot)
        cot_full = jnp.concatenate([lo, hi], 1)
        partial = jnp.einsum("tki,to->kio", own_taps, cot_full, preferred_element_type=jnp.float32)
        summed = lax.psum_scatter(partial, "batch", scatter_dimension=2, tiled=True)
        weight_grad = lax.psum(summed, "seq")
    return (block_out[None], input_grad[None], weight_grad)


def solution(mesh):
    in_specs = (
        P(("group", "batch"), "seq", "chan"),
        P(None, "chan", None),
        P(("group", "batch"), "seq", "chan"),
    )
    out_specs = (
        P(("group", "batch"), "seq", "chan"),
        P(("group", "batch"), "seq", "chan"),
        P("group", "chan", "batch"),
    )
    return jax.shard_map(shards, mesh=mesh, in_specs=in_specs, out_specs=out_specs, check_vma=False)
```

```python
import jax
import jax.numpy as jnp
from jax import lax
from jax.sharding import PartitionSpec as P

SWAP = [(0, 1), (1, 0)]


def shift_from(block, axis, distance):
    size = lax.axis_size(axis)
    route = [(i - distance, i) for i in range(size) if 0 <= i - distance < size]
    return lax.ppermute(block, axis, route)


def half_of(array, index, axis):
    size = array.shape[axis] // 2
    return lax.dynamic_slice_in_dim(array, index * size, size, axis)


def tap_stack(ext, rows, spread, order):
    return jnp.stack([ext[k * spread : k * spread + rows] for k in order], 1)


def line_total(pieces):
    position = lax.axis_index("seq")
    inner = (position == 1) | (position == 2)
    inward, outward, middle = [(0, 1), (3, 2)], [(1, 0), (2, 3)], [(1, 2), (2, 1)]
    count = len(pieces)
    pairs, wholes, totals = {}, {}, {}
    for step in range(count + 2):
        going_in = step < count
        going_out = step >= 2
        if going_in and going_out:
            sent = jnp.where(inner, wholes[step - 2], pieces[step])
            got = lax.ppermute(sent, "seq", inward + outward)
        elif going_in:
            got = lax.ppermute(pieces[step], "seq", inward)
        else:
            got = lax.ppermute(wholes[step - 2], "seq", outward)
        if going_in:
            pairs[step] = pieces[step] + got
        if going_out:
            totals[step - 2] = jnp.where(inner, wholes[step - 2], got)
        if 1 <= step <= count:
            ready = pairs[step - 1]
            wholes[step - 1] = ready + lax.ppermute(ready, "seq", middle)
    return [totals[n] for n in range(count)]


def shards(seq_in, conv_weight, cotangent):
    local_in = seq_in[0]
    local_cot = cotangent[0]
    rows = local_in.shape[0] // 2
    width = local_in.shape[1]
    spread = rows // 2
    c = lax.axis_index("chan")
    pairing = lax.broadcasted_iota(jnp.int32, (rows, 2 * rows), 1) // 2 == lax.broadcasted_iota(
        jnp.int32, (rows, 2 * rows), 0
    )
    pairing = jnp.where(pairing, 0.5, 0.0).astype(jnp.bfloat16)
    pooled = jnp.dot(pairing, local_in, preferred_element_type=jnp.float32)
    activation = jax.nn.gelu(pooled).astype(jnp.bfloat16)

    both = jnp.stack([activation, local_cot])
    par_mid = lax.ppermute(both, "chan", SWAP)
    from_prev = shift_from(both[:, rows - spread :], "seq", 1)
    from_next = shift_from(both[:, :spread], "seq", -1)
    par_halo = lax.ppermute(jnp.stack([from_prev, from_next]), "chan", SWAP)
    own_ext = jnp.concatenate([from_prev, both, from_next], 1)
    par_ext = jnp.concatenate([par_halo[0], par_mid, par_halo[1]], 1)

    w_own = half_of(conv_weight, c, 2)
    w_other = half_of(conv_weight, 1 - c, 2)
    w_par = lax.ppermute(w_other, "chan", SWAP)

    conv_out = jnp.einsum(
        "tki,kio->to", tap_stack(own_ext[0], rows, spread, (0, 1, 2)), w_own,
        preferred_element_type=jnp.float32,
    ) + jnp.einsum(
        "tki,kio->to", tap_stack(par_ext[0], rows, spread, (0, 1, 2)), w_par,
        preferred_element_type=jnp.float32,
    )
    block_out = (pooled + conv_out).astype(jnp.bfloat16)

    activ_grad = jnp.einsum(
        "tko,kio->ti", tap_stack(own_ext[1], rows, spread, (2, 1, 0)), w_own,
        preferred_element_type=jnp.float32,
    ) + jnp.einsum(
        "tko,kio->ti", tap_stack(par_ext[1], rows, spread, (2, 1, 0)), w_other,
        preferred_element_type=jnp.float32,
    )
    unused, gelu_back = jax.vjp(jax.nn.gelu, pooled)
    pooled_grad = local_cot.astype(jnp.float32) + gelu_back(activ_grad)[0]
    input_grad = jnp.repeat(0.5 * pooled_grad, 2, axis=0).astype(jnp.bfloat16)

    own_taps = tap_stack(own_ext[0], rows, spread, (0, 1, 2))
    par_cot = par_mid[1]
    batch_count = lax.axis_size("batch")
    seq_count = lax.axis_size("seq")
    if batch_count == 2:
        b = lax.axis_index("batch")
        cot_mine = jnp.where(b == c, local_cot, par_cot)
        same_core = lax.ppermute(local_cot, ("batch", "chan"), [(2, 0), (1, 3)])
        cross_core = lax.ppermute(local_cot, ("batch", "chan"), [(2, 1), (1, 2)])
        far_cot = jnp.where(b == c, same_core, cross_core)
        far_mid = lax.ppermute(activation, "batch", SWAP)
        far_halo = lax.ppermute(jnp.stack([from_prev[0], from_next[0]]), "batch", SWAP)
        far_act = jnp.concatenate([far_halo[0], far_mid, far_halo[1]], 0)
        far_taps = tap_stack(far_act, rows, spread, (0, 1, 2))
        by_k = {}
        previous = None
        for k in (1, 0, 2):
            grad_k = jnp.dot(
                own_taps[:, k].T, cot_mine, preferred_element_type=jnp.float32
            ) + jnp.dot(far_taps[:, k].T, far_cot, preferred_element_type=jnp.float32)
            if previous is not None:
                grad_k, previous = lax.optimization_barrier((grad_k, previous))
            by_k[k] = lax.psum(grad_k, "seq")
            previous = by_k[k]
        weight_grad = jnp.stack([by_k[0], by_k[1], by_k[2]])
    else:
        lo = jnp.where(c == 0, local_cot, par_cot)
        hi = jnp.where(c == 0, par_cot, local_cot)
        cot_full = jnp.concatenate([lo, hi], 1)
        partial = jnp.einsum("tki,to->kio", own_taps, cot_full, preferred_element_type=jnp.float32)
        summed = lax.psum_scatter(partial, "batch", scatter_dimension=2, tiled=True)
        weight_grad = lax.psum(summed, "seq")
    return (block_out[None], input_grad[None], weight_grad)


def solution(mesh):
    in_specs = (
        P(("group", "batch"), "seq", "chan"),
        P(None, "chan", None),
        P(("group", "batch"), "seq", "chan"),
    )
    out_specs = (
        P(("group", "batch"), "seq", "chan"),
        P(("group", "batch"), "seq", "chan"),
        P("group", "chan", "batch"),
    )
    return jax.shard_map(shards, mesh=mesh, in_specs=in_specs, out_specs=out_specs, check_vma=False)
```

```python
import jax
import jax.numpy as jnp
from jax import lax
from jax.sharding import PartitionSpec as P

SWAP = [(0, 1), (1, 0)]


def shift_from(block, axis, distance):
    size = lax.axis_size(axis)
    route = [(i - distance, i) for i in range(size) if 0 <= i - distance < size]
    return lax.ppermute(block, axis, route)


def half_of(array, index, axis):
    size = array.shape[axis] // 2
    return lax.dynamic_slice_in_dim(array, index * size, size, axis)


def tap_stack(ext, rows, spread, order):
    return jnp.stack([ext[k * spread : k * spread + rows] for k in order], 1)


def line_total(pieces):
    position = lax.axis_index("seq")
    inner = (position == 1) | (position == 2)
    inward, outward, middle = [(0, 1), (3, 2)], [(1, 0), (2, 3)], [(1, 2), (2, 1)]
    count = len(pieces)
    pairs, wholes, totals = {}, {}, {}
    for step in range(count + 2):
        going_in = step < count
        going_out = step >= 2
        if going_in and going_out:
            sent = jnp.where(inner, wholes[step - 2], pieces[step])
            got = lax.ppermute(sent, "seq", inward + outward)
        elif going_in:
            got = lax.ppermute(pieces[step], "seq", inward)
        else:
            got = lax.ppermute(wholes[step - 2], "seq", outward)
        if going_in:
            pairs[step] = pieces[step] + got
        if going_out:
            totals[step - 2] = jnp.where(inner, wholes[step - 2], got)
        if 1 <= step <= count:
            ready = pairs[step - 1]
            wholes[step - 1] = ready + lax.ppermute(ready, "seq", middle)
    return [totals[n] for n in range(count)]


def seq_total(block):
    count = lax.axis_size("seq")
    s = lax.axis_index("seq")
    rows = block.shape[1] // count
    quarters = block.reshape(block.shape[0], count, rows, block.shape[2])
    mine = lax.dynamic_index_in_dim(quarters, s, 1, keepdims=False)
    for d in range(1, count):
        going = lax.dynamic_index_in_dim(quarters, (s + d) % count, 1, keepdims=False)
        mine = mine + lax.ppermute(going, "seq", [(j, (j + d) % count) for j in range(count)])
    gathered = [mine] + [
        lax.ppermute(mine, "seq", [(j, (j + d) % count) for j in range(count)]) for d in range(1, count)
    ]
    stacked = jnp.stack(gathered, 1)
    order = (s - jnp.arange(count)) % count
    return jnp.take(stacked, order, axis=1).reshape(block.shape)


def shards(seq_in, conv_weight, cotangent):
    local_in = seq_in[0]
    local_cot = cotangent[0]
    rows = local_in.shape[0] // 2
    width = local_in.shape[1]
    spread = rows // 2
    c = lax.axis_index("chan")
    pairing = lax.broadcasted_iota(jnp.int32, (rows, 2 * rows), 1) // 2 == lax.broadcasted_iota(
        jnp.int32, (rows, 2 * rows), 0
    )
    pairing = jnp.where(pairing, 0.5, 0.0).astype(jnp.bfloat16)
    pooled = jnp.dot(pairing, local_in, preferred_element_type=jnp.float32)
    activation = jax.nn.gelu(pooled).astype(jnp.bfloat16)

    both = jnp.stack([activation, local_cot])
    par_mid = lax.ppermute(both, "chan", SWAP)
    from_prev = shift_from(both[:, rows - spread :], "seq", 1)
    from_next = shift_from(both[:, :spread], "seq", -1)
    par_halo = lax.ppermute(jnp.stack([from_prev, from_next]), "chan", SWAP)
    own_ext = jnp.concatenate([from_prev, both, from_next], 1)
    par_ext = jnp.concatenate([par_halo[0], par_mid, par_halo[1]], 1)

    w_own = half_of(conv_weight, c, 2)
    w_other = half_of(conv_weight, 1 - c, 2)
    w_par = lax.ppermute(w_other, "chan", SWAP)

    conv_out = jnp.einsum(
        "tki,kio->to", tap_stack(own_ext[0], rows, spread, (0, 1, 2)), w_own,
        preferred_element_type=jnp.float32,
    ) + jnp.einsum(
        "tki,kio->to", tap_stack(par_ext[0], rows, spread, (0, 1, 2)), w_par,
        preferred_element_type=jnp.float32,
    )
    block_out = (pooled + conv_out).astype(jnp.bfloat16)

    activ_grad = jnp.einsum(
        "tko,kio->ti", tap_stack(own_ext[1], rows, spread, (2, 1, 0)), w_own,
        preferred_element_type=jnp.float32,
    ) + jnp.einsum(
        "tko,kio->ti", tap_stack(par_ext[1], rows, spread, (2, 1, 0)), w_other,
        preferred_element_type=jnp.float32,
    )
    unused, gelu_back = jax.vjp(jax.nn.gelu, pooled)
    pooled_grad = local_cot.astype(jnp.float32) + gelu_back(activ_grad)[0]
    input_grad = jnp.repeat(0.5 * pooled_grad, 2, axis=0).astype(jnp.bfloat16)

    own_taps = tap_stack(own_ext[0], rows, spread, (0, 1, 2))
    par_cot = par_mid[1]
    batch_count = lax.axis_size("batch")
    seq_count = lax.axis_size("seq")
    if batch_count == 2:
        b = lax.axis_index("batch")
        cot_mine = jnp.where(b == c, local_cot, par_cot)
        same_core = lax.ppermute(local_cot, ("batch", "chan"), [(2, 0), (1, 3)])
        cross_core = lax.ppermute(local_cot, ("batch", "chan"), [(2, 1), (1, 2)])
        far_cot = jnp.where(b == c, same_core, cross_core)
        far_mid = lax.ppermute(activation, "batch", SWAP)
        far_halo = lax.ppermute(jnp.stack([from_prev[0], from_next[0]]), "batch", SWAP)
        far_act = jnp.concatenate([far_halo[0], far_mid, far_halo[1]], 0)
        far_taps = tap_stack(far_act, rows, spread, (0, 1, 2))
        grads = {}
        for k in (1, 0, 2):
            grads[k] = jnp.dot(
                own_taps[:, k].T, cot_mine, preferred_element_type=jnp.float32
            ) + jnp.dot(far_taps[:, k].T, far_cot, preferred_element_type=jnp.float32)
        if seq_count == 4:
            middle = seq_total(grads[1][None])
            sides = seq_total(jnp.stack([grads[0], grads[2]]))
            weight_grad = jnp.concatenate([sides[:1], middle, sides[1:]], 0)
        else:
            weight_grad = lax.psum(jnp.stack([grads[0], grads[1], grads[2]]), "seq")
    else:
        lo = jnp.where(c == 0, local_cot, par_cot)
        hi = jnp.where(c == 0, par_cot, local_cot)
        cot_full = jnp.concatenate([lo, hi], 1)
        partial = jnp.einsum("tki,to->kio", own_taps, cot_full, preferred_element_type=jnp.float32)
        summed = lax.psum_scatter(partial, "batch", scatter_dimension=2, tiled=True)
        weight_grad = lax.psum(summed, "seq")
    return (block_out[None], input_grad[None], weight_grad)


def solution(mesh):
    in_specs = (
        P(("group", "batch"), "seq", "chan"),
        P(None, "chan", None),
        P(("group", "batch"), "seq", "chan"),
    )
    out_specs = (
        P(("group", "batch"), "seq", "chan"),
        P(("group", "batch"), "seq", "chan"),
        P("group", "chan", "batch"),
    )
    return jax.shard_map(shards, mesh=mesh, in_specs=in_specs, out_specs=out_specs, check_vma=False)
```

```python
import jax
import jax.numpy as jnp
from jax import lax
from jax.sharding import PartitionSpec as P

SWAP = [(0, 1), (1, 0)]


def shift_from(block, axis, distance):
    size = lax.axis_size(axis)
    route = [(i - distance, i) for i in range(size) if 0 <= i - distance < size]
    return lax.ppermute(block, axis, route)


def half_of(array, index, axis):
    size = array.shape[axis] // 2
    return lax.dynamic_slice_in_dim(array, index * size, size, axis)


def tap_stack(ext, rows, spread, order):
    return jnp.stack([ext[k * spread : k * spread + rows] for k in order], 1)


def line_total(pieces):
    position = lax.axis_index("seq")
    inner = (position == 1) | (position == 2)
    inward, outward, middle = [(0, 1), (3, 2)], [(1, 0), (2, 3)], [(1, 2), (2, 1)]
    count = len(pieces)
    pairs, wholes, totals = {}, {}, {}
    for step in range(count + 2):
        going_in = step < count
        going_out = step >= 2
        if going_in and going_out:
            sent = jnp.where(inner, wholes[step - 2], pieces[step])
            got = lax.ppermute(sent, "seq", inward + outward)
        elif going_in:
            got = lax.ppermute(pieces[step], "seq", inward)
        else:
            got = lax.ppermute(wholes[step - 2], "seq", outward)
        if going_in:
            pairs[step] = pieces[step] + got
        if going_out:
            totals[step - 2] = jnp.where(inner, wholes[step - 2], got)
        if 1 <= step <= count:
            ready = pairs[step - 1]
            wholes[step - 1] = ready + lax.ppermute(ready, "seq", middle)
    return [totals[n] for n in range(count)]


def seq_total(block):
    count = lax.axis_size("seq")
    s = lax.axis_index("seq")
    rows = block.shape[1] // count
    quarters = block.reshape(block.shape[0], count, rows, block.shape[2])
    mine = lax.dynamic_index_in_dim(quarters, s, 1, keepdims=False)
    for d in range(1, count):
        going = lax.dynamic_index_in_dim(quarters, (s + d) % count, 1, keepdims=False)
        mine = mine + lax.ppermute(going, "seq", [(j, (j + d) % count) for j in range(count)])
    mine = mine.astype(jnp.bfloat16)
    gathered = [mine] + [
        lax.ppermute(mine, "seq", [(j, (j + d) % count) for j in range(count)]) for d in range(1, count)
    ]
    stacked = jnp.stack(gathered, 1)
    order = (s - jnp.arange(count)) % count
    return jnp.take(stacked, order, axis=1).reshape(block.shape).astype(jnp.float32)


def shards(seq_in, conv_weight, cotangent):
    local_in = seq_in[0]
    local_cot = cotangent[0]
    rows = local_in.shape[0] // 2
    width = local_in.shape[1]
    spread = rows // 2
    c = lax.axis_index("chan")
    pairing = lax.broadcasted_iota(jnp.int32, (rows, 2 * rows), 1) // 2 == lax.broadcasted_iota(
        jnp.int32, (rows, 2 * rows), 0
    )
    pairing = jnp.where(pairing, 0.5, 0.0).astype(jnp.bfloat16)
    pooled = jnp.dot(pairing, local_in, preferred_element_type=jnp.float32)
    activation = jax.nn.gelu(pooled).astype(jnp.bfloat16)

    both = jnp.stack([activation, local_cot])
    par_mid = lax.ppermute(both, "chan", SWAP)
    from_prev = shift_from(both[:, rows - spread :], "seq", 1)
    from_next = shift_from(both[:, :spread], "seq", -1)
    par_halo = lax.ppermute(jnp.stack([from_prev, from_next]), "chan", SWAP)
    own_ext = jnp.concatenate([from_prev, both, from_next], 1)
    par_ext = jnp.concatenate([par_halo[0], par_mid, par_halo[1]], 1)

    w_own = half_of(conv_weight, c, 2)
    w_other = half_of(conv_weight, 1 - c, 2)
    w_par = lax.ppermute(w_other, "chan", SWAP)

    conv_out = jnp.einsum(
        "tki,kio->to", tap_stack(own_ext[0], rows, spread, (0, 1, 2)), w_own,
        preferred_element_type=jnp.float32,
    ) + jnp.einsum(
        "tki,kio->to", tap_stack(par_ext[0], rows, spread, (0, 1, 2)), w_par,
        preferred_element_type=jnp.float32,
    )
    block_out = (pooled + conv_out).astype(jnp.bfloat16)

    activ_grad = jnp.einsum(
        "tko,kio->ti", tap_stack(own_ext[1], rows, spread, (2, 1, 0)), w_own,
        preferred_element_type=jnp.float32,
    ) + jnp.einsum(
        "tko,kio->ti", tap_stack(par_ext[1], rows, spread, (2, 1, 0)), w_other,
        preferred_element_type=jnp.float32,
    )
    unused, gelu_back = jax.vjp(jax.nn.gelu, pooled)
    pooled_grad = local_cot.astype(jnp.float32) + gelu_back(activ_grad)[0]
    input_grad = jnp.repeat(0.5 * pooled_grad, 2, axis=0).astype(jnp.bfloat16)

    own_taps = tap_stack(own_ext[0], rows, spread, (0, 1, 2))
    par_cot = par_mid[1]
    batch_count = lax.axis_size("batch")
    seq_count = lax.axis_size("seq")
    if batch_count == 2:
        b = lax.axis_index("batch")
        cot_mine = jnp.where(b == c, local_cot, par_cot)
        same_core = lax.ppermute(local_cot, ("batch", "chan"), [(2, 0), (1, 3)])
        cross_core = lax.ppermute(local_cot, ("batch", "chan"), [(2, 1), (1, 2)])
        far_cot = jnp.where(b == c, same_core, cross_core)
        far_mid = lax.ppermute(activation, "batch", SWAP)
        far_halo = lax.ppermute(jnp.stack([from_prev[0], from_next[0]]), "batch", SWAP)
        far_act = jnp.concatenate([far_halo[0], far_mid, far_halo[1]], 0)
        far_taps = tap_stack(far_act, rows, spread, (0, 1, 2))
        grads = {}
        for k in (1, 0, 2):
            grads[k] = jnp.dot(
                own_taps[:, k].T, cot_mine, preferred_element_type=jnp.float32
            ) + jnp.dot(far_taps[:, k].T, far_cot, preferred_element_type=jnp.float32)
        if seq_count == 4:
            middle = seq_total(grads[1][None])
            sides = seq_total(jnp.stack([grads[0], grads[2]]))
            weight_grad = jnp.concatenate([sides[:1], middle, sides[1:]], 0)
        else:
            weight_grad = lax.psum(jnp.stack([grads[0], grads[1], grads[2]]), "seq")
    else:
        lo = jnp.where(c == 0, local_cot, par_cot)
        hi = jnp.where(c == 0, par_cot, local_cot)
        cot_full = jnp.concatenate([lo, hi], 1)
        partial = jnp.einsum("tki,to->kio", own_taps, cot_full, preferred_element_type=jnp.float32)
        summed = lax.psum_scatter(partial, "batch", scatter_dimension=2, tiled=True)
        weight_grad = lax.psum(summed, "seq")
    return (block_out[None], input_grad[None], weight_grad)


def solution(mesh):
    in_specs = (
        P(("group", "batch"), "seq", "chan"),
        P(None, "chan", None),
        P(("group", "batch"), "seq", "chan"),
    )
    out_specs = (
        P(("group", "batch"), "seq", "chan"),
        P(("group", "batch"), "seq", "chan"),
        P("group", "chan", "batch"),
    )
    return jax.shard_map(shards, mesh=mesh, in_specs=in_specs, out_specs=out_specs, check_vma=False)
```

```python
import jax
import jax.numpy as jnp
from jax import lax
from jax.sharding import PartitionSpec as P

SWAP = [(0, 1), (1, 0)]


def shift_from(block, axis, distance):
    size = lax.axis_size(axis)
    route = [(i - distance, i) for i in range(size) if 0 <= i - distance < size]
    return lax.ppermute(block, axis, route)


def half_of(array, index, axis):
    size = array.shape[axis] // 2
    return lax.dynamic_slice_in_dim(array, index * size, size, axis)


def tap_stack(ext, rows, spread, order):
    return jnp.stack([ext[k * spread : k * spread + rows] for k in order], 1)


def line_total(pieces):
    position = lax.axis_index("seq")
    inner = (position == 1) | (position == 2)
    inward, outward, middle = [(0, 1), (3, 2)], [(1, 0), (2, 3)], [(1, 2), (2, 1)]
    count = len(pieces)
    pairs, wholes, totals = {}, {}, {}
    for step in range(count + 2):
        going_in = step < count
        going_out = step >= 2
        if going_in and going_out:
            sent = jnp.where(inner, wholes[step - 2], pieces[step])
            got = lax.ppermute(sent, "seq", inward + outward)
        elif going_in:
            got = lax.ppermute(pieces[step], "seq", inward)
        else:
            got = lax.ppermute(wholes[step - 2], "seq", outward)
        if going_in:
            pairs[step] = pieces[step] + got
        if going_out:
            totals[step - 2] = jnp.where(inner, wholes[step - 2], got)
        if 1 <= step <= count:
            ready = pairs[step - 1]
            wholes[step - 1] = ready + lax.ppermute(ready, "seq", middle)
    return [totals[n] for n in range(count)]


def seq_total(block):
    count = lax.axis_size("seq")
    s = lax.axis_index("seq")
    rows = block.shape[1] // count
    quarters = block.reshape(block.shape[0], count, rows, block.shape[2])
    mine = lax.dynamic_index_in_dim(quarters, s, 1, keepdims=False)
    for d in range(1, count):
        going = lax.dynamic_index_in_dim(quarters, (s + d) % count, 1, keepdims=False)
        mine = mine + lax.ppermute(going, "seq", [(j, (j + d) % count) for j in range(count)])
    mine = mine.astype(jnp.bfloat16)
    gathered = [mine] + [
        lax.ppermute(mine, "seq", [(j, (j + d) % count) for j in range(count)]) for d in range(1, count)
    ]
    stacked = jnp.stack(gathered, 1)
    order = (s - jnp.arange(count)) % count
    return jnp.take(stacked, order, axis=1).reshape(block.shape).astype(jnp.float32)


def line_total(block):
    s = lax.axis_index("seq")
    odd = (s % 2) == 1
    low = s < 2
    rows = block.shape[0] // 4
    quarters = block.reshape(2, 2, rows, block.shape[1])
    even_set, odd_set = quarters[:, 0], quarters[:, 1]
    pairs, across = [(0, 1), (1, 0), (2, 3), (3, 2)], [(0, 2), (2, 0), (1, 3), (3, 1)]
    pair = jnp.where(odd, odd_set, even_set) + lax.ppermute(
        jnp.where(odd, even_set, odd_set), "seq", pairs
    )
    keep = jnp.where(low, pair[0], pair[1])
    give = jnp.where(low, pair[1], pair[0])
    total = (keep + lax.ppermute(give, "seq", across)).astype(jnp.bfloat16)
    other = lax.ppermute(total, "seq", across)
    own_set = jnp.where(low, jnp.stack([total, other]), jnp.stack([other, total]))
    far_set = lax.ppermute(own_set, "seq", pairs)
    evens = jnp.where(odd, far_set, own_set)
    odds = jnp.where(odd, own_set, far_set)
    return jnp.stack([evens, odds], 1).reshape(block.shape).astype(jnp.float32)


def shards(seq_in, conv_weight, cotangent):
    local_in = seq_in[0]
    local_cot = cotangent[0]
    rows = local_in.shape[0] // 2
    width = local_in.shape[1]
    spread = rows // 2
    c = lax.axis_index("chan")
    pairing = lax.broadcasted_iota(jnp.int32, (rows, 2 * rows), 1) // 2 == lax.broadcasted_iota(
        jnp.int32, (rows, 2 * rows), 0
    )
    pairing = jnp.where(pairing, 0.5, 0.0).astype(jnp.bfloat16)
    pooled = jnp.dot(pairing, local_in, preferred_element_type=jnp.float32)
    activation = jax.nn.gelu(pooled).astype(jnp.bfloat16)

    both = jnp.stack([activation, local_cot])
    par_mid = lax.ppermute(both, "chan", SWAP)
    from_prev = shift_from(both[:, rows - spread :], "seq", 1)
    from_next = shift_from(both[:, :spread], "seq", -1)
    par_halo = lax.ppermute(jnp.stack([from_prev, from_next]), "chan", SWAP)
    own_ext = jnp.concatenate([from_prev, both, from_next], 1)
    par_ext = jnp.concatenate([par_halo[0], par_mid, par_halo[1]], 1)

    w_own = half_of(conv_weight, c, 2)
    w_other = half_of(conv_weight, 1 - c, 2)
    w_par = lax.ppermute(w_other, "chan", SWAP)

    conv_out = jnp.einsum(
        "tki,kio->to", tap_stack(own_ext[0], rows, spread, (0, 1, 2)), w_own,
        preferred_element_type=jnp.float32,
    ) + jnp.einsum(
        "tki,kio->to", tap_stack(par_ext[0], rows, spread, (0, 1, 2)), w_par,
        preferred_element_type=jnp.float32,
    )
    block_out = (pooled + conv_out).astype(jnp.bfloat16)

    activ_grad = jnp.einsum(
        "tko,kio->ti", tap_stack(own_ext[1], rows, spread, (2, 1, 0)), w_own,
        preferred_element_type=jnp.float32,
    ) + jnp.einsum(
        "tko,kio->ti", tap_stack(par_ext[1], rows, spread, (2, 1, 0)), w_other,
        preferred_element_type=jnp.float32,
    )
    unused, gelu_back = jax.vjp(jax.nn.gelu, pooled)
    pooled_grad = local_cot.astype(jnp.float32) + gelu_back(activ_grad)[0]
    input_grad = jnp.repeat(0.5 * pooled_grad, 2, axis=0).astype(jnp.bfloat16)

    own_taps = tap_stack(own_ext[0], rows, spread, (0, 1, 2))
    par_cot = par_mid[1]
    batch_count = lax.axis_size("batch")
    seq_count = lax.axis_size("seq")
    if batch_count == 2:
        b = lax.axis_index("batch")
        cot_mine = jnp.where(b == c, local_cot, par_cot)
        same_core = lax.ppermute(local_cot, ("batch", "chan"), [(2, 0), (1, 3)])
        cross_core = lax.ppermute(local_cot, ("batch", "chan"), [(2, 1), (1, 2)])
        far_cot = jnp.where(b == c, same_core, cross_core)
        far_mid = lax.ppermute(activation, "batch", SWAP)
        far_halo = lax.ppermute(jnp.stack([from_prev[0], from_next[0]]), "batch", SWAP)
        far_act = jnp.concatenate([far_halo[0], far_mid, far_halo[1]], 0)
        far_taps = tap_stack(far_act, rows, spread, (0, 1, 2))
        grads = {}
        for k in (1, 0, 2):
            grads[k] = jnp.dot(
                own_taps[:, k].T, cot_mine, preferred_element_type=jnp.float32
            ) + jnp.dot(far_taps[:, k].T, far_cot, preferred_element_type=jnp.float32)
        if seq_count == 4:
            middle = line_total(grads[1])
            sides = line_total(jnp.concatenate([grads[0], grads[2]], 0))
            weight_grad = jnp.stack([sides[: middle.shape[0]], middle, sides[middle.shape[0] :]])
        else:
            weight_grad = lax.psum(jnp.stack([grads[0], grads[1], grads[2]]), "seq")
    else:
        lo = jnp.where(c == 0, local_cot, par_cot)
        hi = jnp.where(c == 0, par_cot, local_cot)
        cot_full = jnp.concatenate([lo, hi], 1)
        partial = jnp.einsum("tki,to->kio", own_taps, cot_full, preferred_element_type=jnp.float32)
        summed = lax.psum_scatter(partial, "batch", scatter_dimension=2, tiled=True)
        weight_grad = lax.psum(summed, "seq")
    return (block_out[None], input_grad[None], weight_grad)


def solution(mesh):
    in_specs = (
        P(("group", "batch"), "seq", "chan"),
        P(None, "chan", None),
        P(("group", "batch"), "seq", "chan"),
    )
    out_specs = (
        P(("group", "batch"), "seq", "chan"),
        P(("group", "batch"), "seq", "chan"),
        P("group", "chan", "batch"),
    )
    return jax.shard_map(shards, mesh=mesh, in_specs=in_specs, out_specs=out_specs, check_vma=False)
```

```python
import jax
import jax.numpy as jnp
from jax import lax
from jax.sharding import PartitionSpec as P

SWAP = [(0, 1), (1, 0)]


def shift_from(block, axis, distance):
    size = lax.axis_size(axis)
    route = [(i - distance, i) for i in range(size) if 0 <= i - distance < size]
    return lax.ppermute(block, axis, route)


def half_of(array, index, axis):
    size = array.shape[axis] // 2
    return lax.dynamic_slice_in_dim(array, index * size, size, axis)


def tap_stack(ext, rows, spread, order):
    return jnp.stack([ext[k * spread : k * spread + rows] for k in order], 1)


def line_total(pieces):
    position = lax.axis_index("seq")
    inner = (position == 1) | (position == 2)
    inward, outward, middle = [(0, 1), (3, 2)], [(1, 0), (2, 3)], [(1, 2), (2, 1)]
    count = len(pieces)
    pairs, wholes, totals = {}, {}, {}
    for step in range(count + 2):
        going_in = step < count
        going_out = step >= 2
        if going_in and going_out:
            sent = jnp.where(inner, wholes[step - 2], pieces[step])
            got = lax.ppermute(sent, "seq", inward + outward)
        elif going_in:
            got = lax.ppermute(pieces[step], "seq", inward)
        else:
            got = lax.ppermute(wholes[step - 2], "seq", outward)
        if going_in:
            pairs[step] = pieces[step] + got
        if going_out:
            totals[step - 2] = jnp.where(inner, wholes[step - 2], got)
        if 1 <= step <= count:
            ready = pairs[step - 1]
            wholes[step - 1] = ready + lax.ppermute(ready, "seq", middle)
    return [totals[n] for n in range(count)]


def seq_total(block):
    count = lax.axis_size("seq")
    s = lax.axis_index("seq")
    rows = block.shape[1] // count
    quarters = block.reshape(block.shape[0], count, rows, block.shape[2])
    mine = lax.dynamic_index_in_dim(quarters, s, 1, keepdims=False)
    for d in range(1, count):
        going = lax.dynamic_index_in_dim(quarters, (s + d) % count, 1, keepdims=False)
        mine = mine + lax.ppermute(going, "seq", [(j, (j + d) % count) for j in range(count)])
    mine = mine.astype(jnp.bfloat16)
    gathered = [mine] + [
        lax.ppermute(mine, "seq", [(j, (j + d) % count) for j in range(count)]) for d in range(1, count)
    ]
    stacked = jnp.stack(gathered, 1)
    order = (s - jnp.arange(count)) % count
    return jnp.take(stacked, order, axis=1).reshape(block.shape).astype(jnp.float32)


def line_total(block):
    s = lax.axis_index("seq")
    odd = (s % 2) == 1
    low = s < 2
    rows = block.shape[0] // 4
    quarters = block.reshape(2, 2, rows, block.shape[1])
    even_set, odd_set = quarters[:, 0], quarters[:, 1]
    pairs, across = [(0, 1), (1, 0), (2, 3), (3, 2)], [(0, 2), (2, 0), (1, 3), (3, 1)]
    pair = jnp.where(odd, odd_set, even_set) + lax.ppermute(
        jnp.where(odd, even_set, odd_set), "seq", pairs
    )
    keep = jnp.where(low, pair[0], pair[1])
    give = jnp.where(low, pair[1], pair[0])
    total = (keep + lax.ppermute(give, "seq", across)).astype(jnp.bfloat16)
    other = lax.ppermute(total, "seq", across)
    own_set = jnp.where(low, jnp.stack([total, other]), jnp.stack([other, total]))
    far_set = lax.ppermute(own_set, "seq", pairs)
    evens = jnp.where(odd, far_set, own_set)
    odds = jnp.where(odd, own_set, far_set)
    return jnp.stack([evens, odds], 1).reshape(block.shape).astype(jnp.float32)


def shards(seq_in, conv_weight, cotangent):
    local_in = seq_in[0]
    local_cot = cotangent[0]
    rows = local_in.shape[0] // 2
    width = local_in.shape[1]
    spread = rows // 2
    c = lax.axis_index("chan")
    pairing = lax.broadcasted_iota(jnp.int32, (rows, 2 * rows), 1) // 2 == lax.broadcasted_iota(
        jnp.int32, (rows, 2 * rows), 0
    )
    pairing = jnp.where(pairing, 0.5, 0.0).astype(jnp.bfloat16)
    pooled = jnp.dot(pairing, local_in, preferred_element_type=jnp.float32)
    activation = jax.nn.gelu(pooled).astype(jnp.bfloat16)

    both = jnp.stack([activation, local_cot])
    par_mid = lax.ppermute(both, "chan", SWAP)
    from_prev = shift_from(both[:, rows - spread :], "seq", 1)
    from_next = shift_from(both[:, :spread], "seq", -1)
    par_halo = lax.ppermute(jnp.stack([from_prev, from_next]), "chan", SWAP)
    own_ext = jnp.concatenate([from_prev, both, from_next], 1)
    par_ext = jnp.concatenate([par_halo[0], par_mid, par_halo[1]], 1)

    w_own = half_of(conv_weight, c, 2)
    w_other = half_of(conv_weight, 1 - c, 2)
    w_par = lax.ppermute(w_other, "chan", SWAP)

    conv_out = jnp.einsum(
        "tki,kio->to", tap_stack(own_ext[0], rows, spread, (0, 1, 2)), w_own,
        preferred_element_type=jnp.float32,
    ) + jnp.einsum(
        "tki,kio->to", tap_stack(par_ext[0], rows, spread, (0, 1, 2)), w_par,
        preferred_element_type=jnp.float32,
    )
    block_out = (pooled + conv_out).astype(jnp.bfloat16)

    activ_grad = jnp.einsum(
        "tko,kio->ti", tap_stack(own_ext[1], rows, spread, (2, 1, 0)), w_own,
        preferred_element_type=jnp.float32,
    ) + jnp.einsum(
        "tko,kio->ti", tap_stack(par_ext[1], rows, spread, (2, 1, 0)), w_other,
        preferred_element_type=jnp.float32,
    )
    unused, gelu_back = jax.vjp(jax.nn.gelu, pooled)
    pooled_grad = local_cot.astype(jnp.float32) + gelu_back(activ_grad)[0]
    input_grad = jnp.repeat(0.5 * pooled_grad, 2, axis=0).astype(jnp.bfloat16)

    own_taps = tap_stack(own_ext[0], rows, spread, (0, 1, 2))
    par_cot = par_mid[1]
    batch_count = lax.axis_size("batch")
    seq_count = lax.axis_size("seq")
    if batch_count == 2:
        b = lax.axis_index("batch")
        cot_mine = jnp.where(b == c, local_cot, par_cot)
        same_core = lax.ppermute(local_cot, ("batch", "chan"), [(2, 0), (1, 3)])
        cross_core = lax.ppermute(local_cot, ("batch", "chan"), [(2, 1), (1, 2)])
        far_cot = jnp.where(b == c, same_core, cross_core)
        far_mid = lax.ppermute(activation, "batch", SWAP)
        far_prev = lax.ppermute(
            activation[rows - spread :],
            ("seq", "batch"),
            [((j - 1) * 2 + 1 - h, j * 2 + h) for j in range(1, seq_count) for h in range(2)],
        )
        far_next = lax.ppermute(
            activation[:spread],
            ("seq", "batch"),
            [((j + 1) * 2 + 1 - h, j * 2 + h) for j in range(seq_count - 1) for h in range(2)],
        )
        far_act = jnp.concatenate([far_prev, far_mid, far_next], 0)
        far_taps = tap_stack(far_act, rows, spread, (0, 1, 2))
        grads = {}
        for k in (1, 0, 2):
            grads[k] = jnp.dot(
                own_taps[:, k].T, cot_mine, preferred_element_type=jnp.float32
            ) + jnp.dot(far_taps[:, k].T, far_cot, preferred_element_type=jnp.float32)
        if seq_count == 4:
            summed = line_total(jnp.concatenate([grads[0], grads[1], grads[2]], 0))
            weight_grad = summed.reshape(3, -1, summed.shape[1])
        else:
            weight_grad = lax.psum(jnp.stack([grads[0], grads[1], grads[2]]), "seq")
    else:
        lo = jnp.where(c == 0, local_cot, par_cot)
        hi = jnp.where(c == 0, par_cot, local_cot)
        cot_full = jnp.concatenate([lo, hi], 1)
        partial = jnp.einsum("tki,to->kio", own_taps, cot_full, preferred_element_type=jnp.float32)
        summed = lax.psum_scatter(partial, "batch", scatter_dimension=2, tiled=True)
        weight_grad = lax.psum(summed, "seq")
    return (block_out[None], input_grad[None], weight_grad)


def solution(mesh):
    in_specs = (
        P(("group", "batch"), "seq", "chan"),
        P(None, "chan", None),
        P(("group", "batch"), "seq", "chan"),
    )
    out_specs = (
        P(("group", "batch"), "seq", "chan"),
        P(("group", "batch"), "seq", "chan"),
        P("group", "chan", "batch"),
    )
    return jax.shard_map(shards, mesh=mesh, in_specs=in_specs, out_specs=out_specs, check_vma=False)
```

```python
import jax
import jax.numpy as jnp
from jax import lax
from jax.sharding import PartitionSpec as P

SWAP = [(0, 1), (1, 0)]


def shift_from(block, axis, distance):
    size = lax.axis_size(axis)
    route = [(i - distance, i) for i in range(size) if 0 <= i - distance < size]
    return lax.ppermute(block, axis, route)


def half_of(array, index, axis):
    size = array.shape[axis] // 2
    return lax.dynamic_slice_in_dim(array, index * size, size, axis)


def tap_stack(ext, rows, spread, order):
    return jnp.stack([ext[k * spread : k * spread + rows] for k in order], 1)


def line_total(pieces):
    position = lax.axis_index("seq")
    inner = (position == 1) | (position == 2)
    inward, outward, middle = [(0, 1), (3, 2)], [(1, 0), (2, 3)], [(1, 2), (2, 1)]
    count = len(pieces)
    pairs, wholes, totals = {}, {}, {}
    for step in range(count + 2):
        going_in = step < count
        going_out = step >= 2
        if going_in and going_out:
            sent = jnp.where(inner, wholes[step - 2], pieces[step])
            got = lax.ppermute(sent, "seq", inward + outward)
        elif going_in:
            got = lax.ppermute(pieces[step], "seq", inward)
        else:
            got = lax.ppermute(wholes[step - 2], "seq", outward)
        if going_in:
            pairs[step] = pieces[step] + got
        if going_out:
            totals[step - 2] = jnp.where(inner, wholes[step - 2], got)
        if 1 <= step <= count:
            ready = pairs[step - 1]
            wholes[step - 1] = ready + lax.ppermute(ready, "seq", middle)
    return [totals[n] for n in range(count)]


def seq_total(block):
    count = lax.axis_size("seq")
    s = lax.axis_index("seq")
    rows = block.shape[1] // count
    quarters = block.reshape(block.shape[0], count, rows, block.shape[2])
    mine = lax.dynamic_index_in_dim(quarters, s, 1, keepdims=False)
    for d in range(1, count):
        going = lax.dynamic_index_in_dim(quarters, (s + d) % count, 1, keepdims=False)
        mine = mine + lax.ppermute(going, "seq", [(j, (j + d) % count) for j in range(count)])
    mine = mine.astype(jnp.bfloat16)
    gathered = [mine] + [
        lax.ppermute(mine, "seq", [(j, (j + d) % count) for j in range(count)]) for d in range(1, count)
    ]
    stacked = jnp.stack(gathered, 1)
    order = (s - jnp.arange(count)) % count
    return jnp.take(stacked, order, axis=1).reshape(block.shape).astype(jnp.float32)


def line_total(block):
    s = lax.axis_index("seq")
    odd = (s % 2) == 1
    low = s < 2
    rows = block.shape[0] // 4
    quarters = block.reshape(2, 2, rows, block.shape[1])
    even_set, odd_set = quarters[:, 0], quarters[:, 1]
    pairs, across = [(0, 1), (1, 0), (2, 3), (3, 2)], [(0, 2), (2, 0), (1, 3), (3, 1)]
    pair = jnp.where(odd, odd_set, even_set) + lax.ppermute(
        jnp.where(odd, even_set, odd_set), "seq", pairs
    )
    keep = jnp.where(low, pair[0], pair[1])
    give = jnp.where(low, pair[1], pair[0])
    total = (keep + lax.ppermute(give, "seq", across)).astype(jnp.bfloat16)
    other = lax.ppermute(total, "seq", across)
    own_set = jnp.where(low, jnp.stack([total, other]), jnp.stack([other, total]))
    far_set = lax.ppermute(own_set, "seq", pairs)
    evens = jnp.where(odd, far_set, own_set)
    odds = jnp.where(odd, own_set, far_set)
    return jnp.stack([evens, odds], 1).reshape(block.shape).astype(jnp.float32)


def shards(seq_in, conv_weight, cotangent):
    local_in = seq_in[0]
    local_cot = cotangent[0]
    rows = local_in.shape[0] // 2
    width = local_in.shape[1]
    spread = rows // 2
    c = lax.axis_index("chan")
    pairing = lax.broadcasted_iota(jnp.int32, (rows, 2 * rows), 1) // 2 == lax.broadcasted_iota(
        jnp.int32, (rows, 2 * rows), 0
    )
    pairing = jnp.where(pairing, 0.5, 0.0).astype(jnp.bfloat16)
    pooled = jnp.dot(pairing, local_in, preferred_element_type=jnp.float32)
    activation = jax.nn.gelu(pooled).astype(jnp.bfloat16)

    both = jnp.stack([activation, local_cot])
    par_mid = lax.ppermute(both, "chan", SWAP)
    from_prev = shift_from(both[:, rows - spread :], "seq", 1)
    from_next = shift_from(both[:, :spread], "seq", -1)
    par_halo = lax.ppermute(jnp.stack([from_prev, from_next]), "chan", SWAP)
    own_ext = jnp.concatenate([from_prev, both, from_next], 1)
    par_ext = jnp.concatenate([par_halo[0], par_mid, par_halo[1]], 1)

    w_own = half_of(conv_weight, c, 2)
    w_other = half_of(conv_weight, 1 - c, 2)
    w_par = lax.ppermute(w_other, "chan", SWAP)

    conv_out = jnp.einsum(
        "tki,kio->to", tap_stack(own_ext[0], rows, spread, (0, 1, 2)), w_own,
        preferred_element_type=jnp.float32,
    ) + jnp.einsum(
        "tki,kio->to", tap_stack(par_ext[0], rows, spread, (0, 1, 2)), w_par,
        preferred_element_type=jnp.float32,
    )
    block_out = (pooled + conv_out).astype(jnp.bfloat16)

    activ_grad = jnp.einsum(
        "tko,kio->ti", tap_stack(own_ext[1], rows, spread, (2, 1, 0)), w_own,
        preferred_element_type=jnp.float32,
    ) + jnp.einsum(
        "tko,kio->ti", tap_stack(par_ext[1], rows, spread, (2, 1, 0)), w_other,
        preferred_element_type=jnp.float32,
    )
    unused, gelu_back = jax.vjp(jax.nn.gelu, pooled)
    pooled_grad = local_cot.astype(jnp.float32) + gelu_back(activ_grad)[0]
    input_grad = jnp.repeat(0.5 * pooled_grad, 2, axis=0).astype(jnp.bfloat16)

    own_taps = tap_stack(own_ext[0], rows, spread, (0, 1, 2))
    par_cot = par_mid[1]
    batch_count = lax.axis_size("batch")
    seq_count = lax.axis_size("seq")
    if batch_count == 2:
        b = lax.axis_index("batch")
        cot_mine = jnp.where(b == c, local_cot, par_cot)
        same_core = lax.ppermute(local_cot, ("batch", "chan"), [(2, 0), (1, 3)])
        cross_core = lax.ppermute(local_cot, ("batch", "chan"), [(2, 1), (1, 2)])
        far_cot = jnp.where(b == c, same_core, cross_core)
        far_mid = lax.ppermute(activation, "batch", SWAP)
        cot_next = shift_from(far_cot[:spread], "seq", -1)
        cot_prev = shift_from(far_cot[rows - spread :], "seq", 1)
        far_shifted = {
            1: far_cot,
            0: jnp.concatenate([far_cot[spread:], cot_next], 0),
            2: jnp.concatenate([cot_prev, far_cot[: rows - spread]], 0),
        }
        grads = {}
        for k in (1, 0, 2):
            grads[k] = jnp.dot(
                own_taps[:, k].T, cot_mine, preferred_element_type=jnp.float32
            ) + jnp.dot(far_mid.T, far_shifted[k], preferred_element_type=jnp.float32)
        if seq_count == 4:
            middle = line_total(grads[1])
            sides = line_total(jnp.concatenate([grads[0], grads[2]], 0))
            weight_grad = jnp.stack([sides[: middle.shape[0]], middle, sides[middle.shape[0] :]])
        else:
            weight_grad = lax.psum(jnp.stack([grads[0], grads[1], grads[2]]), "seq")
    else:
        lo = jnp.where(c == 0, local_cot, par_cot)
        hi = jnp.where(c == 0, par_cot, local_cot)
        cot_full = jnp.concatenate([lo, hi], 1)
        partial = jnp.einsum("tki,to->kio", own_taps, cot_full, preferred_element_type=jnp.float32)
        summed = lax.psum_scatter(partial, "batch", scatter_dimension=2, tiled=True)
        weight_grad = lax.psum(summed, "seq")
    return (block_out[None], input_grad[None], weight_grad)


def solution(mesh):
    in_specs = (
        P(("group", "batch"), "seq", "chan"),
        P(None, "chan", None),
        P(("group", "batch"), "seq", "chan"),
    )
    out_specs = (
        P(("group", "batch"), "seq", "chan"),
        P(("group", "batch"), "seq", "chan"),
        P("group", "chan", "batch"),
    )
    return jax.shard_map(shards, mesh=mesh, in_specs=in_specs, out_specs=out_specs, check_vma=False)
```

```python
import jax
import jax.numpy as jnp
from jax import lax
from jax.sharding import PartitionSpec as P

SWAP = [(0, 1), (1, 0)]


def shift_from(block, axis, distance):
    size = lax.axis_size(axis)
    route = [(i - distance, i) for i in range(size) if 0 <= i - distance < size]
    return lax.ppermute(block, axis, route)


def half_of(array, index, axis):
    size = array.shape[axis] // 2
    return lax.dynamic_slice_in_dim(array, index * size, size, axis)


def tap_stack(ext, rows, spread, order):
    return jnp.stack([ext[k * spread : k * spread + rows] for k in order], 1)


def line_total(pieces):
    position = lax.axis_index("seq")
    inner = (position == 1) | (position == 2)
    inward, outward, middle = [(0, 1), (3, 2)], [(1, 0), (2, 3)], [(1, 2), (2, 1)]
    count = len(pieces)
    pairs, wholes, totals = {}, {}, {}
    for step in range(count + 2):
        going_in = step < count
        going_out = step >= 2
        if going_in and going_out:
            sent = jnp.where(inner, wholes[step - 2], pieces[step])
            got = lax.ppermute(sent, "seq", inward + outward)
        elif going_in:
            got = lax.ppermute(pieces[step], "seq", inward)
        else:
            got = lax.ppermute(wholes[step - 2], "seq", outward)
        if going_in:
            pairs[step] = pieces[step] + got
        if going_out:
            totals[step - 2] = jnp.where(inner, wholes[step - 2], got)
        if 1 <= step <= count:
            ready = pairs[step - 1]
            wholes[step - 1] = ready + lax.ppermute(ready, "seq", middle)
    return [totals[n] for n in range(count)]


def seq_total(block):
    count = lax.axis_size("seq")
    s = lax.axis_index("seq")
    rows = block.shape[1] // count
    quarters = block.reshape(block.shape[0], count, rows, block.shape[2])
    mine = lax.dynamic_index_in_dim(quarters, s, 1, keepdims=False)
    for d in range(1, count):
        going = lax.dynamic_index_in_dim(quarters, (s + d) % count, 1, keepdims=False)
        mine = mine + lax.ppermute(going, "seq", [(j, (j + d) % count) for j in range(count)])
    mine = mine.astype(jnp.bfloat16)
    gathered = [mine] + [
        lax.ppermute(mine, "seq", [(j, (j + d) % count) for j in range(count)]) for d in range(1, count)
    ]
    stacked = jnp.stack(gathered, 1)
    order = (s - jnp.arange(count)) % count
    return jnp.take(stacked, order, axis=1).reshape(block.shape).astype(jnp.float32)


def line_total(block):
    s = lax.axis_index("seq")
    odd = (s % 2) == 1
    low = s < 2
    rows = block.shape[0] // 4
    quarters = block.reshape(2, 2, rows, block.shape[1])
    even_set, odd_set = quarters[:, 0], quarters[:, 1]
    pairs, across = [(0, 1), (1, 0), (2, 3), (3, 2)], [(0, 2), (2, 0), (1, 3), (3, 1)]
    pair = jnp.where(odd, odd_set, even_set) + lax.ppermute(
        jnp.where(odd, even_set, odd_set), "seq", pairs
    )
    keep = jnp.where(low, pair[0], pair[1])
    give = jnp.where(low, pair[1], pair[0])
    total = (keep + lax.ppermute(give, "seq", across)).astype(jnp.bfloat16)
    other = lax.ppermute(total, "seq", across)
    own_set = jnp.where(low, jnp.stack([total, other]), jnp.stack([other, total]))
    far_set = lax.ppermute(own_set, "seq", pairs)
    evens = jnp.where(odd, far_set, own_set)
    odds = jnp.where(odd, own_set, far_set)
    return jnp.stack([evens, odds], 1).reshape(block.shape).astype(jnp.float32)


def shards(seq_in, conv_weight, cotangent):
    local_in = seq_in[0]
    local_cot = cotangent[0]
    rows = local_in.shape[0] // 2
    width = local_in.shape[1]
    spread = rows // 2
    c = lax.axis_index("chan")
    pairing = lax.broadcasted_iota(jnp.int32, (rows, 2 * rows), 1) // 2 == lax.broadcasted_iota(
        jnp.int32, (rows, 2 * rows), 0
    )
    pairing = jnp.where(pairing, 0.5, 0.0).astype(jnp.bfloat16)
    pooled = jnp.dot(pairing, local_in, preferred_element_type=jnp.float32)
    activation = jax.nn.gelu(pooled).astype(jnp.bfloat16)

    both = jnp.stack([activation, local_cot])
    w_own = half_of(conv_weight, c, 2)
    w_other = half_of(conv_weight, 1 - c, 2)
    swapped = lax.ppermute(
        jnp.concatenate([both.reshape(-1, width), w_other.reshape(-1, width)], 0), "chan", SWAP
    )
    par_mid = swapped[: 2 * rows].reshape(both.shape)
    w_par = swapped[2 * rows :].reshape(w_other.shape)
    from_prev = shift_from(both[:, rows - spread :], "seq", 1)
    from_next = shift_from(both[:, :spread], "seq", -1)
    par_halo = lax.ppermute(jnp.stack([from_prev, from_next]), "chan", SWAP)
    own_ext = jnp.concatenate([from_prev, both, from_next], 1)
    par_ext = jnp.concatenate([par_halo[0], par_mid, par_halo[1]], 1)


    conv_out = jnp.einsum(
        "tki,kio->to", tap_stack(own_ext[0], rows, spread, (0, 1, 2)), w_own,
        preferred_element_type=jnp.float32,
    ) + jnp.einsum(
        "tki,kio->to", tap_stack(par_ext[0], rows, spread, (0, 1, 2)), w_par,
        preferred_element_type=jnp.float32,
    )
    block_out = (pooled + conv_out).astype(jnp.bfloat16)

    activ_grad = jnp.einsum(
        "tko,kio->ti", tap_stack(own_ext[1], rows, spread, (2, 1, 0)), w_own,
        preferred_element_type=jnp.float32,
    ) + jnp.einsum(
        "tko,kio->ti", tap_stack(par_ext[1], rows, spread, (2, 1, 0)), w_other,
        preferred_element_type=jnp.float32,
    )
    unused, gelu_back = jax.vjp(jax.nn.gelu, pooled)
    pooled_grad = local_cot.astype(jnp.float32) + gelu_back(activ_grad)[0]
    input_grad = jnp.repeat(0.5 * pooled_grad, 2, axis=0).astype(jnp.bfloat16)

    own_taps = tap_stack(own_ext[0], rows, spread, (0, 1, 2))
    par_cot = par_mid[1]
    batch_count = lax.axis_size("batch")
    seq_count = lax.axis_size("seq")
    if batch_count == 2:
        b = lax.axis_index("batch")
        cot_mine = jnp.where(b == c, local_cot, par_cot)
        same_core = lax.ppermute(local_cot, ("batch", "chan"), [(2, 0), (1, 3)])
        cross_core = lax.ppermute(local_cot, ("batch", "chan"), [(2, 1), (1, 2)])
        far_cot = jnp.where(b == c, same_core, cross_core)
        far_mid = lax.ppermute(activation, "batch", SWAP)
        cot_next = shift_from(far_cot[:spread], "seq", -1)
        cot_prev = shift_from(far_cot[rows - spread :], "seq", 1)
        far_shifted = {
            1: far_cot,
            0: jnp.concatenate([far_cot[spread:], cot_next], 0),
            2: jnp.concatenate([cot_prev, far_cot[: rows - spread]], 0),
        }
        grads = {}
        for k in (1, 0, 2):
            grads[k] = jnp.dot(
                own_taps[:, k].T, cot_mine, preferred_element_type=jnp.float32
            ) + jnp.dot(far_mid.T, far_shifted[k], preferred_element_type=jnp.float32)
        if seq_count == 4:
            middle = line_total(grads[1])
            sides = line_total(jnp.concatenate([grads[0], grads[2]], 0))
            weight_grad = jnp.stack([sides[: middle.shape[0]], middle, sides[middle.shape[0] :]])
        else:
            weight_grad = lax.psum(jnp.stack([grads[0], grads[1], grads[2]]), "seq")
    else:
        lo = jnp.where(c == 0, local_cot, par_cot)
        hi = jnp.where(c == 0, par_cot, local_cot)
        cot_full = jnp.concatenate([lo, hi], 1)
        partial = jnp.einsum("tki,to->kio", own_taps, cot_full, preferred_element_type=jnp.float32)
        summed = lax.psum_scatter(partial, "batch", scatter_dimension=2, tiled=True)
        weight_grad = lax.psum(summed, "seq")
    return (block_out[None], input_grad[None], weight_grad)


def solution(mesh):
    in_specs = (
        P(("group", "batch"), "seq", "chan"),
        P(None, "chan", None),
        P(("group", "batch"), "seq", "chan"),
    )
    out_specs = (
        P(("group", "batch"), "seq", "chan"),
        P(("group", "batch"), "seq", "chan"),
        P("group", "chan", "batch"),
    )
    return jax.shard_map(shards, mesh=mesh, in_specs=in_specs, out_specs=out_specs, check_vma=False)
```

```python
import jax
import jax.numpy as jnp
from jax import lax
from jax.sharding import PartitionSpec as P

SWAP = [(0, 1), (1, 0)]


def shift_from(block, axis, distance):
    size = lax.axis_size(axis)
    route = [(i - distance, i) for i in range(size) if 0 <= i - distance < size]
    return lax.ppermute(block, axis, route)


def half_of(array, index, axis):
    size = array.shape[axis] // 2
    return lax.dynamic_slice_in_dim(array, index * size, size, axis)


def tap_stack(ext, rows, spread, order):
    return jnp.stack([ext[k * spread : k * spread + rows] for k in order], 1)


def line_total(pieces):
    position = lax.axis_index("seq")
    inner = (position == 1) | (position == 2)
    inward, outward, middle = [(0, 1), (3, 2)], [(1, 0), (2, 3)], [(1, 2), (2, 1)]
    count = len(pieces)
    pairs, wholes, totals = {}, {}, {}
    for step in range(count + 2):
        going_in = step < count
        going_out = step >= 2
        if going_in and going_out:
            sent = jnp.where(inner, wholes[step - 2], pieces[step])
            got = lax.ppermute(sent, "seq", inward + outward)
        elif going_in:
            got = lax.ppermute(pieces[step], "seq", inward)
        else:
            got = lax.ppermute(wholes[step - 2], "seq", outward)
        if going_in:
            pairs[step] = pieces[step] + got
        if going_out:
            totals[step - 2] = jnp.where(inner, wholes[step - 2], got)
        if 1 <= step <= count:
            ready = pairs[step - 1]
            wholes[step - 1] = ready + lax.ppermute(ready, "seq", middle)
    return [totals[n] for n in range(count)]


def line_total(block):
    s = lax.axis_index("seq")
    odd = (s % 2) == 1
    low = s < 2
    rows = block.shape[0] // 4
    quarters = block.reshape(2, 2, rows, block.shape[1])
    even_set, odd_set = quarters[:, 0], quarters[:, 1]
    pairs, across = [(0, 1), (1, 0), (2, 3), (3, 2)], [(0, 2), (2, 0), (1, 3), (3, 1)]
    pair = jnp.where(odd, odd_set, even_set) + lax.ppermute(
        jnp.where(odd, even_set, odd_set), "seq", pairs
    )
    keep = jnp.where(low, pair[0], pair[1])
    give = jnp.where(low, pair[1], pair[0])
    total = (keep + lax.ppermute(give, "seq", across)).astype(jnp.bfloat16)
    other = lax.ppermute(total, "seq", across)
    own_set = jnp.where(low, jnp.stack([total, other]), jnp.stack([other, total]))
    far_set = lax.ppermute(own_set, "seq", pairs)
    evens = jnp.where(odd, far_set, own_set)
    odds = jnp.where(odd, own_set, far_set)
    return jnp.stack([evens, odds], 1).reshape(block.shape).astype(jnp.float32)


def shards(seq_in, conv_weight, cotangent):
    local_in = seq_in[0]
    local_cot = cotangent[0]
    rows = local_in.shape[0] // 2
    width = local_in.shape[1]
    spread = rows // 2
    c = lax.axis_index("chan")
    pairing = lax.broadcasted_iota(jnp.int32, (rows, 2 * rows), 1) // 2 == lax.broadcasted_iota(
        jnp.int32, (rows, 2 * rows), 0
    )
    pairing = jnp.where(pairing, 0.5, 0.0).astype(jnp.bfloat16)
    pooled = jnp.dot(pairing, local_in, preferred_element_type=jnp.float32)
    activation = jax.nn.gelu(pooled).astype(jnp.bfloat16)

    if lax.axis_size("batch") == 2:
        b = lax.axis_index("batch")
        same_core = lax.ppermute(local_cot, ("batch", "chan"), [(2, 0), (1, 3)])
        cross_core = lax.ppermute(local_cot, ("batch", "chan"), [(2, 1), (1, 2)])
        far_cot = jnp.where(b == c, same_core, cross_core)
        far_mid = lax.ppermute(activation, "batch", SWAP)

    both = jnp.stack([activation, local_cot])
    w_own = half_of(conv_weight, c, 2)
    w_other = half_of(conv_weight, 1 - c, 2)
    swapped = lax.ppermute(
        jnp.concatenate([both.reshape(-1, width), w_other.reshape(-1, width)], 0), "chan", SWAP
    )
    par_mid = swapped[: 2 * rows].reshape(both.shape)
    w_par = swapped[2 * rows :].reshape(w_other.shape)
    from_prev = shift_from(both[:, rows - spread :], "seq", 1)
    from_next = shift_from(both[:, :spread], "seq", -1)
    par_halo = lax.ppermute(jnp.stack([from_prev, from_next]), "chan", SWAP)
    own_ext = jnp.concatenate([from_prev, both, from_next], 1)
    par_ext = jnp.concatenate([par_halo[0], par_mid, par_halo[1]], 1)

    conv_out = jnp.einsum(
        "tki,kio->to", tap_stack(own_ext[0], rows, spread, (0, 1, 2)), w_own,
        preferred_element_type=jnp.float32,
    ) + jnp.einsum(
        "tki,kio->to", tap_stack(par_ext[0], rows, spread, (0, 1, 2)), w_par,
        preferred_element_type=jnp.float32,
    )
    block_out = (pooled + conv_out).astype(jnp.bfloat16)

    activ_grad = jnp.einsum(
        "tko,kio->ti", tap_stack(own_ext[1], rows, spread, (2, 1, 0)), w_own,
        preferred_element_type=jnp.float32,
    ) + jnp.einsum(
        "tko,kio->ti", tap_stack(par_ext[1], rows, spread, (2, 1, 0)), w_other,
        preferred_element_type=jnp.float32,
    )
    unused, gelu_back = jax.vjp(jax.nn.gelu, pooled)
    pooled_grad = local_cot.astype(jnp.float32) + gelu_back(activ_grad)[0]
    input_grad = jnp.repeat(0.5 * pooled_grad, 2, axis=0).astype(jnp.bfloat16)

    own_taps = tap_stack(own_ext[0], rows, spread, (0, 1, 2))
    par_cot = par_mid[1]
    batch_count = lax.axis_size("batch")
    seq_count = lax.axis_size("seq")
    if batch_count == 2:
        cot_mine = jnp.where(b == c, local_cot, par_cot)
        cot_next = shift_from(far_cot[:spread], "seq", -1)
        cot_prev = shift_from(far_cot[rows - spread :], "seq", 1)
        far_shifted = {
            1: far_cot,
            0: jnp.concatenate([far_cot[spread:], cot_next], 0),
            2: jnp.concatenate([cot_prev, far_cot[: rows - spread]], 0),
        }
        grads = {}
        for k in (1, 0, 2):
            grads[k] = jnp.dot(
                own_taps[:, k].T, cot_mine, preferred_element_type=jnp.float32
            ) + jnp.dot(far_mid.T, far_shifted[k], preferred_element_type=jnp.float32)
        if seq_count == 4:
            middle = line_total(grads[1])
            sides = line_total(jnp.concatenate([grads[0], grads[2]], 0))
            weight_grad = jnp.stack([sides[: middle.shape[0]], middle, sides[middle.shape[0] :]])
        else:
            weight_grad = lax.psum(jnp.stack([grads[0], grads[1], grads[2]]), "seq")
    else:
        lo = jnp.where(c == 0, local_cot, par_cot)
        hi = jnp.where(c == 0, par_cot, local_cot)
        cot_full = jnp.concatenate([lo, hi], 1)
        partial = jnp.einsum("tki,to->kio", own_taps, cot_full, preferred_element_type=jnp.float32)
        summed = lax.psum_scatter(partial, "batch", scatter_dimension=2, tiled=True)
        weight_grad = lax.psum(summed, "seq")
    return (block_out[None], input_grad[None], weight_grad)


def solution(mesh):
    in_specs = (
        P(("group", "batch"), "seq", "chan"),
        P(None, "chan", None),
        P(("group", "batch"), "seq", "chan"),
    )
    out_specs = (
        P(("group", "batch"), "seq", "chan"),
        P(("group", "batch"), "seq", "chan"),
        P("group", "chan", "batch"),
    )
    return jax.shard_map(shards, mesh=mesh, in_specs=in_specs, out_specs=out_specs, check_vma=False)
```

```python
import jax
import jax.numpy as jnp
from jax import lax
from jax.sharding import PartitionSpec as P

SWAP = [(0, 1), (1, 0)]


def shift_from(block, axis, distance):
    size = lax.axis_size(axis)
    route = [(i - distance, i) for i in range(size) if 0 <= i - distance < size]
    return lax.ppermute(block, axis, route)


def half_of(array, index, axis):
    size = array.shape[axis] // 2
    return lax.dynamic_slice_in_dim(array, index * size, size, axis)


def tap_stack(ext, rows, spread, order):
    return jnp.stack([ext[k * spread : k * spread + rows] for k in order], 1)


def line_total(pieces):
    position = lax.axis_index("seq")
    inner = (position == 1) | (position == 2)
    inward, outward, middle = [(0, 1), (3, 2)], [(1, 0), (2, 3)], [(1, 2), (2, 1)]
    count = len(pieces)
    pairs, wholes, totals = {}, {}, {}
    for step in range(count + 2):
        going_in = step < count
        going_out = step >= 2
        if going_in and going_out:
            sent = jnp.where(inner, wholes[step - 2], pieces[step])
            got = lax.ppermute(sent, "seq", inward + outward)
        elif going_in:
            got = lax.ppermute(pieces[step], "seq", inward)
        else:
            got = lax.ppermute(wholes[step - 2], "seq", outward)
        if going_in:
            pairs[step] = pieces[step] + got
        if going_out:
            totals[step - 2] = jnp.where(inner, wholes[step - 2], got)
        if 1 <= step <= count:
            ready = pairs[step - 1]
            wholes[step - 1] = ready + lax.ppermute(ready, "seq", middle)
    return [totals[n] for n in range(count)]


def line_total(block):
    s = lax.axis_index("seq")
    odd = (s % 2) == 1
    low = s < 2
    rows = block.shape[0] // 4
    quarters = block.reshape(2, 2, rows, block.shape[1])
    even_set, odd_set = quarters[:, 0], quarters[:, 1]
    pairs, across = [(0, 1), (1, 0), (2, 3), (3, 2)], [(0, 2), (2, 0), (1, 3), (3, 1)]
    pair = jnp.where(odd, odd_set, even_set) + lax.ppermute(
        jnp.where(odd, even_set, odd_set), "seq", pairs
    )
    keep = jnp.where(low, pair[0], pair[1])
    give = jnp.where(low, pair[1], pair[0])
    total = (keep + lax.ppermute(give, "seq", across)).astype(jnp.bfloat16)
    other = lax.ppermute(total, "seq", across)
    own_set = jnp.where(low, jnp.stack([total, other]), jnp.stack([other, total]))
    far_set = lax.ppermute(own_set, "seq", pairs)
    evens = jnp.where(odd, far_set, own_set)
    odds = jnp.where(odd, own_set, far_set)
    return jnp.stack([evens, odds], 1).reshape(block.shape).astype(jnp.float32)


def shards(seq_in, conv_weight, cotangent):
    local_in = seq_in[0]
    local_cot = cotangent[0]
    rows = local_in.shape[0] // 2
    width = local_in.shape[1]
    spread = rows // 2
    c = lax.axis_index("chan")
    pairing = lax.broadcasted_iota(jnp.int32, (rows, 2 * rows), 1) // 2 == lax.broadcasted_iota(
        jnp.int32, (rows, 2 * rows), 0
    )
    pairing = jnp.where(pairing, 0.5, 0.0).astype(jnp.bfloat16)
    pooled = jnp.dot(pairing, local_in, preferred_element_type=jnp.float32)
    activation = jax.nn.gelu(pooled).astype(jnp.bfloat16)

    if lax.axis_size("batch") == 2:
        b = lax.axis_index("batch")
        same_core = lax.ppermute(local_cot, ("batch", "chan"), [(2, 0), (1, 3)])
        cross_core = lax.ppermute(local_cot, ("batch", "chan"), [(2, 1), (1, 2)])
        far_cot = jnp.where(b == c, same_core, cross_core)
        far_mid = lax.ppermute(activation, "batch", SWAP)
        activation, far_mid = lax.optimization_barrier((activation, far_mid))

    both = jnp.stack([activation, local_cot])
    w_own = half_of(conv_weight, c, 2)
    w_other = half_of(conv_weight, 1 - c, 2)
    swapped = lax.ppermute(
        jnp.concatenate([both.reshape(-1, width), w_other.reshape(-1, width)], 0), "chan", SWAP
    )
    par_mid = swapped[: 2 * rows].reshape(both.shape)
    w_par = swapped[2 * rows :].reshape(w_other.shape)
    from_prev = shift_from(both[:, rows - spread :], "seq", 1)
    from_next = shift_from(both[:, :spread], "seq", -1)
    par_halo = lax.ppermute(jnp.stack([from_prev, from_next]), "chan", SWAP)
    own_ext = jnp.concatenate([from_prev, both, from_next], 1)
    par_ext = jnp.concatenate([par_halo[0], par_mid, par_halo[1]], 1)

    conv_out = jnp.einsum(
        "tki,kio->to", tap_stack(own_ext[0], rows, spread, (0, 1, 2)), w_own,
        preferred_element_type=jnp.float32,
    ) + jnp.einsum(
        "tki,kio->to", tap_stack(par_ext[0], rows, spread, (0, 1, 2)), w_par,
        preferred_element_type=jnp.float32,
    )
    block_out = (pooled + conv_out).astype(jnp.bfloat16)

    activ_grad = jnp.einsum(
        "tko,kio->ti", tap_stack(own_ext[1], rows, spread, (2, 1, 0)), w_own,
        preferred_element_type=jnp.float32,
    ) + jnp.einsum(
        "tko,kio->ti", tap_stack(par_ext[1], rows, spread, (2, 1, 0)), w_other,
        preferred_element_type=jnp.float32,
    )
    unused, gelu_back = jax.vjp(jax.nn.gelu, pooled)
    pooled_grad = local_cot.astype(jnp.float32) + gelu_back(activ_grad)[0]
    input_grad = jnp.repeat(0.5 * pooled_grad, 2, axis=0).astype(jnp.bfloat16)

    own_taps = tap_stack(own_ext[0], rows, spread, (0, 1, 2))
    par_cot = par_mid[1]
    batch_count = lax.axis_size("batch")
    seq_count = lax.axis_size("seq")
    if batch_count == 2:
        cot_mine = jnp.where(b == c, local_cot, par_cot)
        cot_next = shift_from(far_cot[:spread], "seq", -1)
        cot_prev = shift_from(far_cot[rows - spread :], "seq", 1)
        far_shifted = {
            1: far_cot,
            0: jnp.concatenate([far_cot[spread:], cot_next], 0),
            2: jnp.concatenate([cot_prev, far_cot[: rows - spread]], 0),
        }
        grads = {}
        for k in (1, 0, 2):
            grads[k] = jnp.dot(
                own_taps[:, k].T, cot_mine, preferred_element_type=jnp.float32
            ) + jnp.dot(far_mid.T, far_shifted[k], preferred_element_type=jnp.float32)
        if seq_count == 4:
            middle = line_total(grads[1])
            sides = line_total(jnp.concatenate([grads[0], grads[2]], 0))
            weight_grad = jnp.stack([sides[: middle.shape[0]], middle, sides[middle.shape[0] :]])
        else:
            weight_grad = lax.psum(jnp.stack([grads[0], grads[1], grads[2]]), "seq")
    else:
        lo = jnp.where(c == 0, local_cot, par_cot)
        hi = jnp.where(c == 0, par_cot, local_cot)
        cot_full = jnp.concatenate([lo, hi], 1)
        partial = jnp.einsum("tki,to->kio", own_taps, cot_full, preferred_element_type=jnp.float32)
        summed = lax.psum_scatter(partial, "batch", scatter_dimension=2, tiled=True)
        weight_grad = lax.psum(summed, "seq")
    return (block_out[None], input_grad[None], weight_grad)


def solution(mesh):
    in_specs = (
        P(("group", "batch"), "seq", "chan"),
        P(None, "chan", None),
        P(("group", "batch"), "seq", "chan"),
    )
    out_specs = (
        P(("group", "batch"), "seq", "chan"),
        P(("group", "batch"), "seq", "chan"),
        P("group", "chan", "batch"),
    )
    return jax.shard_map(shards, mesh=mesh, in_specs=in_specs, out_specs=out_specs, check_vma=False)
```

```python
import jax
import jax.numpy as jnp
from jax import lax
from jax.sharding import PartitionSpec as P

SWAP = [(0, 1), (1, 0)]


def shift_from(block, axis, distance):
    size = lax.axis_size(axis)
    route = [(i - distance, i) for i in range(size) if 0 <= i - distance < size]
    return lax.ppermute(block, axis, route)


def half_of(array, index, axis):
    size = array.shape[axis] // 2
    return lax.dynamic_slice_in_dim(array, index * size, size, axis)


def tap_stack(ext, rows, spread, order):
    return jnp.stack([ext[k * spread : k * spread + rows] for k in order], 1)


def line_total(pieces):
    position = lax.axis_index("seq")
    inner = (position == 1) | (position == 2)
    inward, outward, middle = [(0, 1), (3, 2)], [(1, 0), (2, 3)], [(1, 2), (2, 1)]
    count = len(pieces)
    pairs, wholes, totals = {}, {}, {}
    for step in range(count + 2):
        going_in = step < count
        going_out = step >= 2
        if going_in and going_out:
            sent = jnp.where(inner, wholes[step - 2], pieces[step])
            got = lax.ppermute(sent, "seq", inward + outward)
        elif going_in:
            got = lax.ppermute(pieces[step], "seq", inward)
        else:
            got = lax.ppermute(wholes[step - 2], "seq", outward)
        if going_in:
            pairs[step] = pieces[step] + got
        if going_out:
            totals[step - 2] = jnp.where(inner, wholes[step - 2], got)
        if 1 <= step <= count:
            ready = pairs[step - 1]
            wholes[step - 1] = ready + lax.ppermute(ready, "seq", middle)
    return [totals[n] for n in range(count)]


def line_total(block):
    s = lax.axis_index("seq")
    odd = (s % 2) == 1
    low = s < 2
    rows = block.shape[0] // 4
    quarters = block.reshape(2, 2, rows, block.shape[1])
    even_set, odd_set = quarters[:, 0], quarters[:, 1]
    pairs, across = [(0, 1), (1, 0), (2, 3), (3, 2)], [(0, 2), (2, 0), (1, 3), (3, 1)]
    pair = jnp.where(odd, odd_set, even_set) + lax.ppermute(
        jnp.where(odd, even_set, odd_set), "seq", pairs
    )
    keep = jnp.where(low, pair[0], pair[1])
    give = jnp.where(low, pair[1], pair[0])
    total = (keep + lax.ppermute(give, "seq", across)).astype(jnp.bfloat16)
    other = lax.ppermute(total, "seq", across)
    own_set = jnp.where(low, jnp.stack([total, other]), jnp.stack([other, total]))
    far_set = lax.ppermute(own_set, "seq", pairs)
    evens = jnp.where(odd, far_set, own_set)
    odds = jnp.where(odd, own_set, far_set)
    return jnp.stack([evens, odds], 1).reshape(block.shape).astype(jnp.float32)


def shards(seq_in, conv_weight, cotangent):
    local_in = seq_in[0]
    local_cot = cotangent[0]
    rows = local_in.shape[0] // 2
    width = local_in.shape[1]
    spread = rows // 2
    c = lax.axis_index("chan")
    pairing = lax.broadcasted_iota(jnp.int32, (rows, 2 * rows), 1) // 2 == lax.broadcasted_iota(
        jnp.int32, (rows, 2 * rows), 0
    )
    pairing = jnp.where(pairing, 0.5, 0.0).astype(jnp.bfloat16)
    pooled = jnp.dot(pairing, local_in, preferred_element_type=jnp.float32)
    activation = jax.nn.gelu(pooled).astype(jnp.bfloat16)

    if lax.axis_size("batch") == 2:
        b = lax.axis_index("batch")
        same_core = lax.ppermute(local_cot, ("batch", "chan"), [(2, 0), (1, 3)])
        cross_core = lax.ppermute(local_cot, ("batch", "chan"), [(2, 1), (1, 2)])
        far_cot = jnp.where(b == c, same_core, cross_core)
        far_mid = lax.ppermute(activation, "batch", SWAP)

    both = jnp.stack([activation, local_cot])
    w_own = half_of(conv_weight, c, 2)
    w_other = half_of(conv_weight, 1 - c, 2)
    swapped = lax.ppermute(
        jnp.concatenate([both.reshape(-1, width), w_other.reshape(-1, width)], 0), "chan", SWAP
    )
    par_mid = swapped[: 2 * rows].reshape(both.shape)
    w_par = swapped[2 * rows :].reshape(w_other.shape)
    from_prev = shift_from(both[:, rows - spread :], "seq", 1)
    from_next = shift_from(both[:, :spread], "seq", -1)
    par_halo = lax.ppermute(jnp.stack([from_prev, from_next]), "chan", SWAP)
    own_ext = jnp.concatenate([from_prev, both, from_next], 1)
    par_ext = jnp.concatenate([par_halo[0], par_mid, par_halo[1]], 1)

    conv_out = jnp.einsum(
        "tki,kio->to", tap_stack(own_ext[0], rows, spread, (0, 1, 2)), w_own,
        preferred_element_type=jnp.float32,
    ) + jnp.einsum(
        "tki,kio->to", tap_stack(par_ext[0], rows, spread, (0, 1, 2)), w_par,
        preferred_element_type=jnp.float32,
    )
    block_out = (pooled + conv_out).astype(jnp.bfloat16)

    activ_grad = jnp.einsum(
        "tko,kio->ti", tap_stack(own_ext[1], rows, spread, (2, 1, 0)), w_own,
        preferred_element_type=jnp.float32,
    ) + jnp.einsum(
        "tko,kio->ti", tap_stack(par_ext[1], rows, spread, (2, 1, 0)), w_other,
        preferred_element_type=jnp.float32,
    )
    unused, gelu_back = jax.vjp(jax.nn.gelu, pooled)
    pooled_grad = local_cot.astype(jnp.float32) + gelu_back(activ_grad)[0]
    input_grad = jnp.repeat(0.5 * pooled_grad, 2, axis=0).astype(jnp.bfloat16)

    own_taps = tap_stack(own_ext[0], rows, spread, (0, 1, 2))
    par_cot = par_mid[1]
    batch_count = lax.axis_size("batch")
    seq_count = lax.axis_size("seq")
    if batch_count == 2:
        cot_mine = jnp.where(b == c, local_cot, par_cot)
        centre = jnp.dot(own_taps[:, 1].T, cot_mine, preferred_element_type=jnp.float32) + jnp.dot(
            far_mid.T, far_cot, preferred_element_type=jnp.float32
        )
        centre, far_cot = lax.optimization_barrier((centre, far_cot))
        cot_next = shift_from(far_cot[:spread], "seq", -1)
        cot_prev = shift_from(far_cot[rows - spread :], "seq", 1)
        far_shifted = {
            1: far_cot,
            0: jnp.concatenate([far_cot[spread:], cot_next], 0),
            2: jnp.concatenate([cot_prev, far_cot[: rows - spread]], 0),
        }
        grads = {1: centre}
        for k in (0, 2):
            grads[k] = jnp.dot(
                own_taps[:, k].T, cot_mine, preferred_element_type=jnp.float32
            ) + jnp.dot(far_mid.T, far_shifted[k], preferred_element_type=jnp.float32)
        if seq_count == 4:
            middle = line_total(grads[1])
            sides = line_total(jnp.concatenate([grads[0], grads[2]], 0))
            weight_grad = jnp.stack([sides[: middle.shape[0]], middle, sides[middle.shape[0] :]])
        else:
            weight_grad = lax.psum(jnp.stack([grads[0], grads[1], grads[2]]), "seq")
    else:
        lo = jnp.where(c == 0, local_cot, par_cot)
        hi = jnp.where(c == 0, par_cot, local_cot)
        cot_full = jnp.concatenate([lo, hi], 1)
        partial = jnp.einsum("tki,to->kio", own_taps, cot_full, preferred_element_type=jnp.float32)
        summed = lax.psum_scatter(partial, "batch", scatter_dimension=2, tiled=True)
        weight_grad = lax.psum(summed, "seq")
    return (block_out[None], input_grad[None], weight_grad)


def solution(mesh):
    in_specs = (
        P(("group", "batch"), "seq", "chan"),
        P(None, "chan", None),
        P(("group", "batch"), "seq", "chan"),
    )
    out_specs = (
        P(("group", "batch"), "seq", "chan"),
        P(("group", "batch"), "seq", "chan"),
        P("group", "chan", "batch"),
    )
    return jax.shard_map(shards, mesh=mesh, in_specs=in_specs, out_specs=out_specs, check_vma=False)
```

```python
import jax
import jax.numpy as jnp
from jax import lax
from jax.sharding import PartitionSpec as P

SWAP = [(0, 1), (1, 0)]


def shift_from(block, axis, distance):
    size = lax.axis_size(axis)
    route = [(i - distance, i) for i in range(size) if 0 <= i - distance < size]
    return lax.ppermute(block, axis, route)


def half_of(array, index, axis):
    size = array.shape[axis] // 2
    return lax.dynamic_slice_in_dim(array, index * size, size, axis)


def tap_stack(ext, rows, spread, order):
    return jnp.stack([ext[k * spread : k * spread + rows] for k in order], 1)


def line_total(pieces):
    position = lax.axis_index("seq")
    inner = (position == 1) | (position == 2)
    inward, outward, middle = [(0, 1), (3, 2)], [(1, 0), (2, 3)], [(1, 2), (2, 1)]
    count = len(pieces)
    pairs, wholes, totals = {}, {}, {}
    for step in range(count + 2):
        going_in = step < count
        going_out = step >= 2
        if going_in and going_out:
            sent = jnp.where(inner, wholes[step - 2], pieces[step])
            got = lax.ppermute(sent, "seq", inward + outward)
        elif going_in:
            got = lax.ppermute(pieces[step], "seq", inward)
        else:
            got = lax.ppermute(wholes[step - 2], "seq", outward)
        if going_in:
            pairs[step] = pieces[step] + got
        if going_out:
            totals[step - 2] = jnp.where(inner, wholes[step - 2], got)
        if 1 <= step <= count:
            ready = pairs[step - 1]
            wholes[step - 1] = ready + lax.ppermute(ready, "seq", middle)
    return [totals[n] for n in range(count)]


def line_total(block):
    s = lax.axis_index("seq")
    odd = (s % 2) == 1
    low = s < 2
    rows = block.shape[0] // 4
    quarters = block.reshape(2, 2, rows, block.shape[1])
    even_set, odd_set = quarters[:, 0], quarters[:, 1]
    pairs, across = [(0, 1), (1, 0), (2, 3), (3, 2)], [(0, 2), (2, 0), (1, 3), (3, 1)]
    pair = jnp.where(odd, odd_set, even_set) + lax.ppermute(
        jnp.where(odd, even_set, odd_set), "seq", pairs
    )
    keep = jnp.where(low, pair[0], pair[1])
    give = jnp.where(low, pair[1], pair[0])
    total = (keep + lax.ppermute(give, "seq", across)).astype(jnp.bfloat16)
    other = lax.ppermute(total, "seq", across)
    own_set = jnp.where(low, jnp.stack([total, other]), jnp.stack([other, total]))
    far_set = lax.ppermute(own_set, "seq", pairs)
    evens = jnp.where(odd, far_set, own_set)
    odds = jnp.where(odd, own_set, far_set)
    return jnp.stack([evens, odds], 1).reshape(block.shape).astype(jnp.float32)


def shards(seq_in, conv_weight, cotangent):
    local_in = seq_in[0]
    local_cot = cotangent[0]
    rows = local_in.shape[0] // 2
    width = local_in.shape[1]
    spread = rows // 2
    c = lax.axis_index("chan")
    pairing = lax.broadcasted_iota(jnp.int32, (rows, 2 * rows), 1) // 2 == lax.broadcasted_iota(
        jnp.int32, (rows, 2 * rows), 0
    )
    pairing = jnp.where(pairing, 0.5, 0.0).astype(jnp.bfloat16)
    pooled = jnp.dot(pairing, local_in, preferred_element_type=jnp.float32)
    activation = jax.nn.gelu(pooled).astype(jnp.bfloat16)

    if lax.axis_size("batch") == 2:
        b = lax.axis_index("batch")
        same_core = lax.ppermute(local_cot, ("batch", "chan"), [(2, 0), (1, 3)])
        cross_core = lax.ppermute(local_cot, ("batch", "chan"), [(2, 1), (1, 2)])
        far_cot = jnp.where(b == c, same_core, cross_core)
        far_mid = lax.ppermute(activation, "batch", SWAP)

    both = jnp.stack([activation, local_cot])
    w_own = half_of(conv_weight, c, 2)
    w_other = half_of(conv_weight, 1 - c, 2)
    swapped = lax.ppermute(
        jnp.concatenate([both.reshape(-1, width), w_other.reshape(-1, width)], 0), "chan", SWAP
    )
    par_mid = swapped[: 2 * rows].reshape(both.shape)
    w_par = swapped[2 * rows :].reshape(w_other.shape)
    from_prev = shift_from(both[:, rows - spread :], "seq", 1)
    from_next = shift_from(both[:, :spread], "seq", -1)
    par_halo = lax.ppermute(jnp.stack([from_prev, from_next]), "chan", SWAP)
    own_ext = jnp.concatenate([from_prev, both, from_next], 1)
    par_ext = jnp.concatenate([par_halo[0], par_mid, par_halo[1]], 1)

    conv_out = jnp.einsum(
        "tki,kio->to", tap_stack(own_ext[0], rows, spread, (0, 1, 2)), w_own,
        preferred_element_type=jnp.float32,
    ) + jnp.einsum(
        "tki,kio->to", tap_stack(par_ext[0], rows, spread, (0, 1, 2)), w_par,
        preferred_element_type=jnp.float32,
    )
    block_out = (pooled + conv_out).astype(jnp.bfloat16)

    activ_grad = jnp.einsum(
        "tko,kio->ti", tap_stack(own_ext[1], rows, spread, (2, 1, 0)), w_own,
        preferred_element_type=jnp.float32,
    ) + jnp.einsum(
        "tko,kio->ti", tap_stack(par_ext[1], rows, spread, (2, 1, 0)), w_other,
        preferred_element_type=jnp.float32,
    )
    unused, gelu_back = jax.vjp(jax.nn.gelu, pooled)
    pooled_grad = local_cot.astype(jnp.float32) + gelu_back(activ_grad)[0]
    input_grad = jnp.repeat(0.5 * pooled_grad, 2, axis=0).astype(jnp.bfloat16)

    own_taps = tap_stack(own_ext[0], rows, spread, (0, 1, 2))
    par_cot = par_mid[1]
    batch_count = lax.axis_size("batch")
    seq_count = lax.axis_size("seq")
    if batch_count == 2:
        cot_mine = jnp.where(b == c, local_cot, par_cot)
        centre = jnp.dot(own_taps[:, 1].T, cot_mine, preferred_element_type=jnp.float32) + jnp.dot(
            far_mid.T, far_cot, preferred_element_type=jnp.float32
        )
        cot_next = shift_from(far_cot[:spread], "seq", -1)
        cot_prev = shift_from(far_cot[rows - spread :], "seq", 1)
        far_shifted = {
            1: far_cot,
            0: jnp.concatenate([far_cot[spread:], cot_next], 0),
            2: jnp.concatenate([cot_prev, far_cot[: rows - spread]], 0),
        }
        grads = {1: centre}
        for k in (0, 2):
            grads[k] = jnp.dot(
                own_taps[:, k].T, cot_mine, preferred_element_type=jnp.float32
            ) + jnp.dot(far_mid.T, far_shifted[k], preferred_element_type=jnp.float32)
        if seq_count == 4:
            middle = lax.psum(grads[1], "seq")
            sides = line_total(jnp.concatenate([grads[0], grads[2]], 0))
            weight_grad = jnp.stack([sides[: middle.shape[0]], middle, sides[middle.shape[0] :]])
        else:
            weight_grad = lax.psum(jnp.stack([grads[0], grads[1], grads[2]]), "seq")
    else:
        lo = jnp.where(c == 0, local_cot, par_cot)
        hi = jnp.where(c == 0, par_cot, local_cot)
        cot_full = jnp.concatenate([lo, hi], 1)
        partial = jnp.einsum("tki,to->kio", own_taps, cot_full, preferred_element_type=jnp.float32)
        summed = lax.psum_scatter(partial, "batch", scatter_dimension=2, tiled=True)
        weight_grad = lax.psum(summed, "seq")
    return (block_out[None], input_grad[None], weight_grad)


def solution(mesh):
    in_specs = (
        P(("group", "batch"), "seq", "chan"),
        P(None, "chan", None),
        P(("group", "batch"), "seq", "chan"),
    )
    out_specs = (
        P(("group", "batch"), "seq", "chan"),
        P(("group", "batch"), "seq", "chan"),
        P("group", "chan", "batch"),
    )
    return jax.shard_map(shards, mesh=mesh, in_specs=in_specs, out_specs=out_specs, check_vma=False)
```

```python
import jax
import jax.numpy as jnp
from jax import lax
from jax.sharding import PartitionSpec as P

SWAP = [(0, 1), (1, 0)]


def shift_from(block, axis, distance):
    size = lax.axis_size(axis)
    route = [(i - distance, i) for i in range(size) if 0 <= i - distance < size]
    return lax.ppermute(block, axis, route)


def half_of(array, index, axis):
    size = array.shape[axis] // 2
    return lax.dynamic_slice_in_dim(array, index * size, size, axis)


def tap_stack(ext, rows, spread, order):
    return jnp.stack([ext[k * spread : k * spread + rows] for k in order], 1)


def line_total(pieces):
    position = lax.axis_index("seq")
    inner = (position == 1) | (position == 2)
    inward, outward, middle = [(0, 1), (3, 2)], [(1, 0), (2, 3)], [(1, 2), (2, 1)]
    count = len(pieces)
    pairs, wholes, totals = {}, {}, {}
    for step in range(count + 2):
        going_in = step < count
        going_out = step >= 2
        if going_in and going_out:
            sent = jnp.where(inner, wholes[step - 2], pieces[step])
            got = lax.ppermute(sent, "seq", inward + outward)
        elif going_in:
            got = lax.ppermute(pieces[step], "seq", inward)
        else:
            got = lax.ppermute(wholes[step - 2], "seq", outward)
        if going_in:
            pairs[step] = pieces[step] + got
        if going_out:
            totals[step - 2] = jnp.where(inner, wholes[step - 2], got)
        if 1 <= step <= count:
            ready = pairs[step - 1]
            wholes[step - 1] = ready + lax.ppermute(ready, "seq", middle)
    return [totals[n] for n in range(count)]


def line_total(block):
    s = lax.axis_index("seq")
    odd = (s % 2) == 1
    low = s < 2
    rows = block.shape[0] // 4
    quarters = block.reshape(2, 2, rows, block.shape[1])
    even_set, odd_set = quarters[:, 0], quarters[:, 1]
    pairs, across = [(0, 1), (1, 0), (2, 3), (3, 2)], [(0, 2), (2, 0), (1, 3), (3, 1)]
    pair = jnp.where(odd, odd_set, even_set) + lax.ppermute(
        jnp.where(odd, even_set, odd_set), "seq", pairs
    )
    keep = jnp.where(low, pair[0], pair[1])
    give = jnp.where(low, pair[1], pair[0])
    total = (keep + lax.ppermute(give, "seq", across)).astype(jnp.bfloat16)
    other = lax.ppermute(total, "seq", across)
    own_set = jnp.where(low, jnp.stack([total, other]), jnp.stack([other, total]))
    far_set = lax.ppermute(own_set, "seq", pairs)
    evens = jnp.where(odd, far_set, own_set)
    odds = jnp.where(odd, own_set, far_set)
    return jnp.stack([evens, odds], 1).reshape(block.shape).astype(jnp.float32)


def shards(seq_in, conv_weight, cotangent):
    local_in = seq_in[0]
    local_cot = cotangent[0]
    rows = local_in.shape[0] // 2
    width = local_in.shape[1]
    spread = rows // 2
    c = lax.axis_index("chan")
    pairing = lax.broadcasted_iota(jnp.int32, (rows, 2 * rows), 1) // 2 == lax.broadcasted_iota(
        jnp.int32, (rows, 2 * rows), 0
    )
    pairing = jnp.where(pairing, 0.5, 0.0).astype(jnp.bfloat16)
    pooled = jnp.dot(pairing, local_in, preferred_element_type=jnp.float32)
    activation = jax.nn.gelu(pooled).astype(jnp.bfloat16)

    if lax.axis_size("batch") == 2:
        b = lax.axis_index("batch")
        same_core = lax.ppermute(local_cot, ("batch", "chan"), [(2, 0), (1, 3)])
        cross_core = lax.ppermute(local_cot, ("batch", "chan"), [(2, 1), (1, 2)])
        far_cot = jnp.where(b == c, same_core, cross_core)
        far_mid = lax.ppermute(activation, "batch", SWAP)

    both = jnp.stack([activation, local_cot])
    w_own = half_of(conv_weight, c, 2)
    w_other = half_of(conv_weight, 1 - c, 2)
    swapped = lax.ppermute(
        jnp.concatenate([both.reshape(-1, width), w_other.reshape(-1, width)], 0), "chan", SWAP
    )
    par_mid = swapped[: 2 * rows].reshape(both.shape)
    w_par = swapped[2 * rows :].reshape(w_other.shape)
    from_prev = shift_from(both[:, rows - spread :], "seq", 1)
    from_next = shift_from(both[:, :spread], "seq", -1)
    par_halo = lax.ppermute(jnp.stack([from_prev, from_next]), "chan", SWAP)
    own_ext = jnp.concatenate([from_prev, both, from_next], 1)
    par_ext = jnp.concatenate([par_halo[0], par_mid, par_halo[1]], 1)

    conv_out = jnp.einsum(
        "tki,kio->to", tap_stack(own_ext[0], rows, spread, (0, 1, 2)), w_own,
        preferred_element_type=jnp.float32,
    ) + jnp.einsum(
        "tki,kio->to", tap_stack(par_ext[0], rows, spread, (0, 1, 2)), w_par,
        preferred_element_type=jnp.float32,
    )
    block_out = (pooled + conv_out).astype(jnp.bfloat16)

    activ_grad = jnp.einsum(
        "tko,kio->ti", tap_stack(own_ext[1], rows, spread, (2, 1, 0)), w_own,
        preferred_element_type=jnp.float32,
    ) + jnp.einsum(
        "tko,kio->ti", tap_stack(par_ext[1], rows, spread, (2, 1, 0)), w_other,
        preferred_element_type=jnp.float32,
    )
    unused, gelu_back = jax.vjp(jax.nn.gelu, pooled)
    pooled_grad = local_cot.astype(jnp.float32) + gelu_back(activ_grad)[0]
    input_grad = jnp.repeat(0.5 * pooled_grad, 2, axis=0).astype(jnp.bfloat16)

    own_taps = tap_stack(own_ext[0], rows, spread, (0, 1, 2))
    par_cot = par_mid[1]
    batch_count = lax.axis_size("batch")
    seq_count = lax.axis_size("seq")
    if batch_count == 2:
        cot_mine = jnp.where(b == c, local_cot, par_cot)
        centre = jnp.dot(activation.T, cot_mine, preferred_element_type=jnp.float32) + jnp.dot(
            far_mid.T, far_cot, preferred_element_type=jnp.float32
        )
        cot_next = shift_from(far_cot[:spread], "seq", -1)
        cot_prev = shift_from(far_cot[rows - spread :], "seq", 1)
        far_shifted = {
            1: far_cot,
            0: jnp.concatenate([far_cot[spread:], cot_next], 0),
            2: jnp.concatenate([cot_prev, far_cot[: rows - spread]], 0),
        }
        grads = {1: centre}
        for k in (0, 2):
            grads[k] = jnp.dot(
                own_taps[:, k].T, cot_mine, preferred_element_type=jnp.float32
            ) + jnp.dot(far_mid.T, far_shifted[k], preferred_element_type=jnp.float32)
        if seq_count == 4:
            middle = line_total(grads[1])
            sides = line_total(jnp.concatenate([grads[0], grads[2]], 0))
            weight_grad = jnp.stack([sides[: middle.shape[0]], middle, sides[middle.shape[0] :]])
        else:
            weight_grad = lax.psum(jnp.stack([grads[0], grads[1], grads[2]]), "seq")
    else:
        lo = jnp.where(c == 0, local_cot, par_cot)
        hi = jnp.where(c == 0, par_cot, local_cot)
        cot_full = jnp.concatenate([lo, hi], 1)
        partial = jnp.einsum("tki,to->kio", own_taps, cot_full, preferred_element_type=jnp.float32)
        summed = lax.psum_scatter(partial, "batch", scatter_dimension=2, tiled=True)
        weight_grad = lax.psum(summed, "seq")
    return (block_out[None], input_grad[None], weight_grad)


def solution(mesh):
    in_specs = (
        P(("group", "batch"), "seq", "chan"),
        P(None, "chan", None),
        P(("group", "batch"), "seq", "chan"),
    )
    out_specs = (
        P(("group", "batch"), "seq", "chan"),
        P(("group", "batch"), "seq", "chan"),
        P("group", "chan", "batch"),
    )
    return jax.shard_map(shards, mesh=mesh, in_specs=in_specs, out_specs=out_specs, check_vma=False)
```

```python
import jax
import jax.numpy as jnp
from jax import lax
from jax.sharding import PartitionSpec as P

SWAP = [(0, 1), (1, 0)]


def shift_from(block, axis, distance):
    size = lax.axis_size(axis)
    route = [(i - distance, i) for i in range(size) if 0 <= i - distance < size]
    return lax.ppermute(block, axis, route)


def half_of(array, index, axis):
    size = array.shape[axis] // 2
    return lax.dynamic_slice_in_dim(array, index * size, size, axis)


def tap_stack(ext, rows, spread, order):
    return jnp.stack([ext[k * spread : k * spread + rows] for k in order], 1)


def line_total(pieces):
    position = lax.axis_index("seq")
    inner = (position == 1) | (position == 2)
    inward, outward, middle = [(0, 1), (3, 2)], [(1, 0), (2, 3)], [(1, 2), (2, 1)]
    count = len(pieces)
    pairs, wholes, totals = {}, {}, {}
    for step in range(count + 2):
        going_in = step < count
        going_out = step >= 2
        if going_in and going_out:
            sent = jnp.where(inner, wholes[step - 2], pieces[step])
            got = lax.ppermute(sent, "seq", inward + outward)
        elif going_in:
            got = lax.ppermute(pieces[step], "seq", inward)
        else:
            got = lax.ppermute(wholes[step - 2], "seq", outward)
        if going_in:
            pairs[step] = pieces[step] + got
        if going_out:
            totals[step - 2] = jnp.where(inner, wholes[step - 2], got)
        if 1 <= step <= count:
            ready = pairs[step - 1]
            wholes[step - 1] = ready + lax.ppermute(ready, "seq", middle)
    return [totals[n] for n in range(count)]


def line_total(block):
    s = lax.axis_index("seq")
    odd = (s % 2) == 1
    low = s < 2
    rows = block.shape[0] // 4
    quarters = block.reshape(2, 2, rows, block.shape[1])
    even_set, odd_set = quarters[:, 0], quarters[:, 1]
    pairs, across = [(0, 1), (1, 0), (2, 3), (3, 2)], [(0, 2), (2, 0), (1, 3), (3, 1)]
    pair = jnp.where(odd, odd_set, even_set) + lax.ppermute(
        jnp.where(odd, even_set, odd_set), "seq", pairs
    )
    keep = jnp.where(low, pair[0], pair[1])
    give = jnp.where(low, pair[1], pair[0])
    total = (keep + lax.ppermute(give, "seq", across)).astype(jnp.bfloat16)
    other = lax.ppermute(total, "seq", across)
    own_set = jnp.where(low, jnp.stack([total, other]), jnp.stack([other, total]))
    far_set = lax.ppermute(own_set, "seq", pairs)
    evens = jnp.where(odd, far_set, own_set)
    odds = jnp.where(odd, own_set, far_set)
    return jnp.stack([evens, odds], 1).reshape(block.shape).astype(jnp.float32)


def shards(seq_in, conv_weight, cotangent):
    local_in = seq_in[0]
    local_cot = cotangent[0]
    rows = local_in.shape[0] // 2
    width = local_in.shape[1]
    spread = rows // 2
    c = lax.axis_index("chan")
    pairing = lax.broadcasted_iota(jnp.int32, (rows, 2 * rows), 1) // 2 == lax.broadcasted_iota(
        jnp.int32, (rows, 2 * rows), 0
    )
    pairing = jnp.where(pairing, 0.5, 0.0).astype(jnp.bfloat16)
    pooled = jnp.dot(pairing, local_in, preferred_element_type=jnp.float32)
    activation = jax.nn.gelu(pooled).astype(jnp.bfloat16)

    if lax.axis_size("batch") == 2:
        b = lax.axis_index("batch")
        same_core = lax.ppermute(local_cot, ("batch", "chan"), [(2, 0), (1, 3)])
        cross_core = lax.ppermute(local_cot, ("batch", "chan"), [(2, 1), (1, 2)])
        far_cot = jnp.where(b == c, same_core, cross_core)
        far_mid = lax.ppermute(activation, "batch", SWAP)

    both = jnp.stack([activation, local_cot])
    w_own = half_of(conv_weight, c, 2)
    w_other = half_of(conv_weight, 1 - c, 2)
    swapped = lax.ppermute(
        jnp.concatenate([both.reshape(-1, width), w_other.reshape(-1, width)], 0), "chan", SWAP
    )
    par_mid = swapped[: 2 * rows].reshape(both.shape)
    w_par = swapped[2 * rows :].reshape(w_other.shape)
    from_prev = shift_from(both[:, rows - spread :], "seq", 1)
    from_next = shift_from(both[:, :spread], "seq", -1)
    par_halo = lax.ppermute(jnp.stack([from_prev, from_next]), "chan", SWAP)
    own_ext = jnp.concatenate([from_prev, both, from_next], 1)
    par_ext = jnp.concatenate([par_halo[0], par_mid, par_halo[1]], 1)

    conv_out = jnp.einsum(
        "tki,kio->to", tap_stack(own_ext[0], rows, spread, (0, 1, 2)), w_own,
        preferred_element_type=jnp.float32,
    ) + jnp.einsum(
        "tki,kio->to", tap_stack(par_ext[0], rows, spread, (0, 1, 2)), w_par,
        preferred_element_type=jnp.float32,
    )
    block_out = (pooled + conv_out).astype(jnp.bfloat16)

    activ_grad = jnp.einsum(
        "tko,kio->ti", tap_stack(own_ext[1], rows, spread, (2, 1, 0)), w_own,
        preferred_element_type=jnp.float32,
    ) + jnp.einsum(
        "tko,kio->ti", tap_stack(par_ext[1], rows, spread, (2, 1, 0)), w_other,
        preferred_element_type=jnp.float32,
    )
    unused, gelu_back = jax.vjp(jax.nn.gelu, pooled)
    pooled_grad = local_cot.astype(jnp.float32) + gelu_back(activ_grad)[0]
    input_grad = jnp.repeat(0.5 * pooled_grad, 2, axis=0).astype(jnp.bfloat16)

    own_taps = tap_stack(own_ext[0], rows, spread, (0, 1, 2))
    par_cot = par_mid[1]
    batch_count = lax.axis_size("batch")
    seq_count = lax.axis_size("seq")
    if batch_count == 2:
        cot_mine = jnp.where(b == c, local_cot, par_cot)
        cot_next = shift_from(far_cot[:spread], "seq", -1)
        cot_prev = shift_from(far_cot[rows - spread :], "seq", 1)
        far_shifted = {
            1: far_cot,
            0: jnp.concatenate([far_cot[spread:], cot_next], 0),
            2: jnp.concatenate([cot_prev, far_cot[: rows - spread]], 0),
        }
        grads = {}
        for k in (1, 0, 2):
            grads[k] = jnp.dot(
                own_taps[:, k].T, cot_mine, preferred_element_type=jnp.float32
            ) + jnp.dot(far_mid.T, far_shifted[k], preferred_element_type=jnp.float32)
        if seq_count == 4:
            weight_grad = jnp.stack([line_total(grads[k]) for k in range(3)])
        else:
            weight_grad = lax.psum(jnp.stack([grads[0], grads[1], grads[2]]), "seq")
    else:
        lo = jnp.where(c == 0, local_cot, par_cot)
        hi = jnp.where(c == 0, par_cot, local_cot)
        cot_full = jnp.concatenate([lo, hi], 1)
        partial = jnp.einsum("tki,to->kio", own_taps, cot_full, preferred_element_type=jnp.float32)
        summed = lax.psum_scatter(partial, "batch", scatter_dimension=2, tiled=True)
        weight_grad = lax.psum(summed, "seq")
    return (block_out[None], input_grad[None], weight_grad)


def solution(mesh):
    in_specs = (
        P(("group", "batch"), "seq", "chan"),
        P(None, "chan", None),
        P(("group", "batch"), "seq", "chan"),
    )
    out_specs = (
        P(("group", "batch"), "seq", "chan"),
        P(("group", "batch"), "seq", "chan"),
        P("group", "chan", "batch"),
    )
    return jax.shard_map(shards, mesh=mesh, in_specs=in_specs, out_specs=out_specs, check_vma=False)
```

```python
import jax
import jax.numpy as jnp
from jax import lax
from jax.sharding import PartitionSpec as P

SWAP = [(0, 1), (1, 0)]


def shift_from(block, axis, distance):
    size = lax.axis_size(axis)
    route = [(i - distance, i) for i in range(size) if 0 <= i - distance < size]
    return lax.ppermute(block, axis, route)


def half_of(array, index, axis):
    size = array.shape[axis] // 2
    return lax.dynamic_slice_in_dim(array, index * size, size, axis)


def tap_stack(ext, rows, spread, order):
    return jnp.stack([ext[k * spread : k * spread + rows] for k in order], 1)


def line_total(pieces):
    position = lax.axis_index("seq")
    inner = (position == 1) | (position == 2)
    inward, outward, middle = [(0, 1), (3, 2)], [(1, 0), (2, 3)], [(1, 2), (2, 1)]
    count = len(pieces)
    pairs, wholes, totals = {}, {}, {}
    for step in range(count + 2):
        going_in = step < count
        going_out = step >= 2
        if going_in and going_out:
            sent = jnp.where(inner, wholes[step - 2], pieces[step])
            got = lax.ppermute(sent, "seq", inward + outward)
        elif going_in:
            got = lax.ppermute(pieces[step], "seq", inward)
        else:
            got = lax.ppermute(wholes[step - 2], "seq", outward)
        if going_in:
            pairs[step] = pieces[step] + got
        if going_out:
            totals[step - 2] = jnp.where(inner, wholes[step - 2], got)
        if 1 <= step <= count:
            ready = pairs[step - 1]
            wholes[step - 1] = ready + lax.ppermute(ready, "seq", middle)
    return [totals[n] for n in range(count)]


def line_total(block):
    s = lax.axis_index("seq")
    odd = (s % 2) == 1
    low = s < 2
    rows = block.shape[0] // 4
    quarters = block.reshape(2, 2, rows, block.shape[1])
    even_set, odd_set = quarters[:, 0], quarters[:, 1]
    pairs, across = [(0, 1), (1, 0), (2, 3), (3, 2)], [(0, 2), (2, 0), (1, 3), (3, 1)]
    pair = jnp.where(odd, odd_set, even_set) + lax.ppermute(
        jnp.where(odd, even_set, odd_set), "seq", pairs
    )
    keep = jnp.where(low, pair[0], pair[1])
    give = jnp.where(low, pair[1], pair[0])
    total = (keep + lax.ppermute(give, "seq", across)).astype(jnp.bfloat16)
    other = lax.ppermute(total, "seq", across)
    own_set = jnp.where(low, jnp.stack([total, other]), jnp.stack([other, total]))
    far_set = lax.ppermute(own_set, "seq", pairs)
    evens = jnp.where(odd, far_set, own_set)
    odds = jnp.where(odd, own_set, far_set)
    return jnp.stack([evens, odds], 1).reshape(block.shape).astype(jnp.float32)


def shards(seq_in, conv_weight, cotangent):
    local_in = seq_in[0]
    local_cot = cotangent[0]
    rows = local_in.shape[0] // 2
    width = local_in.shape[1]
    spread = rows // 2
    c = lax.axis_index("chan")
    pairing = lax.broadcasted_iota(jnp.int32, (rows, 2 * rows), 1) // 2 == lax.broadcasted_iota(
        jnp.int32, (rows, 2 * rows), 0
    )
    pairing = jnp.where(pairing, 0.5, 0.0).astype(jnp.bfloat16)
    pooled = jnp.dot(pairing, local_in, preferred_element_type=jnp.float32)
    activation = jax.nn.gelu(pooled).astype(jnp.bfloat16)

    if lax.axis_size("batch") == 2:
        b = lax.axis_index("batch")
        same_core = lax.ppermute(local_cot, ("batch", "chan"), [(2, 0), (1, 3)])
        cross_core = lax.ppermute(local_cot, ("batch", "chan"), [(2, 1), (1, 2)])
        far_cot = jnp.where(b == c, same_core, cross_core)
        far_mid = lax.ppermute(activation, "batch", SWAP)

    both = jnp.stack([activation, local_cot])
    w_own = half_of(conv_weight, c, 2)
    w_other = half_of(conv_weight, 1 - c, 2)
    swapped = lax.ppermute(
        jnp.concatenate([both.reshape(-1, width), w_other.reshape(-1, width)], 0), "chan", SWAP
    )
    par_mid = swapped[: 2 * rows].reshape(both.shape)
    w_par = swapped[2 * rows :].reshape(w_other.shape)
    if lax.axis_size("batch") == 2:
        going_up = jnp.concatenate([both, far_cot[None]], 0)
        up = shift_from(going_up[:, rows - spread :], "seq", 1)
        down = shift_from(going_up[:, :spread], "seq", -1)
        from_prev, cot_prev = up[:2], up[2]
        from_next, cot_next = down[:2], down[2]
    else:
        from_prev = shift_from(both[:, rows - spread :], "seq", 1)
        from_next = shift_from(both[:, :spread], "seq", -1)
    par_halo = lax.ppermute(jnp.stack([from_prev, from_next]), "chan", SWAP)
    own_ext = jnp.concatenate([from_prev, both, from_next], 1)
    par_ext = jnp.concatenate([par_halo[0], par_mid, par_halo[1]], 1)

    conv_out = jnp.einsum(
        "tki,kio->to", tap_stack(own_ext[0], rows, spread, (0, 1, 2)), w_own,
        preferred_element_type=jnp.float32,
    ) + jnp.einsum(
        "tki,kio->to", tap_stack(par_ext[0], rows, spread, (0, 1, 2)), w_par,
        preferred_element_type=jnp.float32,
    )
    block_out = (pooled + conv_out).astype(jnp.bfloat16)

    activ_grad = jnp.einsum(
        "tko,kio->ti", tap_stack(own_ext[1], rows, spread, (2, 1, 0)), w_own,
        preferred_element_type=jnp.float32,
    ) + jnp.einsum(
        "tko,kio->ti", tap_stack(par_ext[1], rows, spread, (2, 1, 0)), w_other,
        preferred_element_type=jnp.float32,
    )
    unused, gelu_back = jax.vjp(jax.nn.gelu, pooled)
    pooled_grad = local_cot.astype(jnp.float32) + gelu_back(activ_grad)[0]
    input_grad = jnp.repeat(0.5 * pooled_grad, 2, axis=0).astype(jnp.bfloat16)

    own_taps = tap_stack(own_ext[0], rows, spread, (0, 1, 2))
    par_cot = par_mid[1]
    batch_count = lax.axis_size("batch")
    seq_count = lax.axis_size("seq")
    if batch_count == 2:
        cot_mine = jnp.where(b == c, local_cot, par_cot)
        far_shifted = {
            1: far_cot,
            0: jnp.concatenate([far_cot[spread:], cot_next], 0),
            2: jnp.concatenate([cot_prev, far_cot[: rows - spread]], 0),
        }
        grads = {}
        for k in (1, 0, 2):
            grads[k] = jnp.dot(
                own_taps[:, k].T, cot_mine, preferred_element_type=jnp.float32
            ) + jnp.dot(far_mid.T, far_shifted[k], preferred_element_type=jnp.float32)
        if seq_count == 4:
            middle = line_total(grads[1])
            sides = line_total(jnp.concatenate([grads[0], grads[2]], 0))
            weight_grad = jnp.stack([sides[: middle.shape[0]], middle, sides[middle.shape[0] :]])
        else:
            weight_grad = lax.psum(jnp.stack([grads[0], grads[1], grads[2]]), "seq")
    else:
        lo = jnp.where(c == 0, local_cot, par_cot)
        hi = jnp.where(c == 0, par_cot, local_cot)
        cot_full = jnp.concatenate([lo, hi], 1)
        partial = jnp.einsum("tki,to->kio", own_taps, cot_full, preferred_element_type=jnp.float32)
        summed = lax.psum_scatter(partial, "batch", scatter_dimension=2, tiled=True)
        weight_grad = lax.psum(summed, "seq")
    return (block_out[None], input_grad[None], weight_grad)


def solution(mesh):
    in_specs = (
        P(("group", "batch"), "seq", "chan"),
        P(None, "chan", None),
        P(("group", "batch"), "seq", "chan"),
    )
    out_specs = (
        P(("group", "batch"), "seq", "chan"),
        P(("group", "batch"), "seq", "chan"),
        P("group", "chan", "batch"),
    )
    return jax.shard_map(shards, mesh=mesh, in_specs=in_specs, out_specs=out_specs, check_vma=False)
```

```python
import jax
import jax.numpy as jnp
from jax import lax
from jax.sharding import PartitionSpec as P

SWAP = [(0, 1), (1, 0)]


def shift_from(block, axis, distance):
    size = lax.axis_size(axis)
    route = [(i - distance, i) for i in range(size) if 0 <= i - distance < size]
    return lax.ppermute(block, axis, route)


def half_of(array, index, axis):
    size = array.shape[axis] // 2
    return lax.dynamic_slice_in_dim(array, index * size, size, axis)


def tap_stack(ext, rows, spread, order):
    return jnp.stack([ext[k * spread : k * spread + rows] for k in order], 1)


def line_total(pieces):
    position = lax.axis_index("seq")
    inner = (position == 1) | (position == 2)
    inward, outward, middle = [(0, 1), (3, 2)], [(1, 0), (2, 3)], [(1, 2), (2, 1)]
    count = len(pieces)
    pairs, wholes, totals = {}, {}, {}
    for step in range(count + 2):
        going_in = step < count
        going_out = step >= 2
        if going_in and going_out:
            sent = jnp.where(inner, wholes[step - 2], pieces[step])
            got = lax.ppermute(sent, "seq", inward + outward)
        elif going_in:
            got = lax.ppermute(pieces[step], "seq", inward)
        else:
            got = lax.ppermute(wholes[step - 2], "seq", outward)
        if going_in:
            pairs[step] = pieces[step] + got
        if going_out:
            totals[step - 2] = jnp.where(inner, wholes[step - 2], got)
        if 1 <= step <= count:
            ready = pairs[step - 1]
            wholes[step - 1] = ready + lax.ppermute(ready, "seq", middle)
    return [totals[n] for n in range(count)]


def line_total(block):
    s = lax.axis_index("seq")
    odd = (s % 2) == 1
    low = s < 2
    rows = block.shape[0] // 4
    quarters = block.reshape(2, 2, rows, block.shape[1])
    even_set, odd_set = quarters[:, 0], quarters[:, 1]
    pairs, across = [(0, 1), (1, 0), (2, 3), (3, 2)], [(0, 2), (2, 0), (1, 3), (3, 1)]
    pair = jnp.where(odd, odd_set, even_set) + lax.ppermute(
        jnp.where(odd, even_set, odd_set), "seq", pairs
    )
    keep = jnp.where(low, pair[0], pair[1])
    give = jnp.where(low, pair[1], pair[0])
    total = (keep + lax.ppermute(give, "seq", across)).astype(jnp.bfloat16)
    other = lax.ppermute(total, "seq", across)
    own_set = jnp.where(low, jnp.stack([total, other]), jnp.stack([other, total]))
    far_set = lax.ppermute(own_set, "seq", pairs)
    evens = jnp.where(odd, far_set, own_set)
    odds = jnp.where(odd, own_set, far_set)
    return jnp.stack([evens, odds], 1).reshape(block.shape).astype(jnp.float32)


def shards(seq_in, conv_weight, cotangent):
    local_in = seq_in[0]
    local_cot = cotangent[0]
    rows = local_in.shape[0] // 2
    width = local_in.shape[1]
    spread = rows // 2
    c = lax.axis_index("chan")
    pairing = lax.broadcasted_iota(jnp.int32, (rows, 2 * rows), 1) // 2 == lax.broadcasted_iota(
        jnp.int32, (rows, 2 * rows), 0
    )
    pairing = jnp.where(pairing, 0.5, 0.0).astype(jnp.bfloat16)
    pooled = jnp.dot(pairing, local_in, preferred_element_type=jnp.float32)
    activation = jax.nn.gelu(pooled).astype(jnp.bfloat16)

    if lax.axis_size("batch") == 2:
        b = lax.axis_index("batch")
        same_core = lax.ppermute(local_cot, ("batch", "chan"), [(2, 0), (1, 3)])
        far_mid = lax.ppermute(activation, "batch", SWAP)

    both = jnp.stack([activation, local_cot])
    w_own = half_of(conv_weight, c, 2)
    w_other = half_of(conv_weight, 1 - c, 2)
    sending = [both.reshape(-1, width), w_other.reshape(-1, width)]
    if lax.axis_size("batch") == 2:
        sending.append(same_core)
    swapped = lax.ppermute(jnp.concatenate(sending, 0), "chan", SWAP)
    par_mid = swapped[: 2 * rows].reshape(both.shape)
    w_par = swapped[2 * rows : 2 * rows + w_other.shape[0] * w_other.shape[1]].reshape(w_other.shape)
    if lax.axis_size("batch") == 2:
        far_cot = jnp.where(b == c, same_core, swapped[-rows:])
    from_prev = shift_from(both[:, rows - spread :], "seq", 1)
    from_next = shift_from(both[:, :spread], "seq", -1)
    par_halo = lax.ppermute(jnp.stack([from_prev, from_next]), "chan", SWAP)
    own_ext = jnp.concatenate([from_prev, both, from_next], 1)
    par_ext = jnp.concatenate([par_halo[0], par_mid, par_halo[1]], 1)

    conv_out = jnp.einsum(
        "tki,kio->to", tap_stack(own_ext[0], rows, spread, (0, 1, 2)), w_own,
        preferred_element_type=jnp.float32,
    ) + jnp.einsum(
        "tki,kio->to", tap_stack(par_ext[0], rows, spread, (0, 1, 2)), w_par,
        preferred_element_type=jnp.float32,
    )
    block_out = (pooled + conv_out).astype(jnp.bfloat16)

    activ_grad = jnp.einsum(
        "tko,kio->ti", tap_stack(own_ext[1], rows, spread, (2, 1, 0)), w_own,
        preferred_element_type=jnp.float32,
    ) + jnp.einsum(
        "tko,kio->ti", tap_stack(par_ext[1], rows, spread, (2, 1, 0)), w_other,
        preferred_element_type=jnp.float32,
    )
    unused, gelu_back = jax.vjp(jax.nn.gelu, pooled)
    pooled_grad = local_cot.astype(jnp.float32) + gelu_back(activ_grad)[0]
    input_grad = jnp.repeat(0.5 * pooled_grad, 2, axis=0).astype(jnp.bfloat16)

    own_taps = tap_stack(own_ext[0], rows, spread, (0, 1, 2))
    par_cot = par_mid[1]
    batch_count = lax.axis_size("batch")
    seq_count = lax.axis_size("seq")
    if batch_count == 2:
        cot_mine = jnp.where(b == c, local_cot, par_cot)
        cot_next = shift_from(far_cot[:spread], "seq", -1)
        cot_prev = shift_from(far_cot[rows - spread :], "seq", 1)
        far_shifted = {
            1: far_cot,
            0: jnp.concatenate([far_cot[spread:], cot_next], 0),
            2: jnp.concatenate([cot_prev, far_cot[: rows - spread]], 0),
        }
        grads = {}
        for k in (1, 0, 2):
            grads[k] = jnp.dot(
                own_taps[:, k].T, cot_mine, preferred_element_type=jnp.float32
            ) + jnp.dot(far_mid.T, far_shifted[k], preferred_element_type=jnp.float32)
        if seq_count == 4:
            middle = line_total(grads[1])
            sides = line_total(jnp.concatenate([grads[0], grads[2]], 0))
            weight_grad = jnp.stack([sides[: middle.shape[0]], middle, sides[middle.shape[0] :]])
        else:
            weight_grad = lax.psum(jnp.stack([grads[0], grads[1], grads[2]]), "seq")
    else:
        lo = jnp.where(c == 0, local_cot, par_cot)
        hi = jnp.where(c == 0, par_cot, local_cot)
        cot_full = jnp.concatenate([lo, hi], 1)
        partial = jnp.einsum("tki,to->kio", own_taps, cot_full, preferred_element_type=jnp.float32)
        summed = lax.psum_scatter(partial, "batch", scatter_dimension=2, tiled=True)
        weight_grad = lax.psum(summed, "seq")
    return (block_out[None], input_grad[None], weight_grad)


def solution(mesh):
    in_specs = (
        P(("group", "batch"), "seq", "chan"),
        P(None, "chan", None),
        P(("group", "batch"), "seq", "chan"),
    )
    out_specs = (
        P(("group", "batch"), "seq", "chan"),
        P(("group", "batch"), "seq", "chan"),
        P("group", "chan", "batch"),
    )
    return jax.shard_map(shards, mesh=mesh, in_specs=in_specs, out_specs=out_specs, check_vma=False)
```

```python
import jax
import jax.numpy as jnp
from jax import lax
from jax.sharding import PartitionSpec as P

SWAP = [(0, 1), (1, 0)]


def shift_from(block, axis, distance):
    size = lax.axis_size(axis)
    route = [(i - distance, i) for i in range(size) if 0 <= i - distance < size]
    return lax.ppermute(block, axis, route)


def half_of(array, index, axis):
    size = array.shape[axis] // 2
    return lax.dynamic_slice_in_dim(array, index * size, size, axis)


def tap_stack(ext, rows, spread, order):
    return jnp.stack([ext[k * spread : k * spread + rows] for k in order], 1)


def line_total(pieces):
    position = lax.axis_index("seq")
    inner = (position == 1) | (position == 2)
    inward, outward, middle = [(0, 1), (3, 2)], [(1, 0), (2, 3)], [(1, 2), (2, 1)]
    count = len(pieces)
    pairs, wholes, totals = {}, {}, {}
    for step in range(count + 2):
        going_in = step < count
        going_out = step >= 2
        if going_in and going_out:
            sent = jnp.where(inner, wholes[step - 2], pieces[step])
            got = lax.ppermute(sent, "seq", inward + outward)
        elif going_in:
            got = lax.ppermute(pieces[step], "seq", inward)
        else:
            got = lax.ppermute(wholes[step - 2], "seq", outward)
        if going_in:
            pairs[step] = pieces[step] + got
        if going_out:
            totals[step - 2] = jnp.where(inner, wholes[step - 2], got)
        if 1 <= step <= count:
            ready = pairs[step - 1]
            wholes[step - 1] = ready + lax.ppermute(ready, "seq", middle)
    return [totals[n] for n in range(count)]


def line_total(block):
    s = lax.axis_index("seq")
    odd = (s % 2) == 1
    low = s < 2
    rows = block.shape[0] // 4
    quarters = block.reshape(2, 2, rows, block.shape[1])
    even_set, odd_set = quarters[:, 0], quarters[:, 1]
    pairs, across = [(0, 1), (1, 0), (2, 3), (3, 2)], [(0, 2), (2, 0), (1, 3), (3, 1)]
    pair = jnp.where(odd, odd_set, even_set) + lax.ppermute(
        jnp.where(odd, even_set, odd_set), "seq", pairs
    )
    keep = jnp.where(low, pair[0], pair[1])
    give = jnp.where(low, pair[1], pair[0])
    total = (keep + lax.ppermute(give, "seq", across)).astype(jnp.bfloat16)
    gathered = [total] + [
        lax.ppermute(total, "seq", [(j, (j + d) % 4) for j in range(4)]) for d in range(1, 4)
    ]
    order = (s - jnp.arange(4)) % 4
    return jnp.take(jnp.stack(gathered), order, axis=0).reshape(block.shape).astype(jnp.float32)


def shards(seq_in, conv_weight, cotangent):
    local_in = seq_in[0]
    local_cot = cotangent[0]
    rows = local_in.shape[0] // 2
    width = local_in.shape[1]
    spread = rows // 2
    c = lax.axis_index("chan")
    pairing = lax.broadcasted_iota(jnp.int32, (rows, 2 * rows), 1) // 2 == lax.broadcasted_iota(
        jnp.int32, (rows, 2 * rows), 0
    )
    pairing = jnp.where(pairing, 0.5, 0.0).astype(jnp.bfloat16)
    pooled = jnp.dot(pairing, local_in, preferred_element_type=jnp.float32)
    activation = jax.nn.gelu(pooled).astype(jnp.bfloat16)

    if lax.axis_size("batch") == 2:
        b = lax.axis_index("batch")
        same_core = lax.ppermute(local_cot, ("batch", "chan"), [(2, 0), (1, 3)])
        cross_core = lax.ppermute(local_cot, ("batch", "chan"), [(2, 1), (1, 2)])
        far_cot = jnp.where(b == c, same_core, cross_core)
        far_mid = lax.ppermute(activation, "batch", SWAP)

    both = jnp.stack([activation, local_cot])
    w_own = half_of(conv_weight, c, 2)
    w_other = half_of(conv_weight, 1 - c, 2)
    swapped = lax.ppermute(
        jnp.concatenate([both.reshape(-1, width), w_other.reshape(-1, width)], 0), "chan", SWAP
    )
    par_mid = swapped[: 2 * rows].reshape(both.shape)
    w_par = swapped[2 * rows :].reshape(w_other.shape)
    from_prev = shift_from(both[:, rows - spread :], "seq", 1)
    from_next = shift_from(both[:, :spread], "seq", -1)
    par_halo = lax.ppermute(jnp.stack([from_prev, from_next]), "chan", SWAP)
    own_ext = jnp.concatenate([from_prev, both, from_next], 1)
    par_ext = jnp.concatenate([par_halo[0], par_mid, par_halo[1]], 1)

    conv_out = jnp.einsum(
        "tki,kio->to", tap_stack(own_ext[0], rows, spread, (0, 1, 2)), w_own,
        preferred_element_type=jnp.float32,
    ) + jnp.einsum(
        "tki,kio->to", tap_stack(par_ext[0], rows, spread, (0, 1, 2)), w_par,
        preferred_element_type=jnp.float32,
    )
    block_out = (pooled + conv_out).astype(jnp.bfloat16)

    activ_grad = jnp.einsum(
        "tko,kio->ti", tap_stack(own_ext[1], rows, spread, (2, 1, 0)), w_own,
        preferred_element_type=jnp.float32,
    ) + jnp.einsum(
        "tko,kio->ti", tap_stack(par_ext[1], rows, spread, (2, 1, 0)), w_other,
        preferred_element_type=jnp.float32,
    )
    unused, gelu_back = jax.vjp(jax.nn.gelu, pooled)
    pooled_grad = local_cot.astype(jnp.float32) + gelu_back(activ_grad)[0]
    input_grad = jnp.repeat(0.5 * pooled_grad, 2, axis=0).astype(jnp.bfloat16)

    own_taps = tap_stack(own_ext[0], rows, spread, (0, 1, 2))
    par_cot = par_mid[1]
    batch_count = lax.axis_size("batch")
    seq_count = lax.axis_size("seq")
    if batch_count == 2:
        cot_mine = jnp.where(b == c, local_cot, par_cot)
        cot_next = shift_from(far_cot[:spread], "seq", -1)
        cot_prev = shift_from(far_cot[rows - spread :], "seq", 1)
        far_shifted = {
            1: far_cot,
            0: jnp.concatenate([far_cot[spread:], cot_next], 0),
            2: jnp.concatenate([cot_prev, far_cot[: rows - spread]], 0),
        }
        grads = {}
        for k in (1, 0, 2):
            grads[k] = jnp.dot(
                own_taps[:, k].T, cot_mine, preferred_element_type=jnp.float32
            ) + jnp.dot(far_mid.T, far_shifted[k], preferred_element_type=jnp.float32)
        if seq_count == 4:
            middle = line_total(grads[1])
            sides = line_total(jnp.concatenate([grads[0], grads[2]], 0))
            weight_grad = jnp.stack([sides[: middle.shape[0]], middle, sides[middle.shape[0] :]])
        else:
            weight_grad = lax.psum(jnp.stack([grads[0], grads[1], grads[2]]), "seq")
    else:
        lo = jnp.where(c == 0, local_cot, par_cot)
        hi = jnp.where(c == 0, par_cot, local_cot)
        cot_full = jnp.concatenate([lo, hi], 1)
        partial = jnp.einsum("tki,to->kio", own_taps, cot_full, preferred_element_type=jnp.float32)
        summed = lax.psum_scatter(partial, "batch", scatter_dimension=2, tiled=True)
        weight_grad = lax.psum(summed, "seq")
    return (block_out[None], input_grad[None], weight_grad)


def solution(mesh):
    in_specs = (
        P(("group", "batch"), "seq", "chan"),
        P(None, "chan", None),
        P(("group", "batch"), "seq", "chan"),
    )
    out_specs = (
        P(("group", "batch"), "seq", "chan"),
        P(("group", "batch"), "seq", "chan"),
        P("group", "chan", "batch"),
    )
    return jax.shard_map(shards, mesh=mesh, in_specs=in_specs, out_specs=out_specs, check_vma=False)
```

```python
import jax
import jax.numpy as jnp
from jax import lax
from jax.sharding import PartitionSpec as P

SWAP = [(0, 1), (1, 0)]


def shift_from(block, axis, distance):
    size = lax.axis_size(axis)
    route = [(i - distance, i) for i in range(size) if 0 <= i - distance < size]
    return lax.ppermute(block, axis, route)


def half_of(array, index, axis):
    size = array.shape[axis] // 2
    return lax.dynamic_slice_in_dim(array, index * size, size, axis)


def tap_stack(ext, rows, spread, order):
    return jnp.stack([ext[k * spread : k * spread + rows] for k in order], 1)


def line_total(pieces):
    position = lax.axis_index("seq")
    inner = (position == 1) | (position == 2)
    inward, outward, middle = [(0, 1), (3, 2)], [(1, 0), (2, 3)], [(1, 2), (2, 1)]
    count = len(pieces)
    pairs, wholes, totals = {}, {}, {}
    for step in range(count + 2):
        going_in = step < count
        going_out = step >= 2
        if going_in and going_out:
            sent = jnp.where(inner, wholes[step - 2], pieces[step])
            got = lax.ppermute(sent, "seq", inward + outward)
        elif going_in:
            got = lax.ppermute(pieces[step], "seq", inward)
        else:
            got = lax.ppermute(wholes[step - 2], "seq", outward)
        if going_in:
            pairs[step] = pieces[step] + got
        if going_out:
            totals[step - 2] = jnp.where(inner, wholes[step - 2], got)
        if 1 <= step <= count:
            ready = pairs[step - 1]
            wholes[step - 1] = ready + lax.ppermute(ready, "seq", middle)
    return [totals[n] for n in range(count)]


def line_total(block):
    s = lax.axis_index("seq")
    odd = (s % 2) == 1
    low = s < 2
    rows = block.shape[0] // 4
    quarters = block.reshape(2, 2, rows, block.shape[1])
    even_set, odd_set = quarters[:, 0], quarters[:, 1]
    pairs, across = [(0, 1), (1, 0), (2, 3), (3, 2)], [(0, 2), (2, 0), (1, 3), (3, 1)]
    pair = jnp.where(odd, odd_set, even_set) + lax.ppermute(
        jnp.where(odd, even_set, odd_set), "seq", pairs
    )
    keep = jnp.where(low, pair[0], pair[1])
    give = jnp.where(low, pair[1], pair[0])
    total = (keep + lax.ppermute(give, "seq", across)).astype(jnp.bfloat16)
    other = lax.ppermute(total, "seq", across)
    own_set = jnp.where(low, jnp.stack([total, other]), jnp.stack([other, total]))
    far_set = lax.ppermute(own_set, "seq", pairs)
    evens = jnp.where(odd, far_set, own_set)
    odds = jnp.where(odd, own_set, far_set)
    return jnp.stack([evens, odds], 1).reshape(block.shape).astype(jnp.float32)


def shards(seq_in, conv_weight, cotangent):
    local_in = seq_in[0]
    local_cot = cotangent[0]
    rows = local_in.shape[0] // 2
    width = local_in.shape[1]
    spread = rows // 2
    c = lax.axis_index("chan")
    par_cot_early = lax.ppermute(local_cot, "chan", SWAP)
    pairing = lax.broadcasted_iota(jnp.int32, (rows, 2 * rows), 1) // 2 == lax.broadcasted_iota(
        jnp.int32, (rows, 2 * rows), 0
    )
    pairing = jnp.where(pairing, 0.5, 0.0).astype(jnp.bfloat16)
    pooled = jnp.dot(pairing, local_in, preferred_element_type=jnp.float32)
    activation = jax.nn.gelu(pooled).astype(jnp.bfloat16)

    if lax.axis_size("batch") == 2:
        b = lax.axis_index("batch")
        same_core = lax.ppermute(local_cot, ("batch", "chan"), [(2, 0), (1, 3)])
        cross_core = lax.ppermute(local_cot, ("batch", "chan"), [(2, 1), (1, 2)])
        far_cot = jnp.where(b == c, same_core, cross_core)
        far_mid = lax.ppermute(activation, "batch", SWAP)

    both = jnp.stack([activation, local_cot])
    w_own = half_of(conv_weight, c, 2)
    w_other = half_of(conv_weight, 1 - c, 2)
    swapped = lax.ppermute(
        jnp.concatenate([activation, w_other.reshape(-1, width)], 0), "chan", SWAP
    )
    par_mid = jnp.stack([swapped[:rows], par_cot_early])
    w_par = swapped[rows:].reshape(w_other.shape)
    from_prev = shift_from(both[:, rows - spread :], "seq", 1)
    from_next = shift_from(both[:, :spread], "seq", -1)
    par_halo = lax.ppermute(jnp.stack([from_prev, from_next]), "chan", SWAP)
    own_ext = jnp.concatenate([from_prev, both, from_next], 1)
    par_ext = jnp.concatenate([par_halo[0], par_mid, par_halo[1]], 1)

    conv_out = jnp.einsum(
        "tki,kio->to", tap_stack(own_ext[0], rows, spread, (0, 1, 2)), w_own,
        preferred_element_type=jnp.float32,
    ) + jnp.einsum(
        "tki,kio->to", tap_stack(par_ext[0], rows, spread, (0, 1, 2)), w_par,
        preferred_element_type=jnp.float32,
    )
    block_out = (pooled + conv_out).astype(jnp.bfloat16)

    activ_grad = jnp.einsum(
        "tko,kio->ti", tap_stack(own_ext[1], rows, spread, (2, 1, 0)), w_own,
        preferred_element_type=jnp.float32,
    ) + jnp.einsum(
        "tko,kio->ti", tap_stack(par_ext[1], rows, spread, (2, 1, 0)), w_other,
        preferred_element_type=jnp.float32,
    )
    unused, gelu_back = jax.vjp(jax.nn.gelu, pooled)
    pooled_grad = local_cot.astype(jnp.float32) + gelu_back(activ_grad)[0]
    input_grad = jnp.repeat(0.5 * pooled_grad, 2, axis=0).astype(jnp.bfloat16)

    own_taps = tap_stack(own_ext[0], rows, spread, (0, 1, 2))
    par_cot = par_mid[1]
    batch_count = lax.axis_size("batch")
    seq_count = lax.axis_size("seq")
    if batch_count == 2:
        cot_mine = jnp.where(b == c, local_cot, par_cot)
        cot_next = shift_from(far_cot[:spread], "seq", -1)
        cot_prev = shift_from(far_cot[rows - spread :], "seq", 1)
        far_shifted = {
            1: far_cot,
            0: jnp.concatenate([far_cot[spread:], cot_next], 0),
            2: jnp.concatenate([cot_prev, far_cot[: rows - spread]], 0),
        }
        grads = {}
        for k in (1, 0, 2):
            grads[k] = jnp.dot(
                own_taps[:, k].T, cot_mine, preferred_element_type=jnp.float32
            ) + jnp.dot(far_mid.T, far_shifted[k], preferred_element_type=jnp.float32)
        if seq_count == 4:
            middle = line_total(grads[1])
            sides = line_total(jnp.concatenate([grads[0], grads[2]], 0))
            weight_grad = jnp.stack([sides[: middle.shape[0]], middle, sides[middle.shape[0] :]])
        else:
            weight_grad = lax.psum(jnp.stack([grads[0], grads[1], grads[2]]), "seq")
    else:
        lo = jnp.where(c == 0, local_cot, par_cot)
        hi = jnp.where(c == 0, par_cot, local_cot)
        cot_full = jnp.concatenate([lo, hi], 1)
        partial = jnp.einsum("tki,to->kio", own_taps, cot_full, preferred_element_type=jnp.float32)
        summed = lax.psum_scatter(partial, "batch", scatter_dimension=2, tiled=True)
        weight_grad = lax.psum(summed, "seq")
    return (block_out[None], input_grad[None], weight_grad)


def solution(mesh):
    in_specs = (
        P(("group", "batch"), "seq", "chan"),
        P(None, "chan", None),
        P(("group", "batch"), "seq", "chan"),
    )
    out_specs = (
        P(("group", "batch"), "seq", "chan"),
        P(("group", "batch"), "seq", "chan"),
        P("group", "chan", "batch"),
    )
    return jax.shard_map(shards, mesh=mesh, in_specs=in_specs, out_specs=out_specs, check_vma=False)
```

```python
import jax
import jax.numpy as jnp
from jax import lax
from jax.sharding import PartitionSpec as P

SWAP = [(0, 1), (1, 0)]


def shift_from(block, axis, distance):
    size = lax.axis_size(axis)
    route = [(i - distance, i) for i in range(size) if 0 <= i - distance < size]
    return lax.ppermute(block, axis, route)


def half_of(array, index, axis):
    size = array.shape[axis] // 2
    return lax.dynamic_slice_in_dim(array, index * size, size, axis)


def tap_stack(ext, rows, spread, order):
    return jnp.stack([ext[k * spread : k * spread + rows] for k in order], 1)


def line_total(pieces):
    position = lax.axis_index("seq")
    inner = (position == 1) | (position == 2)
    inward, outward, middle = [(0, 1), (3, 2)], [(1, 0), (2, 3)], [(1, 2), (2, 1)]
    count = len(pieces)
    pairs, wholes, totals = {}, {}, {}
    for step in range(count + 2):
        going_in = step < count
        going_out = step >= 2
        if going_in and going_out:
            sent = jnp.where(inner, wholes[step - 2], pieces[step])
            got = lax.ppermute(sent, "seq", inward + outward)
        elif going_in:
            got = lax.ppermute(pieces[step], "seq", inward)
        else:
            got = lax.ppermute(wholes[step - 2], "seq", outward)
        if going_in:
            pairs[step] = pieces[step] + got
        if going_out:
            totals[step - 2] = jnp.where(inner, wholes[step - 2], got)
        if 1 <= step <= count:
            ready = pairs[step - 1]
            wholes[step - 1] = ready + lax.ppermute(ready, "seq", middle)
    return [totals[n] for n in range(count)]


def direct_total(block):
    s = lax.axis_index("seq")
    rows = block.shape[0] // 4
    quarters = block.reshape(4, rows, block.shape[1])
    mine = lax.dynamic_index_in_dim(quarters, s, 0, keepdims=False)
    for d in range(1, 4):
        going = lax.dynamic_index_in_dim(quarters, (s + d) % 4, 0, keepdims=False)
        mine = mine + lax.ppermute(going, "seq", [(j, (j + d) % 4) for j in range(4)])
    mine = mine.astype(jnp.bfloat16)
    gathered = [mine] + [
        lax.ppermute(mine, "seq", [(j, (j + d) % 4) for j in range(4)]) for d in range(1, 4)
    ]
    order = (s - jnp.arange(4)) % 4
    return jnp.take(jnp.stack(gathered), order, axis=0).reshape(block.shape).astype(jnp.float32)


def line_total(block):
    s = lax.axis_index("seq")
    odd = (s % 2) == 1
    low = s < 2
    rows = block.shape[0] // 4
    quarters = block.reshape(2, 2, rows, block.shape[1])
    even_set, odd_set = quarters[:, 0], quarters[:, 1]
    pairs, across = [(0, 1), (1, 0), (2, 3), (3, 2)], [(0, 2), (2, 0), (1, 3), (3, 1)]
    pair = jnp.where(odd, odd_set, even_set) + lax.ppermute(
        jnp.where(odd, even_set, odd_set), "seq", pairs
    )
    keep = jnp.where(low, pair[0], pair[1])
    give = jnp.where(low, pair[1], pair[0])
    total = (keep + lax.ppermute(give, "seq", across)).astype(jnp.bfloat16)
    other = lax.ppermute(total, "seq", across)
    own_set = jnp.where(low, jnp.stack([total, other]), jnp.stack([other, total]))
    far_set = lax.ppermute(own_set, "seq", pairs)
    evens = jnp.where(odd, far_set, own_set)
    odds = jnp.where(odd, own_set, far_set)
    return jnp.stack([evens, odds], 1).reshape(block.shape).astype(jnp.float32)


def shards(seq_in, conv_weight, cotangent):
    local_in = seq_in[0]
    local_cot = cotangent[0]
    rows = local_in.shape[0] // 2
    width = local_in.shape[1]
    spread = rows // 2
    c = lax.axis_index("chan")
    pairing = lax.broadcasted_iota(jnp.int32, (rows, 2 * rows), 1) // 2 == lax.broadcasted_iota(
        jnp.int32, (rows, 2 * rows), 0
    )
    pairing = jnp.where(pairing, 0.5, 0.0).astype(jnp.bfloat16)
    pooled = jnp.dot(pairing, local_in, preferred_element_type=jnp.float32)
    activation = jax.nn.gelu(pooled).astype(jnp.bfloat16)

    if lax.axis_size("batch") == 2:
        b = lax.axis_index("batch")
        same_core = lax.ppermute(local_cot, ("batch", "chan"), [(2, 0), (1, 3)])
        cross_core = lax.ppermute(local_cot, ("batch", "chan"), [(2, 1), (1, 2)])
        far_cot = jnp.where(b == c, same_core, cross_core)
        far_mid = lax.ppermute(activation, "batch", SWAP)

    both = jnp.stack([activation, local_cot])
    w_own = half_of(conv_weight, c, 2)
    w_other = half_of(conv_weight, 1 - c, 2)
    swapped = lax.ppermute(
        jnp.concatenate([both.reshape(-1, width), w_other.reshape(-1, width)], 0), "chan", SWAP
    )
    par_mid = swapped[: 2 * rows].reshape(both.shape)
    w_par = swapped[2 * rows :].reshape(w_other.shape)
    from_prev = shift_from(both[:, rows - spread :], "seq", 1)
    from_next = shift_from(both[:, :spread], "seq", -1)
    par_halo = lax.ppermute(jnp.stack([from_prev, from_next]), "chan", SWAP)
    own_ext = jnp.concatenate([from_prev, both, from_next], 1)
    par_ext = jnp.concatenate([par_halo[0], par_mid, par_halo[1]], 1)

    conv_out = jnp.einsum(
        "tki,kio->to", tap_stack(own_ext[0], rows, spread, (0, 1, 2)), w_own,
        preferred_element_type=jnp.float32,
    ) + jnp.einsum(
        "tki,kio->to", tap_stack(par_ext[0], rows, spread, (0, 1, 2)), w_par,
        preferred_element_type=jnp.float32,
    )
    block_out = (pooled + conv_out).astype(jnp.bfloat16)

    activ_grad = jnp.einsum(
        "tko,kio->ti", tap_stack(own_ext[1], rows, spread, (2, 1, 0)), w_own,
        preferred_element_type=jnp.float32,
    ) + jnp.einsum(
        "tko,kio->ti", tap_stack(par_ext[1], rows, spread, (2, 1, 0)), w_other,
        preferred_element_type=jnp.float32,
    )
    unused, gelu_back = jax.vjp(jax.nn.gelu, pooled)
    pooled_grad = local_cot.astype(jnp.float32) + gelu_back(activ_grad)[0]
    input_grad = jnp.repeat(0.5 * pooled_grad, 2, axis=0).astype(jnp.bfloat16)

    own_taps = tap_stack(own_ext[0], rows, spread, (0, 1, 2))
    par_cot = par_mid[1]
    batch_count = lax.axis_size("batch")
    seq_count = lax.axis_size("seq")
    if batch_count == 2:
        cot_mine = jnp.where(b == c, local_cot, par_cot)
        cot_next = shift_from(far_cot[:spread], "seq", -1)
        cot_prev = shift_from(far_cot[rows - spread :], "seq", 1)
        far_shifted = {
            1: far_cot,
            0: jnp.concatenate([far_cot[spread:], cot_next], 0),
            2: jnp.concatenate([cot_prev, far_cot[: rows - spread]], 0),
        }
        grads = {}
        for k in (1, 0, 2):
            grads[k] = jnp.dot(
                own_taps[:, k].T, cot_mine, preferred_element_type=jnp.float32
            ) + jnp.dot(far_mid.T, far_shifted[k], preferred_element_type=jnp.float32)
        if seq_count == 4:
            middle = direct_total(grads[1])
            sides = line_total(jnp.concatenate([grads[0], grads[2]], 0))
            weight_grad = jnp.stack([sides[: middle.shape[0]], middle, sides[middle.shape[0] :]])
        else:
            weight_grad = lax.psum(jnp.stack([grads[0], grads[1], grads[2]]), "seq")
    else:
        lo = jnp.where(c == 0, local_cot, par_cot)
        hi = jnp.where(c == 0, par_cot, local_cot)
        cot_full = jnp.concatenate([lo, hi], 1)
        partial = jnp.einsum("tki,to->kio", own_taps, cot_full, preferred_element_type=jnp.float32)
        summed = lax.psum_scatter(partial, "batch", scatter_dimension=2, tiled=True)
        weight_grad = lax.psum(summed, "seq")
    return (block_out[None], input_grad[None], weight_grad)


def solution(mesh):
    in_specs = (
        P(("group", "batch"), "seq", "chan"),
        P(None, "chan", None),
        P(("group", "batch"), "seq", "chan"),
    )
    out_specs = (
        P(("group", "batch"), "seq", "chan"),
        P(("group", "batch"), "seq", "chan"),
        P("group", "chan", "batch"),
    )
    return jax.shard_map(shards, mesh=mesh, in_specs=in_specs, out_specs=out_specs, check_vma=False)
```

```python
import jax
import jax.numpy as jnp
from jax import lax
from jax.sharding import PartitionSpec as P

SWAP = [(0, 1), (1, 0)]


def shift_from(block, axis, distance):
    size = lax.axis_size(axis)
    route = [(i - distance, i) for i in range(size) if 0 <= i - distance < size]
    return lax.ppermute(block, axis, route)


def half_of(array, index, axis):
    size = array.shape[axis] // 2
    return lax.dynamic_slice_in_dim(array, index * size, size, axis)


def tap_stack(ext, rows, spread, order):
    return jnp.stack([ext[k * spread : k * spread + rows] for k in order], 1)


def line_total(pieces):
    position = lax.axis_index("seq")
    inner = (position == 1) | (position == 2)
    inward, outward, middle = [(0, 1), (3, 2)], [(1, 0), (2, 3)], [(1, 2), (2, 1)]
    count = len(pieces)
    pairs, wholes, totals = {}, {}, {}
    for step in range(count + 2):
        going_in = step < count
        going_out = step >= 2
        if going_in and going_out:
            sent = jnp.where(inner, wholes[step - 2], pieces[step])
            got = lax.ppermute(sent, "seq", inward + outward)
        elif going_in:
            got = lax.ppermute(pieces[step], "seq", inward)
        else:
            got = lax.ppermute(wholes[step - 2], "seq", outward)
        if going_in:
            pairs[step] = pieces[step] + got
        if going_out:
            totals[step - 2] = jnp.where(inner, wholes[step - 2], got)
        if 1 <= step <= count:
            ready = pairs[step - 1]
            wholes[step - 1] = ready + lax.ppermute(ready, "seq", middle)
    return [totals[n] for n in range(count)]


def line_total(block):
    s = lax.axis_index("seq")
    odd = (s % 2) == 1
    low = s < 2
    rows = block.shape[0] // 4
    quarters = block.reshape(2, 2, rows, block.shape[1])
    even_set, odd_set = quarters[:, 0], quarters[:, 1]
    pairs, across = [(0, 1), (1, 0), (2, 3), (3, 2)], [(0, 2), (2, 0), (1, 3), (3, 1)]
    pair = jnp.where(odd, odd_set, even_set) + lax.ppermute(
        jnp.where(odd, even_set, odd_set), "seq", pairs
    )
    keep = jnp.where(low, pair[0], pair[1])
    give = jnp.where(low, pair[1], pair[0])
    total = (keep + lax.ppermute(give, "seq", across)).astype(jnp.bfloat16)
    other = lax.ppermute(total, "seq", across)
    own_set = jnp.where(low, jnp.stack([total, other]), jnp.stack([other, total]))
    far_set = lax.ppermute(own_set, "seq", pairs)
    evens = jnp.where(odd, far_set, own_set)
    odds = jnp.where(odd, own_set, far_set)
    return jnp.stack([evens, odds], 1).reshape(block.shape).astype(jnp.float32)


def shards(seq_in, conv_weight, cotangent):
    local_in = seq_in[0]
    local_cot = cotangent[0]
    rows = local_in.shape[0] // 2
    width = local_in.shape[1]
    spread = rows // 2
    c = lax.axis_index("chan")
    pairing = lax.broadcasted_iota(jnp.int32, (rows, 2 * rows), 1) // 2 == lax.broadcasted_iota(
        jnp.int32, (rows, 2 * rows), 0
    )
    pairing = jnp.where(pairing, 0.5, 0.0).astype(jnp.bfloat16)
    pooled = jnp.dot(pairing, local_in, preferred_element_type=jnp.float32)
    activation = jax.nn.gelu(pooled).astype(jnp.bfloat16)

    if lax.axis_size("batch") == 2:
        b = lax.axis_index("batch")
        far_both = lax.ppermute(jnp.stack([activation, local_cot]), "batch", SWAP)
        cross_core = lax.ppermute(local_cot, ("batch", "chan"), [(2, 1), (1, 2)])
        far_cot = jnp.where(b == c, far_both[1], cross_core)
        far_mid = far_both[0]

    both = jnp.stack([activation, local_cot])
    w_own = half_of(conv_weight, c, 2)
    w_other = half_of(conv_weight, 1 - c, 2)
    swapped = lax.ppermute(
        jnp.concatenate([both.reshape(-1, width), w_other.reshape(-1, width)], 0), "chan", SWAP
    )
    par_mid = swapped[: 2 * rows].reshape(both.shape)
    w_par = swapped[2 * rows :].reshape(w_other.shape)
    from_prev = shift_from(both[:, rows - spread :], "seq", 1)
    from_next = shift_from(both[:, :spread], "seq", -1)
    par_halo = lax.ppermute(jnp.stack([from_prev, from_next]), "chan", SWAP)
    own_ext = jnp.concatenate([from_prev, both, from_next], 1)
    par_ext = jnp.concatenate([par_halo[0], par_mid, par_halo[1]], 1)

    conv_out = jnp.einsum(
        "tki,kio->to", tap_stack(own_ext[0], rows, spread, (0, 1, 2)), w_own,
        preferred_element_type=jnp.float32,
    ) + jnp.einsum(
        "tki,kio->to", tap_stack(par_ext[0], rows, spread, (0, 1, 2)), w_par,
        preferred_element_type=jnp.float32,
    )
    block_out = (pooled + conv_out).astype(jnp.bfloat16)

    activ_grad = jnp.einsum(
        "tko,kio->ti", tap_stack(own_ext[1], rows, spread, (2, 1, 0)), w_own,
        preferred_element_type=jnp.float32,
    ) + jnp.einsum(
        "tko,kio->ti", tap_stack(par_ext[1], rows, spread, (2, 1, 0)), w_other,
        preferred_element_type=jnp.float32,
    )
    unused, gelu_back = jax.vjp(jax.nn.gelu, pooled)
    pooled_grad = local_cot.astype(jnp.float32) + gelu_back(activ_grad)[0]
    input_grad = jnp.repeat(0.5 * pooled_grad, 2, axis=0).astype(jnp.bfloat16)

    own_taps = tap_stack(own_ext[0], rows, spread, (0, 1, 2))
    par_cot = par_mid[1]
    batch_count = lax.axis_size("batch")
    seq_count = lax.axis_size("seq")
    if batch_count == 2:
        cot_mine = jnp.where(b == c, local_cot, par_cot)
        cot_next = shift_from(far_cot[:spread], "seq", -1)
        cot_prev = shift_from(far_cot[rows - spread :], "seq", 1)
        far_shifted = {
            1: far_cot,
            0: jnp.concatenate([far_cot[spread:], cot_next], 0),
            2: jnp.concatenate([cot_prev, far_cot[: rows - spread]], 0),
        }
        grads = {}
        for k in (1, 0, 2):
            grads[k] = jnp.dot(
                own_taps[:, k].T, cot_mine, preferred_element_type=jnp.float32
            ) + jnp.dot(far_mid.T, far_shifted[k], preferred_element_type=jnp.float32)
        if seq_count == 4:
            middle = line_total(grads[1])
            sides = line_total(jnp.concatenate([grads[0], grads[2]], 0))
            weight_grad = jnp.stack([sides[: middle.shape[0]], middle, sides[middle.shape[0] :]])
        else:
            weight_grad = lax.psum(jnp.stack([grads[0], grads[1], grads[2]]), "seq")
    else:
        lo = jnp.where(c == 0, local_cot, par_cot)
        hi = jnp.where(c == 0, par_cot, local_cot)
        cot_full = jnp.concatenate([lo, hi], 1)
        partial = jnp.einsum("tki,to->kio", own_taps, cot_full, preferred_element_type=jnp.float32)
        summed = lax.psum_scatter(partial, "batch", scatter_dimension=2, tiled=True)
        weight_grad = lax.psum(summed, "seq")
    return (block_out[None], input_grad[None], weight_grad)


def solution(mesh):
    in_specs = (
        P(("group", "batch"), "seq", "chan"),
        P(None, "chan", None),
        P(("group", "batch"), "seq", "chan"),
    )
    out_specs = (
        P(("group", "batch"), "seq", "chan"),
        P(("group", "batch"), "seq", "chan"),
        P("group", "chan", "batch"),
    )
    return jax.shard_map(shards, mesh=mesh, in_specs=in_specs, out_specs=out_specs, check_vma=False)
```

```python
import jax
import numpy as np
import jax.numpy as jnp
from jax import lax
from jax.sharding import PartitionSpec as P

SWAP = [(0, 1), (1, 0)]


def shift_from(block, axis, distance):
    size = lax.axis_size(axis)
    route = [(i - distance, i) for i in range(size) if 0 <= i - distance < size]
    return lax.ppermute(block, axis, route)


def half_of(array, index, axis):
    size = array.shape[axis] // 2
    return lax.dynamic_slice_in_dim(array, index * size, size, axis)


def tap_stack(ext, rows, spread, order):
    return jnp.stack([ext[k * spread : k * spread + rows] for k in order], 1)


def line_total(pieces):
    position = lax.axis_index("seq")
    inner = (position == 1) | (position == 2)
    inward, outward, middle = [(0, 1), (3, 2)], [(1, 0), (2, 3)], [(1, 2), (2, 1)]
    count = len(pieces)
    pairs, wholes, totals = {}, {}, {}
    for step in range(count + 2):
        going_in = step < count
        going_out = step >= 2
        if going_in and going_out:
            sent = jnp.where(inner, wholes[step - 2], pieces[step])
            got = lax.ppermute(sent, "seq", inward + outward)
        elif going_in:
            got = lax.ppermute(pieces[step], "seq", inward)
        else:
            got = lax.ppermute(wholes[step - 2], "seq", outward)
        if going_in:
            pairs[step] = pieces[step] + got
        if going_out:
            totals[step - 2] = jnp.where(inner, wholes[step - 2], got)
        if 1 <= step <= count:
            ready = pairs[step - 1]
            wholes[step - 1] = ready + lax.ppermute(ready, "seq", middle)
    return [totals[n] for n in range(count)]


def line_total(block):
    s = lax.axis_index("seq")
    odd = (s % 2) == 1
    low = s < 2
    rows = block.shape[0] // 4
    quarters = block.reshape(2, 2, rows, block.shape[1])
    even_set, odd_set = quarters[:, 0], quarters[:, 1]
    pairs, across = [(0, 1), (1, 0), (2, 3), (3, 2)], [(0, 2), (2, 0), (1, 3), (3, 1)]
    pair = jnp.where(odd, odd_set, even_set) + lax.ppermute(
        jnp.where(odd, even_set, odd_set), "seq", pairs
    )
    keep = jnp.where(low, pair[0], pair[1])
    give = jnp.where(low, pair[1], pair[0])
    total = (keep + lax.ppermute(give, "seq", across)).astype(jnp.bfloat16)
    other = lax.ppermute(total, "seq", across)
    own_set = jnp.where(low, jnp.stack([total, other]), jnp.stack([other, total]))
    far_set = lax.ppermute(own_set, "seq", pairs)
    evens = jnp.where(odd, far_set, own_set)
    odds = jnp.where(odd, own_set, far_set)
    return jnp.stack([evens, odds], 1).reshape(block.shape).astype(jnp.float32)


def shards(seq_in, conv_weight, cotangent):
    local_in = seq_in[0]
    local_cot = cotangent[0]
    rows = local_in.shape[0] // 2
    width = local_in.shape[1]
    spread = rows // 2
    c = lax.axis_index("chan")
    pairing = jnp.asarray(
        np.kron(np.eye(rows, dtype=np.float32), np.full((1, 2), 0.5, np.float32)), jnp.bfloat16
    )
    pooled = jnp.dot(pairing, local_in, preferred_element_type=jnp.float32)
    activation = jax.nn.gelu(pooled).astype(jnp.bfloat16)

    if lax.axis_size("batch") == 2:
        b = lax.axis_index("batch")
        same_core = lax.ppermute(local_cot, ("batch", "chan"), [(2, 0), (1, 3)])
        cross_core = lax.ppermute(local_cot, ("batch", "chan"), [(2, 1), (1, 2)])
        far_cot = jnp.where(b == c, same_core, cross_core)
        far_mid = lax.ppermute(activation, "batch", SWAP)

    both = jnp.stack([activation, local_cot])
    w_own = half_of(conv_weight, c, 2)
    w_other = half_of(conv_weight, 1 - c, 2)
    swapped = lax.ppermute(
        jnp.concatenate([both.reshape(-1, width), w_other.reshape(-1, width)], 0), "chan", SWAP
    )
    par_mid = swapped[: 2 * rows].reshape(both.shape)
    w_par = swapped[2 * rows :].reshape(w_other.shape)
    from_prev = shift_from(both[:, rows - spread :], "seq", 1)
    from_next = shift_from(both[:, :spread], "seq", -1)
    par_halo = lax.ppermute(jnp.stack([from_prev, from_next]), "chan", SWAP)
    own_ext = jnp.concatenate([from_prev, both, from_next], 1)
    par_ext = jnp.concatenate([par_halo[0], par_mid, par_halo[1]], 1)

    conv_out = jnp.einsum(
        "tki,kio->to", tap_stack(own_ext[0], rows, spread, (0, 1, 2)), w_own,
        preferred_element_type=jnp.float32,
    ) + jnp.einsum(
        "tki,kio->to", tap_stack(par_ext[0], rows, spread, (0, 1, 2)), w_par,
        preferred_element_type=jnp.float32,
    )
    block_out = (pooled + conv_out).astype(jnp.bfloat16)

    activ_grad = jnp.einsum(
        "tko,kio->ti", tap_stack(own_ext[1], rows, spread, (2, 1, 0)), w_own,
        preferred_element_type=jnp.float32,
    ) + jnp.einsum(
        "tko,kio->ti", tap_stack(par_ext[1], rows, spread, (2, 1, 0)), w_other,
        preferred_element_type=jnp.float32,
    )
    unused, gelu_back = jax.vjp(jax.nn.gelu, pooled)
    pooled_grad = local_cot.astype(jnp.float32) + gelu_back(activ_grad)[0]
    input_grad = jnp.repeat(0.5 * pooled_grad, 2, axis=0).astype(jnp.bfloat16)

    own_taps = tap_stack(own_ext[0], rows, spread, (0, 1, 2))
    par_cot = par_mid[1]
    batch_count = lax.axis_size("batch")
    seq_count = lax.axis_size("seq")
    if batch_count == 2:
        cot_mine = jnp.where(b == c, local_cot, par_cot)
        cot_next = shift_from(far_cot[:spread], "seq", -1)
        cot_prev = shift_from(far_cot[rows - spread :], "seq", 1)
        far_shifted = {
            1: far_cot,
            0: jnp.concatenate([far_cot[spread:], cot_next], 0),
            2: jnp.concatenate([cot_prev, far_cot[: rows - spread]], 0),
        }
        grads = {}
        for k in (1, 0, 2):
            grads[k] = jnp.dot(
                own_taps[:, k].T, cot_mine, preferred_element_type=jnp.float32
            ) + jnp.dot(far_mid.T, far_shifted[k], preferred_element_type=jnp.float32)
        if seq_count == 4:
            middle = line_total(grads[1])
            sides = line_total(jnp.concatenate([grads[0], grads[2]], 0))
            weight_grad = jnp.stack([sides[: middle.shape[0]], middle, sides[middle.shape[0] :]])
        else:
            weight_grad = lax.psum(jnp.stack([grads[0], grads[1], grads[2]]), "seq")
    else:
        lo = jnp.where(c == 0, local_cot, par_cot)
        hi = jnp.where(c == 0, par_cot, local_cot)
        cot_full = jnp.concatenate([lo, hi], 1)
        partial = jnp.einsum("tki,to->kio", own_taps, cot_full, preferred_element_type=jnp.float32)
        summed = lax.psum_scatter(partial, "batch", scatter_dimension=2, tiled=True)
        weight_grad = lax.psum(summed, "seq")
    return (block_out[None], input_grad[None], weight_grad)


def solution(mesh):
    in_specs = (
        P(("group", "batch"), "seq", "chan"),
        P(None, "chan", None),
        P(("group", "batch"), "seq", "chan"),
    )
    out_specs = (
        P(("group", "batch"), "seq", "chan"),
        P(("group", "batch"), "seq", "chan"),
        P("group", "chan", "batch"),
    )
    return jax.shard_map(shards, mesh=mesh, in_specs=in_specs, out_specs=out_specs, check_vma=False)
```

```python
import jax
import jax.numpy as jnp
from jax import lax
from jax.sharding import PartitionSpec as P

SWAP = [(0, 1), (1, 0)]


def shift_from(block, axis, distance):
    size = lax.axis_size(axis)
    route = [(i - distance, i) for i in range(size) if 0 <= i - distance < size]
    return lax.ppermute(block, axis, route)


def half_of(array, index, axis):
    size = array.shape[axis] // 2
    return lax.dynamic_slice_in_dim(array, index * size, size, axis)


def tap_stack(ext, rows, spread, order):
    return jnp.stack([ext[k * spread : k * spread + rows] for k in order], 1)


def line_total(pieces):
    position = lax.axis_index("seq")
    inner = (position == 1) | (position == 2)
    inward, outward, middle = [(0, 1), (3, 2)], [(1, 0), (2, 3)], [(1, 2), (2, 1)]
    count = len(pieces)
    pairs, wholes, totals = {}, {}, {}
    for step in range(count + 2):
        going_in = step < count
        going_out = step >= 2
        if going_in and going_out:
            sent = jnp.where(inner, wholes[step - 2], pieces[step])
            got = lax.ppermute(sent, "seq", inward + outward)
        elif going_in:
            got = lax.ppermute(pieces[step], "seq", inward)
        else:
            got = lax.ppermute(wholes[step - 2], "seq", outward)
        if going_in:
            pairs[step] = pieces[step] + got
        if going_out:
            totals[step - 2] = jnp.where(inner, wholes[step - 2], got)
        if 1 <= step <= count:
            ready = pairs[step - 1]
            wholes[step - 1] = ready + lax.ppermute(ready, "seq", middle)
    return [totals[n] for n in range(count)]


def line_total(block):
    s = lax.axis_index("seq")
    odd = (s % 2) == 1
    low = s < 2
    rows = block.shape[0] // 4
    quarters = block.reshape(2, 2, rows, block.shape[1])
    even_set, odd_set = quarters[:, 0], quarters[:, 1]
    pairs, across = [(0, 1), (1, 0), (2, 3), (3, 2)], [(0, 2), (2, 0), (1, 3), (3, 1)]
    pair = jnp.where(odd, odd_set, even_set) + lax.ppermute(
        jnp.where(odd, even_set, odd_set), "seq", pairs
    )
    keep = jnp.where(low, pair[0], pair[1])
    give = jnp.where(low, pair[1], pair[0])
    total = (keep + lax.ppermute(give, "seq", across)).astype(jnp.bfloat16)
    other = lax.ppermute(total, "seq", across)
    own_set = jnp.where(low, jnp.stack([total, other]), jnp.stack([other, total]))
    far_set = lax.ppermute(own_set, "seq", pairs)
    evens = jnp.where(odd, far_set, own_set)
    odds = jnp.where(odd, own_set, far_set)
    return jnp.stack([evens, odds], 1).reshape(block.shape).astype(jnp.float32)


def line_total_across(block):
    s = lax.axis_index("seq")
    odd = (s % 2) == 1
    low = s < 2
    rows = block.shape[0] // 4
    quarters = block.reshape(2, 2, rows, block.shape[1])
    pairs, across = [(0, 1), (1, 0), (2, 3), (3, 2)], [(0, 2), (2, 0), (1, 3), (3, 1)]
    row = jnp.where(low, quarters[0], quarters[1]) + lax.ppermute(
        jnp.where(low, quarters[1], quarters[0]), "seq", across
    )
    keep = jnp.where(odd, row[1], row[0])
    give = jnp.where(odd, row[0], row[1])
    total = (keep + lax.ppermute(give, "seq", pairs)).astype(jnp.bfloat16)
    other = lax.ppermute(total, "seq", pairs)
    own_row = jnp.where(odd, jnp.stack([other, total]), jnp.stack([total, other]))
    far_row = lax.ppermute(own_row, "seq", across)
    lows = jnp.where(low, own_row, far_row)
    highs = jnp.where(low, far_row, own_row)
    return jnp.stack([lows, highs]).reshape(block.shape).astype(jnp.float32)


def shards(seq_in, conv_weight, cotangent):
    local_in = seq_in[0]
    local_cot = cotangent[0]
    rows = local_in.shape[0] // 2
    width = local_in.shape[1]
    spread = rows // 2
    c = lax.axis_index("chan")
    pairing = lax.broadcasted_iota(jnp.int32, (rows, 2 * rows), 1) // 2 == lax.broadcasted_iota(
        jnp.int32, (rows, 2 * rows), 0
    )
    pairing = jnp.where(pairing, 0.5, 0.0).astype(jnp.bfloat16)
    pooled = jnp.dot(pairing, local_in, preferred_element_type=jnp.float32)
    activation = jax.nn.gelu(pooled).astype(jnp.bfloat16)

    if lax.axis_size("batch") == 2:
        b = lax.axis_index("batch")
        same_core = lax.ppermute(local_cot, ("batch", "chan"), [(2, 0), (1, 3)])
        cross_core = lax.ppermute(local_cot, ("batch", "chan"), [(2, 1), (1, 2)])
        far_cot = jnp.where(b == c, same_core, cross_core)
        far_mid = lax.ppermute(activation, "batch", SWAP)

    both = jnp.stack([activation, local_cot])
    w_own = half_of(conv_weight, c, 2)
    w_other = half_of(conv_weight, 1 - c, 2)
    swapped = lax.ppermute(
        jnp.concatenate([both.reshape(-1, width), w_other.reshape(-1, width)], 0), "chan", SWAP
    )
    par_mid = swapped[: 2 * rows].reshape(both.shape)
    w_par = swapped[2 * rows :].reshape(w_other.shape)
    from_prev = shift_from(both[:, rows - spread :], "seq", 1)
    from_next = shift_from(both[:, :spread], "seq", -1)
    par_halo = lax.ppermute(jnp.stack([from_prev, from_next]), "chan", SWAP)
    own_ext = jnp.concatenate([from_prev, both, from_next], 1)
    par_ext = jnp.concatenate([par_halo[0], par_mid, par_halo[1]], 1)

    conv_out = jnp.einsum(
        "tki,kio->to", tap_stack(own_ext[0], rows, spread, (0, 1, 2)), w_own,
        preferred_element_type=jnp.float32,
    ) + jnp.einsum(
        "tki,kio->to", tap_stack(par_ext[0], rows, spread, (0, 1, 2)), w_par,
        preferred_element_type=jnp.float32,
    )
    block_out = (pooled + conv_out).astype(jnp.bfloat16)

    activ_grad = jnp.einsum(
        "tko,kio->ti", tap_stack(own_ext[1], rows, spread, (2, 1, 0)), w_own,
        preferred_element_type=jnp.float32,
    ) + jnp.einsum(
        "tko,kio->ti", tap_stack(par_ext[1], rows, spread, (2, 1, 0)), w_other,
        preferred_element_type=jnp.float32,
    )
    unused, gelu_back = jax.vjp(jax.nn.gelu, pooled)
    pooled_grad = local_cot.astype(jnp.float32) + gelu_back(activ_grad)[0]
    input_grad = jnp.repeat(0.5 * pooled_grad, 2, axis=0).astype(jnp.bfloat16)

    own_taps = tap_stack(own_ext[0], rows, spread, (0, 1, 2))
    par_cot = par_mid[1]
    batch_count = lax.axis_size("batch")
    seq_count = lax.axis_size("seq")
    if batch_count == 2:
        cot_mine = jnp.where(b == c, local_cot, par_cot)
        cot_next = shift_from(far_cot[:spread], "seq", -1)
        cot_prev = shift_from(far_cot[rows - spread :], "seq", 1)
        far_shifted = {
            1: far_cot,
            0: jnp.concatenate([far_cot[spread:], cot_next], 0),
            2: jnp.concatenate([cot_prev, far_cot[: rows - spread]], 0),
        }
        grads = {}
        for k in (1, 0, 2):
            grads[k] = jnp.dot(
                own_taps[:, k].T, cot_mine, preferred_element_type=jnp.float32
            ) + jnp.dot(far_mid.T, far_shifted[k], preferred_element_type=jnp.float32)
        if seq_count == 4:
            middle = line_total(grads[1])
            sides = line_total_across(jnp.concatenate([grads[0], grads[2]], 0))
            weight_grad = jnp.stack([sides[: middle.shape[0]], middle, sides[middle.shape[0] :]])
        else:
            weight_grad = lax.psum(jnp.stack([grads[0], grads[1], grads[2]]), "seq")
    else:
        lo = jnp.where(c == 0, local_cot, par_cot)
        hi = jnp.where(c == 0, par_cot, local_cot)
        cot_full = jnp.concatenate([lo, hi], 1)
        partial = jnp.einsum("tki,to->kio", own_taps, cot_full, preferred_element_type=jnp.float32)
        summed = lax.psum_scatter(partial, "batch", scatter_dimension=2, tiled=True)
        weight_grad = lax.psum(summed, "seq")
    return (block_out[None], input_grad[None], weight_grad)


def solution(mesh):
    in_specs = (
        P(("group", "batch"), "seq", "chan"),
        P(None, "chan", None),
        P(("group", "batch"), "seq", "chan"),
    )
    out_specs = (
        P(("group", "batch"), "seq", "chan"),
        P(("group", "batch"), "seq", "chan"),
        P("group", "chan", "batch"),
    )
    return jax.shard_map(shards, mesh=mesh, in_specs=in_specs, out_specs=out_specs, check_vma=False)
```

```python
import jax
import jax.numpy as jnp
from jax import lax
from jax.sharding import PartitionSpec as P

SWAP = [(0, 1), (1, 0)]


def shift_from(block, axis, distance):
    size = lax.axis_size(axis)
    route = [(i - distance, i) for i in range(size) if 0 <= i - distance < size]
    return lax.ppermute(block, axis, route)


def half_of(array, index, axis):
    size = array.shape[axis] // 2
    return lax.dynamic_slice_in_dim(array, index * size, size, axis)


def tap_stack(ext, rows, spread, order):
    return jnp.stack([ext[k * spread : k * spread + rows] for k in order], 1)


def line_total(pieces):
    position = lax.axis_index("seq")
    inner = (position == 1) | (position == 2)
    inward, outward, middle = [(0, 1), (3, 2)], [(1, 0), (2, 3)], [(1, 2), (2, 1)]
    count = len(pieces)
    pairs, wholes, totals = {}, {}, {}
    for step in range(count + 2):
        going_in = step < count
        going_out = step >= 2
        if going_in and going_out:
            sent = jnp.where(inner, wholes[step - 2], pieces[step])
            got = lax.ppermute(sent, "seq", inward + outward)
        elif going_in:
            got = lax.ppermute(pieces[step], "seq", inward)
        else:
            got = lax.ppermute(wholes[step - 2], "seq", outward)
        if going_in:
            pairs[step] = pieces[step] + got
        if going_out:
            totals[step - 2] = jnp.where(inner, wholes[step - 2], got)
        if 1 <= step <= count:
            ready = pairs[step - 1]
            wholes[step - 1] = ready + lax.ppermute(ready, "seq", middle)
    return [totals[n] for n in range(count)]


def line_total(block):
    s = lax.axis_index("seq")
    odd = (s % 2) == 1
    low = s < 2
    rows = block.shape[0] // 4
    quarters = block.reshape(2, 2, rows, block.shape[1])
    even_set, odd_set = quarters[:, 0], quarters[:, 1]
    pairs, across = [(0, 1), (1, 0), (2, 3), (3, 2)], [(0, 2), (2, 0), (1, 3), (3, 1)]
    pair = jnp.where(odd, odd_set, even_set) + lax.ppermute(
        jnp.where(odd, even_set, odd_set), "seq", pairs
    )
    keep = jnp.where(low, pair[0], pair[1])
    give = jnp.where(low, pair[1], pair[0])
    total = (keep + lax.ppermute(give, "seq", across)).astype(jnp.bfloat16)
    other = lax.ppermute(total, "seq", across)
    own_set = jnp.where(low, jnp.stack([total, other]), jnp.stack([other, total]))
    far_set = lax.ppermute(own_set, "seq", pairs)
    evens = jnp.where(odd, far_set, own_set)
    odds = jnp.where(odd, own_set, far_set)
    return jnp.stack([evens, odds], 1).reshape(block.shape).astype(jnp.float32)


def shards(seq_in, conv_weight, cotangent):
    local_in = seq_in[0]
    local_cot = cotangent[0]
    rows = local_in.shape[0] // 2
    width = local_in.shape[1]
    spread = rows // 2
    c = lax.axis_index("chan")
    pairing = lax.broadcasted_iota(jnp.int32, (rows, 2 * rows), 1) // 2 == lax.broadcasted_iota(
        jnp.int32, (rows, 2 * rows), 0
    )
    pairing = jnp.where(pairing, 0.5, 0.0).astype(jnp.bfloat16)
    pooled = jnp.dot(pairing, local_in, preferred_element_type=jnp.float32)
    activation = jax.nn.gelu(pooled).astype(jnp.bfloat16)

    if lax.axis_size("batch") == 2:
        b = lax.axis_index("batch")
        same_core = lax.ppermute(local_cot, ("batch", "chan"), [(2, 0), (1, 3)])
        cross_core = lax.ppermute(local_cot, ("batch", "chan"), [(2, 1), (1, 2)])
        far_cot = jnp.where(b == c, same_core, cross_core)
        far_mid = lax.ppermute(activation, "batch", SWAP)

    both = jnp.stack([activation, local_cot])
    w_own = half_of(conv_weight, c, 2)
    w_other = half_of(conv_weight, 1 - c, 2)
    swapped = lax.ppermute(
        jnp.concatenate([both.reshape(-1, width), w_other.reshape(-1, width)], 0), "chan", SWAP
    )
    par_mid = swapped[: 2 * rows].reshape(both.shape)
    w_par = swapped[2 * rows :].reshape(w_other.shape)
    from_prev = shift_from(both[:, rows - spread :], "seq", 1)
    from_next = shift_from(both[:, :spread], "seq", -1)
    par_halo = lax.ppermute(jnp.stack([from_prev, from_next]), "chan", SWAP)
    own_ext = jnp.concatenate([from_prev, both, from_next], 1)
    par_ext = jnp.concatenate([par_halo[0], par_mid, par_halo[1]], 1)

    conv_out = jnp.einsum(
        "tki,kio->to", tap_stack(own_ext[0], rows, spread, (0, 1, 2)), w_own,
        preferred_element_type=jnp.float32,
    ) + jnp.einsum(
        "tki,kio->to", tap_stack(par_ext[0], rows, spread, (0, 1, 2)), w_par,
        preferred_element_type=jnp.float32,
    )
    block_out = (pooled + conv_out).astype(jnp.bfloat16)

    activ_grad = jnp.einsum(
        "tko,kio->ti", tap_stack(own_ext[1], rows, spread, (2, 1, 0)), w_own,
        preferred_element_type=jnp.float32,
    ) + jnp.einsum(
        "tko,kio->ti", tap_stack(par_ext[1], rows, spread, (2, 1, 0)), w_other,
        preferred_element_type=jnp.float32,
    )
    unused, gelu_back = jax.vjp(jax.nn.gelu, pooled)
    pooled_grad = local_cot.astype(jnp.float32) + gelu_back(activ_grad)[0]
    input_grad = jnp.repeat(0.5 * pooled_grad, 2, axis=0).astype(jnp.bfloat16)

    own_taps = tap_stack(own_ext[0], rows, spread, (0, 1, 2))
    par_cot = par_mid[1]
    batch_count = lax.axis_size("batch")
    seq_count = lax.axis_size("seq")
    if batch_count == 2:
        cot_mine = jnp.where(b == c, local_cot, par_cot)
        cot_next = shift_from(far_cot[:spread], "seq", -1)
        cot_prev = shift_from(far_cot[rows - spread :], "seq", 1)
        far_shifted = {
            1: far_cot,
            0: jnp.concatenate([far_cot[spread:], cot_next], 0),
            2: jnp.concatenate([cot_prev, far_cot[: rows - spread]], 0),
        }
        grads = {}
        for k in (1, 0, 2):
            grads[k] = jnp.dot(
                own_taps[:, k].T, cot_mine, preferred_element_type=jnp.float32
            ) + jnp.dot(far_mid.T, far_shifted[k], preferred_element_type=jnp.float32)
        if seq_count == 4:
            first = line_total(jnp.concatenate([grads[1], grads[0]], 0))
            last = line_total(grads[2])
            size = last.shape[0]
            weight_grad = jnp.stack([first[size:], first[:size], last])
        else:
            weight_grad = lax.psum(jnp.stack([grads[0], grads[1], grads[2]]), "seq")
    else:
        lo = jnp.where(c == 0, local_cot, par_cot)
        hi = jnp.where(c == 0, par_cot, local_cot)
        cot_full = jnp.concatenate([lo, hi], 1)
        partial = jnp.einsum("tki,to->kio", own_taps, cot_full, preferred_element_type=jnp.float32)
        summed = lax.psum_scatter(partial, "batch", scatter_dimension=2, tiled=True)
        weight_grad = lax.psum(summed, "seq")
    return (block_out[None], input_grad[None], weight_grad)


def solution(mesh):
    in_specs = (
        P(("group", "batch"), "seq", "chan"),
        P(None, "chan", None),
        P(("group", "batch"), "seq", "chan"),
    )
    out_specs = (
        P(("group", "batch"), "seq", "chan"),
        P(("group", "batch"), "seq", "chan"),
        P("group", "chan", "batch"),
    )
    return jax.shard_map(shards, mesh=mesh, in_specs=in_specs, out_specs=out_specs, check_vma=False)
```

```python
import jax
import jax.numpy as jnp
from jax import lax
from jax.sharding import PartitionSpec as P

SWAP = [(0, 1), (1, 0)]


def shift_from(block, axis, distance):
    size = lax.axis_size(axis)
    route = [(i - distance, i) for i in range(size) if 0 <= i - distance < size]
    return lax.ppermute(block, axis, route)


def half_of(array, index, axis):
    size = array.shape[axis] // 2
    return lax.dynamic_slice_in_dim(array, index * size, size, axis)


def tap_stack(ext, rows, spread, order):
    return jnp.stack([ext[k * spread : k * spread + rows] for k in order], 1)


def line_total(pieces):
    position = lax.axis_index("seq")
    inner = (position == 1) | (position == 2)
    inward, outward, middle = [(0, 1), (3, 2)], [(1, 0), (2, 3)], [(1, 2), (2, 1)]
    count = len(pieces)
    pairs, wholes, totals = {}, {}, {}
    for step in range(count + 2):
        going_in = step < count
        going_out = step >= 2
        if going_in and going_out:
            sent = jnp.where(inner, wholes[step - 2], pieces[step])
            got = lax.ppermute(sent, "seq", inward + outward)
        elif going_in:
            got = lax.ppermute(pieces[step], "seq", inward)
        else:
            got = lax.ppermute(wholes[step - 2], "seq", outward)
        if going_in:
            pairs[step] = pieces[step] + got
        if going_out:
            totals[step - 2] = jnp.where(inner, wholes[step - 2], got)
        if 1 <= step <= count:
            ready = pairs[step - 1]
            wholes[step - 1] = ready + lax.ppermute(ready, "seq", middle)
    return [totals[n] for n in range(count)]


def line_total(block):
    s = lax.axis_index("seq")
    odd = (s % 2) == 1
    low = s < 2
    rows = block.shape[0] // 4
    quarters = block.reshape(2, 2, rows, block.shape[1])
    even_set, odd_set = quarters[:, 0], quarters[:, 1]
    pairs, across = [(0, 1), (1, 0), (2, 3), (3, 2)], [(0, 2), (2, 0), (1, 3), (3, 1)]
    pair = jnp.where(odd, odd_set, even_set) + lax.ppermute(
        jnp.where(odd, even_set, odd_set), "seq", pairs
    )
    keep = jnp.where(low, pair[0], pair[1])
    give = jnp.where(low, pair[1], pair[0])
    total = (keep + lax.ppermute(give, "seq", across)).astype(jnp.bfloat16)
    other = lax.ppermute(total, "seq", across)
    own_set = jnp.where(low, jnp.stack([total, other]), jnp.stack([other, total]))
    far_set = lax.ppermute(own_set, "seq", pairs)
    evens = jnp.where(odd, far_set, own_set)
    odds = jnp.where(odd, own_set, far_set)
    return jnp.stack([evens, odds], 1).reshape(block.shape)


def shards(seq_in, conv_weight, cotangent):
    local_in = seq_in[0]
    local_cot = cotangent[0]
    rows = local_in.shape[0] // 2
    width = local_in.shape[1]
    spread = rows // 2
    c = lax.axis_index("chan")
    pairing = lax.broadcasted_iota(jnp.int32, (rows, 2 * rows), 1) // 2 == lax.broadcasted_iota(
        jnp.int32, (rows, 2 * rows), 0
    )
    pairing = jnp.where(pairing, 0.5, 0.0).astype(jnp.bfloat16)
    pooled = jnp.dot(pairing, local_in, preferred_element_type=jnp.float32)
    activation = jax.nn.gelu(pooled).astype(jnp.bfloat16)

    if lax.axis_size("batch") == 2:
        b = lax.axis_index("batch")
        same_core = lax.ppermute(local_cot, ("batch", "chan"), [(2, 0), (1, 3)])
        cross_core = lax.ppermute(local_cot, ("batch", "chan"), [(2, 1), (1, 2)])
        far_cot = jnp.where(b == c, same_core, cross_core)
        far_mid = lax.ppermute(activation, "batch", SWAP)

    both = jnp.stack([activation, local_cot])
    w_own = half_of(conv_weight, c, 2)
    w_other = half_of(conv_weight, 1 - c, 2)
    swapped = lax.ppermute(
        jnp.concatenate([both.reshape(-1, width), w_other.reshape(-1, width)], 0), "chan", SWAP
    )
    par_mid = swapped[: 2 * rows].reshape(both.shape)
    w_par = swapped[2 * rows :].reshape(w_other.shape)
    from_prev = shift_from(both[:, rows - spread :], "seq", 1)
    from_next = shift_from(both[:, :spread], "seq", -1)
    par_halo = lax.ppermute(jnp.stack([from_prev, from_next]), "chan", SWAP)
    own_ext = jnp.concatenate([from_prev, both, from_next], 1)
    par_ext = jnp.concatenate([par_halo[0], par_mid, par_halo[1]], 1)

    conv_out = jnp.einsum(
        "tki,kio->to", tap_stack(own_ext[0], rows, spread, (0, 1, 2)), w_own,
        preferred_element_type=jnp.float32,
    ) + jnp.einsum(
        "tki,kio->to", tap_stack(par_ext[0], rows, spread, (0, 1, 2)), w_par,
        preferred_element_type=jnp.float32,
    )
    block_out = (pooled + conv_out).astype(jnp.bfloat16)

    activ_grad = jnp.einsum(
        "tko,kio->ti", tap_stack(own_ext[1], rows, spread, (2, 1, 0)), w_own,
        preferred_element_type=jnp.float32,
    ) + jnp.einsum(
        "tko,kio->ti", tap_stack(par_ext[1], rows, spread, (2, 1, 0)), w_other,
        preferred_element_type=jnp.float32,
    )
    unused, gelu_back = jax.vjp(jax.nn.gelu, pooled)
    pooled_grad = local_cot.astype(jnp.float32) + gelu_back(activ_grad)[0]
    input_grad = jnp.repeat(0.5 * pooled_grad, 2, axis=0).astype(jnp.bfloat16)

    own_taps = tap_stack(own_ext[0], rows, spread, (0, 1, 2))
    par_cot = par_mid[1]
    batch_count = lax.axis_size("batch")
    seq_count = lax.axis_size("seq")
    if batch_count == 2:
        cot_mine = jnp.where(b == c, local_cot, par_cot)
        cot_next = shift_from(far_cot[:spread], "seq", -1)
        cot_prev = shift_from(far_cot[rows - spread :], "seq", 1)
        far_shifted = {
            1: far_cot,
            0: jnp.concatenate([far_cot[spread:], cot_next], 0),
            2: jnp.concatenate([cot_prev, far_cot[: rows - spread]], 0),
        }
        grads = {}
        for k in (1, 0, 2):
            grads[k] = jnp.dot(
                own_taps[:, k].T, cot_mine, preferred_element_type=jnp.float32
            ) + jnp.dot(far_mid.T, far_shifted[k], preferred_element_type=jnp.float32)
        if seq_count == 4:
            middle = line_total(grads[1])
            sides = line_total(jnp.concatenate([grads[0], grads[2]], 0))
            weight_grad = jnp.stack(
                [sides[: middle.shape[0]], middle, sides[middle.shape[0] :]]
            ).astype(jnp.float32)
        else:
            weight_grad = lax.psum(jnp.stack([grads[0], grads[1], grads[2]]), "seq")
    else:
        lo = jnp.where(c == 0, local_cot, par_cot)
        hi = jnp.where(c == 0, par_cot, local_cot)
        cot_full = jnp.concatenate([lo, hi], 1)
        partial = jnp.einsum("tki,to->kio", own_taps, cot_full, preferred_element_type=jnp.float32)
        summed = lax.psum_scatter(partial, "batch", scatter_dimension=2, tiled=True)
        weight_grad = lax.psum(summed, "seq")
    return (block_out[None], input_grad[None], weight_grad)


def solution(mesh):
    in_specs = (
        P(("group", "batch"), "seq", "chan"),
        P(None, "chan", None),
        P(("group", "batch"), "seq", "chan"),
    )
    out_specs = (
        P(("group", "batch"), "seq", "chan"),
        P(("group", "batch"), "seq", "chan"),
        P("group", "chan", "batch"),
    )
    return jax.shard_map(shards, mesh=mesh, in_specs=in_specs, out_specs=out_specs, check_vma=False)
```

```python
import jax
import numpy as np
import jax.numpy as jnp
from jax import lax
from jax.sharding import PartitionSpec as P

SWAP = [(0, 1), (1, 0)]


def shift_from(block, axis, distance):
    size = lax.axis_size(axis)
    route = [(i - distance, i) for i in range(size) if 0 <= i - distance < size]
    return lax.ppermute(block, axis, route)


def half_of(array, index, axis):
    size = array.shape[axis] // 2
    return lax.dynamic_slice_in_dim(array, index * size, size, axis)


def tap_stack(ext, rows, spread, order):
    return jnp.stack([ext[k * spread : k * spread + rows] for k in order], 1)


def line_total(pieces):
    position = lax.axis_index("seq")
    inner = (position == 1) | (position == 2)
    inward, outward, middle = [(0, 1), (3, 2)], [(1, 0), (2, 3)], [(1, 2), (2, 1)]
    count = len(pieces)
    pairs, wholes, totals = {}, {}, {}
    for step in range(count + 2):
        going_in = step < count
        going_out = step >= 2
        if going_in and going_out:
            sent = jnp.where(inner, wholes[step - 2], pieces[step])
            got = lax.ppermute(sent, "seq", inward + outward)
        elif going_in:
            got = lax.ppermute(pieces[step], "seq", inward)
        else:
            got = lax.ppermute(wholes[step - 2], "seq", outward)
        if going_in:
            pairs[step] = pieces[step] + got
        if going_out:
            totals[step - 2] = jnp.where(inner, wholes[step - 2], got)
        if 1 <= step <= count:
            ready = pairs[step - 1]
            wholes[step - 1] = ready + lax.ppermute(ready, "seq", middle)
    return [totals[n] for n in range(count)]


def line_total(block):
    s = lax.axis_index("seq")
    odd = (s % 2) == 1
    low = s < 2
    rows = block.shape[0] // 4
    quarters = block.reshape(2, 2, rows, block.shape[1])
    even_set, odd_set = quarters[:, 0], quarters[:, 1]
    pairs, across = [(0, 1), (1, 0), (2, 3), (3, 2)], [(0, 2), (2, 0), (1, 3), (3, 1)]
    pair = jnp.where(odd, odd_set, even_set) + lax.ppermute(
        jnp.where(odd, even_set, odd_set), "seq", pairs
    )
    keep = jnp.where(low, pair[0], pair[1])
    give = jnp.where(low, pair[1], pair[0])
    total = (keep + lax.ppermute(give, "seq", across)).astype(jnp.bfloat16)
    other = lax.ppermute(total, "seq", across)
    own_set = jnp.where(low, jnp.stack([total, other]), jnp.stack([other, total]))
    far_set = lax.ppermute(own_set, "seq", pairs)
    evens = jnp.where(odd, far_set, own_set)
    odds = jnp.where(odd, own_set, far_set)
    return jnp.stack([evens, odds], 1).reshape(block.shape)


def shards(seq_in, conv_weight, cotangent):
    local_in = seq_in[0]
    local_cot = cotangent[0]
    rows = local_in.shape[0] // 2
    width = local_in.shape[1]
    spread = rows // 2
    c = lax.axis_index("chan")
    pairing = jnp.asarray(
        np.kron(np.eye(rows, dtype=np.float32), np.full((1, 2), 0.5, np.float32)), jnp.bfloat16
    )
    pooled = jnp.dot(pairing, local_in, preferred_element_type=jnp.float32)
    activation = jax.nn.gelu(pooled).astype(jnp.bfloat16)

    if lax.axis_size("batch") == 2:
        b = lax.axis_index("batch")
        same_core = lax.ppermute(local_cot, ("batch", "chan"), [(2, 0), (1, 3)])
        cross_core = lax.ppermute(local_cot, ("batch", "chan"), [(2, 1), (1, 2)])
        far_cot = jnp.where(b == c, same_core, cross_core)
        far_mid = lax.ppermute(activation, "batch", SWAP)

    both = jnp.stack([activation, local_cot])
    w_own = half_of(conv_weight, c, 2)
    w_other = half_of(conv_weight, 1 - c, 2)
    swapped = lax.ppermute(
        jnp.concatenate([both.reshape(-1, width), w_other.reshape(-1, width)], 0), "chan", SWAP
    )
    par_mid = swapped[: 2 * rows].reshape(both.shape)
    w_par = swapped[2 * rows :].reshape(w_other.shape)
    from_prev = shift_from(both[:, rows - spread :], "seq", 1)
    from_next = shift_from(both[:, :spread], "seq", -1)
    par_halo = lax.ppermute(jnp.stack([from_prev, from_next]), "chan", SWAP)
    own_ext = jnp.concatenate([from_prev, both, from_next], 1)
    par_ext = jnp.concatenate([par_halo[0], par_mid, par_halo[1]], 1)

    conv_out = jnp.einsum(
        "tki,kio->to", tap_stack(own_ext[0], rows, spread, (0, 1, 2)), w_own,
        preferred_element_type=jnp.float32,
    ) + jnp.einsum(
        "tki,kio->to", tap_stack(par_ext[0], rows, spread, (0, 1, 2)), w_par,
        preferred_element_type=jnp.float32,
    )
    block_out = (pooled + conv_out).astype(jnp.bfloat16)

    activ_grad = jnp.einsum(
        "tko,kio->ti", tap_stack(own_ext[1], rows, spread, (2, 1, 0)), w_own,
        preferred_element_type=jnp.float32,
    ) + jnp.einsum(
        "tko,kio->ti", tap_stack(par_ext[1], rows, spread, (2, 1, 0)), w_other,
        preferred_element_type=jnp.float32,
    )
    unused, gelu_back = jax.vjp(jax.nn.gelu, pooled)
    pooled_grad = local_cot.astype(jnp.float32) + gelu_back(activ_grad)[0]
    input_grad = jnp.repeat(0.5 * pooled_grad, 2, axis=0).astype(jnp.bfloat16)

    own_taps = tap_stack(own_ext[0], rows, spread, (0, 1, 2))
    par_cot = par_mid[1]
    batch_count = lax.axis_size("batch")
    seq_count = lax.axis_size("seq")
    if batch_count == 2:
        cot_mine = jnp.where(b == c, local_cot, par_cot)
        cot_next = shift_from(far_cot[:spread], "seq", -1)
        cot_prev = shift_from(far_cot[rows - spread :], "seq", 1)
        far_shifted = {
            1: far_cot,
            0: jnp.concatenate([far_cot[spread:], cot_next], 0),
            2: jnp.concatenate([cot_prev, far_cot[: rows - spread]], 0),
        }
        grads = {}
        for k in (1, 0, 2):
            grads[k] = jnp.dot(
                own_taps[:, k].T, cot_mine, preferred_element_type=jnp.float32
            ) + jnp.dot(far_mid.T, far_shifted[k], preferred_element_type=jnp.float32)
        if seq_count == 4:
            middle = line_total(grads[1])
            sides = line_total(jnp.concatenate([grads[0], grads[2]], 0))
            weight_grad = jnp.stack(
                [sides[: middle.shape[0]], middle, sides[middle.shape[0] :]]
            ).astype(jnp.float32)
        else:
            weight_grad = lax.psum(jnp.stack([grads[0], grads[1], grads[2]]), "seq")
    else:
        lo = jnp.where(c == 0, local_cot, par_cot)
        hi = jnp.where(c == 0, par_cot, local_cot)
        cot_full = jnp.concatenate([lo, hi], 1)
        partial = jnp.einsum("tki,to->kio", own_taps, cot_full, preferred_element_type=jnp.float32)
        summed = lax.psum_scatter(partial, "batch", scatter_dimension=2, tiled=True)
        weight_grad = lax.psum(summed, "seq")
    return (block_out[None], input_grad[None], weight_grad)


def solution(mesh):
    in_specs = (
        P(("group", "batch"), "seq", "chan"),
        P(None, "chan", None),
        P(("group", "batch"), "seq", "chan"),
    )
    out_specs = (
        P(("group", "batch"), "seq", "chan"),
        P(("group", "batch"), "seq", "chan"),
        P("group", "chan", "batch"),
    )
    return jax.shard_map(shards, mesh=mesh, in_specs=in_specs, out_specs=out_specs, check_vma=False)
```
